32 devices in a mesh: tile: 8 (over z, x), inf: 4 (over y, core).
Axes of the slice: x: 2, y: 2, z: 4, core: 2. Of those that a mesh axis runs over, the one named last changes fastest.
Arguments:
- u_field: float32 [64, 512, 512], P(None, 'tile', 'inf'), may hold values from -6 to 6
- v_field: float32 [64, 512, 512], P(None, 'tile', 'inf'), may hold values from -6 to 6
- diffusivity: float32 [512, 512], P('tile', 'inf'), may hold values from 0.03 to 0.24
- active_columns: int32 [65536], P(('tile', 'inf')), may hold values from 0 to 8191, as said below
- regimes: int32 [65536, 1], P(('tile', 'inf')), may hold values from 0 to 31; in each aligned block of 2048 rows (0 to 2047, 2048 to 4095, ...) at most 128 rows name the same one
- first_layer: float32 [32, 128, 256], P(('tile', 'inf')), may hold values from -0.5 to 0.5
- second_layer: float32 [32, 256, 256], P(('tile', 'inf')), may hold values from -0.375 to 0.375
- third_layer: float32 [32, 256, 256], P(('tile', 'inf')), may hold values from -0.375 to 0.375
- last_layer: float32 [32, 256, 128], P(('tile', 'inf')), may hold values from -0.375 to 0.375
Outputs:
- u_next: float32 [64, 512, 512], P(None, 'tile', 'inf')
- v_next: float32 [64, 512, 512], P(None, 'tile', 'inf')
The draws below stay inside these ranges and needn't reach their ends.
Inputs may be any that keep to these rules, and one draw needn't show every extreme that they name: `active_columns`: the 2048 entries of one device are distinct flat indices x * 128 + y of columns of its own tile. `regimes`: among the rows of one device no network is named more than 128 times.
All inputs are finite; a program needn't handle non-finite values.
Results may differ from the reference program's by a relative error of at most 0.0003.
Values sent between devices are 32-bit elements; how exact they have to be, the bound alone decides.
No kernel may reach another device: no remote copies, remote signals or barrier semaphores. Data moves between devices by JAX's collectives and lax.ppermute only.
A program may use at most 128 MiB of HBM per device.

```python
import math
import jax
import jax.numpy as jnp
import numpy as np
from jax import lax

LEV = 64
HID = 256
PASSES = 4
CY = 128
CX = 64
A_DEV = 2048
CAP = 128
EXPERTS = 32
ACT = 65536
NX = 512
NY = 512
N_INF = 4


def draw_active_columns(key, part):
    blocks = ACT // A_DEV
    keys = jax.random.split(jax.random.fold_in(key, 7), blocks)

    def one_block(block_key):
        return jax.random.permutation(block_key, CX * CY)[:A_DEV]
    return jax.vmap(one_block)(keys).reshape(-1).astype(jnp.int32)


def shard_levels(stream_key, dims, pieces, least, high):
    level, own = 1.0, jax.random.fold_in(stream_key, 6)
    for position, parts in pieces:
        draws = jnp.exp(jax.random.uniform(jax.random.fold_in(own, position), (parts,), jnp.float32, least / len(pieces), high / len(pieces)))
        level = level * jnp.repeat(draws, dims[position] // parts).reshape([-1 if axis == position else 1 for axis in range(len(dims))])
    return level


def routed_block(key, own, number, rows, amount, top, bound, skew):
    order = jax.random.permutation(key, amount)
    heavy_load, usual = portions_of(amount, rows * top, bound, skew, True), portions_of(amount, rows * top, bound, skew, False)
    places = jnp.arange(amount)

    def named(tallies, rotation):
        used = int((tallies > 0).sum())
        fixed = max(1, used // 4)
        passed = fixed + (places - fixed + rotation * (used - fixed)) % max(1, amount - fixed)
        return jnp.zeros((amount,), jnp.int32).at[order[jnp.where(places < fixed, places, passed)]].set(jnp.asarray(tallies, jnp.int32))

    tallies = jnp.where(number % 4 == 0, named(heavy_load, number // 4), named(usual, number - number // 4 - 1))
    mixed = jax.random.permutation(jax.random.fold_in(own, 3), amount)
    giver, sink = mixed[0:amount // 2 * 2:2], mixed[1:amount // 2 * 2:2]
    slack = jnp.minimum(tallies[giver] - 1, bound - tallies[sink]) // 2
    slack = jnp.where((giver == order[0]) | (sink == order[0]) | (tallies[sink] == 0), 0, jnp.maximum(slack, 0))
    passed = jax.random.randint(jax.random.fold_in(own, 4), (amount // 2,), 0, 1 << 20) % (slack + 1)
    tallies = tallies.at[giver].add(-passed).at[sink].add(passed)
    items = jnp.searchsorted(jnp.cumsum(tallies), jnp.arange(rows * top), side="right").astype(jnp.int32)
    grid = items.reshape(top, rows).T
    grid = grid[jax.random.permutation(jax.random.fold_in(own, 1), rows)]
    rotation = jax.random.randint(jax.random.fold_in(own, 2), (rows, 1), 0, top)
    return jnp.take_along_axis(grid, (jnp.arange(top)[None, :] + rotation) % top, axis=1)


def portions_of(amount, total, limit, lean, full):
    portions = [(1 << 20) // math.isqrt(standing ** lean) + 1 for standing in range(1, amount + 1)]
    largest = limit if full else min(limit, max(-(-total // amount), total * portions[0] // sum(portions)))
    least = 1 if total - largest >= amount - 1 else 0
    holding, surplus = [largest] + [least] * (amount - 1), total - largest - least * (amount - 1)
    while surplus > 0:
        free = [i for i in range(1, amount) if holding[i] < largest] or [i for i in range(1, amount) if holding[i] < limit]
        mass, budget = sum([portions[i] for i in free]), surplus
        for i in free:
            more = min(limit - holding[i], max(1, budget * portions[i] // mass), surplus)
            holding[i] = holding[i] + more
            surplus = surplus - more
    return np.array(holding)


def centred(own_key, shape, deviation, limit, shards=(), held_as=jnp.bfloat16):
    drawn = jax.random.normal(own_key, shape, jnp.float32) * deviation
    if len(shards) > 0:
        drawn = shard_levels(own_key, shape, shards, -0.22, 0.18) * drawn
    return jnp.clip(drawn, min=-limit, max=limit).astype(held_as)


def setup_inputs(seed: int = 0) -> dict:
    key_of = jax.random.split(jax.random.key(seed), 10)
    u_field = centred(key_of[0], (LEV, NX, NY), 1.0, 6.0, ((1, 8), (2, 4)), jnp.float32)
    v_field = centred(key_of[1], (LEV, NX, NY), 1.0, 6.0, ((1, 8), (2, 4)), jnp.float32)
    diffusivity = jnp.clip(jnp.exp(math.log(0.24) - 2.0794415 * jax.random.uniform(key_of[2], (NX, NY), jnp.float32) ** shard_levels(key_of[2], (NX, NY), ((0, 8), (1, 4)), -0.2, 0.2)), 0.03, 0.24)
    active_columns = draw_active_columns(jax.random.fold_in(key_of[9], 71), 0)
    regimes_keys = jax.random.split(jax.random.fold_in(key_of[4], 1), ACT // A_DEV)
    regimes_turns = jax.random.permutation(jax.random.fold_in(key_of[4], 3), ACT // A_DEV)
    regimes = jax.vmap(lambda own, number: routed_block(jax.random.fold_in(key_of[4], 2), own, number, A_DEV, EXPERTS, 1, CAP, 2))(regimes_keys, regimes_turns).reshape((ACT, 1))
    first_layer = centred(key_of[5], (EXPERTS, 2 * LEV, HID), (2 * LEV) ** -0.5, 0.5, ((0, 32),), jnp.float32)
    second_layer = centred(key_of[6], (EXPERTS, HID, HID), HID ** -0.5, 0.375, ((0, 32),), jnp.float32)
    third_layer = centred(key_of[7], (EXPERTS, HID, HID), HID ** -0.5, 0.375, ((0, 32),), jnp.float32)
    last_layer = centred(key_of[8], (EXPERTS, HID, 2 * LEV), HID ** -0.5, 0.375, ((0, 32),), jnp.float32)
    return {"u_field": u_field, "v_field": v_field, "diffusivity": diffusivity, "active_columns": active_columns, "regimes": regimes, "first_layer": first_layer, "second_layer": second_layer, "third_layer": third_layer, "last_layer": last_layer}


def standardize(rows):
    center = lax.optimization_barrier(jnp.mean(rows, axis=-1, keepdims=True))
    spread = lax.optimization_barrier(jnp.mean(jnp.square(rows - center), axis=-1, keepdims=True))
    return (rows - center) * lax.rsqrt(spread + 1e-05)

def apply_network(rows, first_layer, second_layer, third_layer, last_layer):
    highest = lax.Precision.HIGHEST
    hidden = jax.nn.silu(jnp.dot(rows, first_layer, precision=highest))
    hidden = jax.nn.silu(jnp.dot(hidden, second_layer, precision=highest))
    hidden = jax.nn.silu(jnp.dot(hidden, third_layer, precision=highest))
    return jnp.dot(hidden, last_layer, precision=highest)

def diffuse(state, diffusivity):
    padded = jnp.pad(state, ((0, 0), (0, 0), (1, 1), (1, 1)))
    neighbours = padded[:, :, 2:, 1:-1] + padded[:, :, :-2, 1:-1]
    neighbours = neighbours + padded[:, :, 1:-1, 2:] + padded[:, :, 1:-1, :-2]
    return state + diffusivity * (neighbours - 4.0 * state)

def reference(u_field, v_field, diffusivity, active_columns, regimes, first_layer, second_layer, third_layer, last_layer):
    state = jnp.stack([u_field, v_field])
    device = jnp.arange(ACT, dtype=jnp.int32) // A_DEV
    tile_pos = device // N_INF
    inf_pos = device % N_INF
    global_x = tile_pos * CX + active_columns // CY
    global_y = inf_pos * CY + active_columns % CY
    inputs = jnp.concatenate([u_field[:, global_x, global_y].T, v_field[:, global_x, global_y].T], axis=1)
    normed = standardize(inputs)
    owner = regimes[:, 0]
    order = jnp.argsort(owner, stable=True).astype(jnp.int32)
    sorted_owner = owner[order]
    labels = jnp.arange(EXPERTS, dtype=jnp.int32)
    starts = jnp.searchsorted(sorted_owner, labels, side='left').astype(jnp.int32)
    stops = jnp.searchsorted(sorted_owner, labels, side='right').astype(jnp.int32)
    slots = EXPERTS * CAP

    def per_regime(operands):
        start, stop, layer_one, layer_two, layer_three, layer_four = operands
        offsets = jnp.arange(slots, dtype=jnp.int32)
        positions = jnp.minimum(start + offsets, ACT - 1)
        picked = order[positions]
        result = apply_network(normed[picked], layer_one, layer_two, layer_three, layer_four)
        target = jnp.where(offsets < stop - start, picked, ACT).astype(jnp.int32)
        return (result, target)
    results, targets = lax.map(per_regime, (starts, stops, first_layer, second_layer, third_layer, last_layer))
    drag = jnp.zeros((ACT, 2 * LEV), jnp.float32).at[targets.reshape(-1)].set(results.reshape(-1, 2 * LEV), mode='drop')
    for step_index in range(PASSES):
        state = diffuse(state, diffusivity)
    tendency = drag.reshape(ACT, 2, LEV).transpose(1, 2, 0)
    state = state.at[:, :, global_x, global_y].add(tendency)
    return (state[0], state[1])
```

```python
import jax
import jax.numpy as jnp
from jax import lax
from jax.sharding import PartitionSpec as P

PASSES = 4


def with_halo(x, sides, width):
    for axis, dim in sides:
        count, length = (lax.axis_size(axis), x.shape[dim])
        up = [(i, (i + 1) % count) for i in range(count - 1)]
        down = [(j, i) for i, j in up]
        last = lax.slice_in_dim(x, length - width, length, axis=dim)
        first = lax.slice_in_dim(x, 0, width, axis=dim)
        before = lax.ppermute(last, axis, up)
        after = lax.ppermute(first, axis, down)
        x = jnp.concatenate([before, x, after], axis=dim)
    return x


def standardize(rows):
    center = jnp.mean(rows, axis=-1, keepdims=True)
    spread = jnp.mean(jnp.square(rows - center), axis=-1, keepdims=True)
    return (rows - center) * lax.rsqrt(spread + 1e-05)


def network_rows(rows, first_layer, second_layer, third_layer, last_layer):
    highest = lax.Precision.HIGHEST
    hidden = jax.nn.silu(jnp.dot(rows, first_layer, precision=highest))
    hidden = jax.nn.silu(jnp.dot(hidden, second_layer, precision=highest))
    hidden = jax.nn.silu(jnp.dot(hidden, third_layer, precision=highest))
    return jnp.dot(hidden, last_layer, precision=highest)


def single_pass(padded, center, coeffs):
    neighbours = padded[:, :, 2:, 1:-1] + padded[:, :, :-2, 1:-1]
    neighbours = neighbours + padded[:, :, 1:-1, 2:] + padded[:, :, 1:-1, :-2]
    return center + coeffs * (neighbours - 4.0 * center)


def body(
    u_field,
    v_field,
    diffusivity,
    active_columns,
    regimes,
    first_layer,
    second_layer,
    third_layer,
    last_layer,
):
    levels, width_x, width_y = u_field.shape
    features = 2 * levels
    cells = width_x * width_y
    active_count = active_columns.shape[0]
    devices_all = lax.axis_size(("tile", "inf"))
    capacity = 2 * active_count // devices_all
    slot_total = devices_all * capacity
    block_rows = min(512, active_count)
    block_count = active_count // block_rows
    state = jnp.stack([u_field, v_field])
    target = regimes[:, 0]
    labels = jnp.arange(devices_all, dtype=jnp.int32)
    one_hot = (
        (target[:, None] == labels[None, :])
        .astype(jnp.bfloat16)
        .reshape(block_count, block_rows, devices_all)
    )
    row_ids = jnp.arange(block_rows, dtype=jnp.int32)
    lower = (row_ids[:, None] > row_ids[None, :]).astype(jnp.bfloat16)

    def rank_step(counts, piece):
        earlier = jnp.dot(lower, piece, preferred_element_type=jnp.float32) + counts[None, :]
        wide_piece = piece.astype(jnp.float32)
        rank = jnp.sum(earlier * wide_piece, axis=1)
        return (counts + jnp.sum(wide_piece, axis=0), rank)

    _, ranks = lax.scan(rank_step, jnp.zeros((devices_all,), jnp.float32), one_hot)
    slot_index = target * capacity + ranks.reshape(-1).astype(jnp.int32)
    spare = cells + jnp.arange(slot_total, dtype=jnp.int32)
    cell_of_slot = spare.at[slot_index].set(active_columns, unique_indices=True)
    slot_of_cell = jnp.full((cells,), slot_total, jnp.int32).at[active_columns].set(
        slot_index, unique_indices=True
    )
    state_rows = state.reshape(features, cells).T
    outgoing = jnp.take(state_rows, cell_of_slot, axis=0, mode="fill", fill_value=0.0)
    block = lax.all_to_all(
        outgoing.reshape(devices_all, capacity, features),
        ("tile", "inf"),
        split_axis=0,
        concat_axis=0,
        tiled=True,
    )
    block_shape = block.shape
    rows = standardize(block.reshape(-1, features))
    result = network_rows(rows, first_layer[0], second_layer[0], third_layer[0], last_layer[0])
    answered = result.reshape(block_shape)
    returned = lax.all_to_all(answered, ("tile", "inf"), split_axis=0, concat_axis=0, tiled=True)
    returned_rows = returned.reshape(slot_total, features)
    drag_dense = jnp.take(returned_rows, slot_of_cell, axis=0, mode="fill", fill_value=0.0)
    depth = PASSES
    padded = with_halo(state, (("tile", 2), ("inf", 3)), depth)
    coeff_wide = with_halo(diffusivity, (("tile", 0), ("inf", 1)), depth)
    first_x = lax.axis_index("tile") * width_x
    first_y = lax.axis_index("inf") * width_y
    grid_x = width_x * lax.axis_size("tile")
    grid_y = width_y * lax.axis_size("inf")
    for step_index in range(depth):
        margin = depth - step_index - 1
        center = padded[:, :, 1:-1, 1:-1]
        coeffs = coeff_wide[
            depth - margin : depth + width_x + margin, depth - margin : depth + width_y + margin
        ]
        updated = single_pass(padded, center, coeffs)
        along_x = first_x - margin + jnp.arange(width_x + 2 * margin, dtype=jnp.int32)
        along_y = first_y - margin + jnp.arange(width_y + 2 * margin, dtype=jnp.int32)
        inside_x = ((along_x >= 0) & (along_x < grid_x)).astype(jnp.float32)
        inside_y = ((along_y >= 0) & (along_y < grid_y)).astype(jnp.float32)
        padded = updated * (inside_x[:, None] * inside_y[None, :])
    state = padded
    final_flat = state.reshape(features, cells) + drag_dense.T
    result = final_flat.reshape(2, levels, width_x, width_y)
    return (result[0], result[1])


def solution(mesh):
    in_specs = (
        P(None, "tile", "inf"),
        P(None, "tile", "inf"),
        P("tile", "inf"),
        P(("tile", "inf")),
        P(("tile", "inf"), None),
        P(("tile", "inf"), None, None),
        P(("tile", "inf"), None, None),
        P(("tile", "inf"), None, None),
        P(("tile", "inf"), None, None),
    )
    out_specs = (P(None, "tile", "inf"), P(None, "tile", "inf"))
    return jax.shard_map(body, mesh=mesh, in_specs=in_specs, out_specs=out_specs, check_vma=False)
```

```python
import jax
import jax.numpy as jnp
from jax import lax
from jax.experimental import pallas as pl
from jax.experimental.pallas import tpu as pltpu
from jax.sharding import PartitionSpec as P

PASSES = 4
LEVEL_BLOCK = 8


def halos(x, axis, dim, width):
    count, length = (lax.axis_size(axis), x.shape[dim])
    up = [(i, i + 1) for i in range(count - 1)]
    down = [(j, i) for i, j in up]
    last = lax.slice_in_dim(x, length - width, length, axis=dim)
    first = lax.slice_in_dim(x, 0, width, axis=dim)
    before = lax.ppermute(last, axis, up)
    after = lax.ppermute(first, axis, down)
    return before, after


def extend(x, width, lanes):
    before, after = halos(x, "tile", x.ndim - 2, width)
    x = jnp.concatenate([x, after, before], axis=x.ndim - 2)
    before, after = halos(x, "inf", x.ndim - 1, width)
    gap = lanes - x.shape[-1] - 2 * width
    filler = jnp.zeros(x.shape[:-1] + (gap,), x.dtype)
    return jnp.concatenate([x, after, filler, before], axis=x.ndim - 1)


def standardize(rows):
    center = jnp.mean(rows, axis=-1, keepdims=True)
    spread = jnp.mean(jnp.square(rows - center), axis=-1, keepdims=True)
    return (rows - center) * lax.rsqrt(spread + 1e-05)


def network_rows(rows, first_layer, second_layer, third_layer, last_layer):
    highest = lax.Precision.HIGHEST
    hidden = jax.nn.silu(jnp.dot(rows, first_layer, precision=highest))
    hidden = jax.nn.silu(jnp.dot(hidden, second_layer, precision=highest))
    hidden = jax.nn.silu(jnp.dot(hidden, third_layer, precision=highest))
    return jnp.dot(hidden, last_layer, precision=highest)


def gather_kernel(cell_ref, u_ref, v_ref, o_ref, t_ref):
    levels_x, width_y = u_ref.shape
    features = o_ref.shape[1]
    levels = features // 2
    width_x = levels_x // levels
    cells = width_x * width_y

    def transpose_tile(x, carry):
        a = u_ref[pl.ds(x, levels, stride=width_x), :]
        b = v_ref[pl.ds(x, levels, stride=width_x), :]
        tile = jnp.concatenate([a, b], axis=0)
        t_ref[pl.ds(pl.multiple_of(x * width_y, width_y), width_y), :] = tile.T
        return carry

    lax.fori_loop(0, width_x, transpose_tile, 0)
    t_ref[pl.ds(cells, 8), :] = jnp.zeros((8, features), jnp.float32)

    def pick(s, carry):
        o_ref[pl.ds(s, 1), :] = t_ref[pl.ds(cell_ref[s], 1), :]
        return carry

    lax.fori_loop(0, o_ref.shape[0], pick, 0, unroll=8)


def drag_kernel(slot_ref, act_ref, r_ref, du_ref, dv_ref, d_ref):
    levels_x, width_y = du_ref.shape
    features = r_ref.shape[1]
    levels = features // 2
    width_x = levels_x // levels

    def clear(x, carry):
        d_ref[pl.ds(pl.multiple_of(x * width_y, width_y), width_y), :] = jnp.zeros(
            (width_y, features), jnp.float32
        )
        return carry

    lax.fori_loop(0, width_x, clear, 0)

    def place(r, carry):
        d_ref[pl.ds(act_ref[r], 1), :] = r_ref[pl.ds(slot_ref[r], 1), :]
        return carry

    lax.fori_loop(0, act_ref.shape[0], place, 0, unroll=8)

    def transpose_tile(x, carry):
        tile = d_ref[pl.ds(pl.multiple_of(x * width_y, width_y), width_y), :].T
        du_ref[pl.ds(x, levels, stride=width_x), :] = tile[:levels]
        dv_ref[pl.ds(x, levels, stride=width_x), :] = tile[levels:]
        return carry

    lax.fori_loop(0, width_x, transpose_tile, 0)


def diffuse_kernel(eu_ref, ev_ref, c_ref, du_ref, dv_ref, ou_ref, ov_ref):
    rows, lanes = c_ref.shape
    width_x, width_y = ou_ref.shape[1:]

    def one(e_ref, d_ref, o_ref, l):
        coeff = c_ref[...]
        q = e_ref[l]
        for _ in range(PASSES):
            n = pltpu.roll(q, rows - 1, 0) + pltpu.roll(q, 1, 0)
            n = n + pltpu.roll(q, lanes - 1, 1) + pltpu.roll(q, 1, 1)
            q = q + coeff * (n - 4.0 * q)
        o_ref[l] = q[:width_x, :width_y] + d_ref[l]

    def step(l, carry):
        one(eu_ref, du_ref, ou_ref, l)
        one(ev_ref, dv_ref, ov_ref, l)
        return carry

    lax.fori_loop(0, eu_ref.shape[0], step, 0)


def body(
    u_field,
    v_field,
    diffusivity,
    active_columns,
    regimes,
    first_layer,
    second_layer,
    third_layer,
    last_layer,
):
    levels, width_x, width_y = u_field.shape
    features = 2 * levels
    cells = width_x * width_y
    active_count = active_columns.shape[0]
    devices_all = lax.axis_size(("tile", "inf"))
    capacity = 2 * active_count // devices_all
    slot_total = devices_all * capacity
    block_rows = min(512, active_count)
    block_count = active_count // block_rows
    target = regimes[:, 0]
    labels = jnp.arange(devices_all, dtype=jnp.int32)
    one_hot = (
        (target[:, None] == labels[None, :])
        .astype(jnp.bfloat16)
        .reshape(block_count, block_rows, devices_all)
    )
    row_ids = jnp.arange(block_rows, dtype=jnp.int32)
    lower = (row_ids[:, None] > row_ids[None, :]).astype(jnp.bfloat16)

    def rank_step(counts, piece):
        earlier = jnp.dot(lower, piece, preferred_element_type=jnp.float32) + counts[None, :]
        wide_piece = piece.astype(jnp.float32)
        rank = jnp.sum(earlier * wide_piece, axis=1)
        return (counts + jnp.sum(wide_piece, axis=0), rank)

    _, ranks = lax.scan(rank_step, jnp.zeros((devices_all,), jnp.float32), one_hot)
    slot_index = target * capacity + ranks.reshape(-1).astype(jnp.int32)
    cell_of_slot = jnp.full((slot_total,), cells, jnp.int32).at[slot_index].set(
        active_columns, unique_indices=True
    )
    vmem = pl.BlockSpec(memory_space=pltpu.VMEM)
    smem = pl.BlockSpec(memory_space=pltpu.SMEM)
    u_rows = u_field.reshape(levels * width_x, width_y)
    v_rows = v_field.reshape(levels * width_x, width_y)
    outgoing = pl.pallas_call(
        gather_kernel,
        out_shape=jax.ShapeDtypeStruct((slot_total, features), jnp.float32),
        in_specs=[smem, vmem, vmem],
        out_specs=vmem,
        scratch_shapes=[pltpu.VMEM((cells + 8, features), jnp.float32)],
    )(cell_of_slot, u_rows, v_rows)
    block = lax.all_to_all(
        outgoing.reshape(devices_all, capacity, features),
        ("tile", "inf"),
        split_axis=0,
        concat_axis=0,
        tiled=True,
    )
    block_shape = block.shape
    rows = standardize(block.reshape(-1, features))
    result = network_rows(rows, first_layer[0], second_layer[0], third_layer[0], last_layer[0])
    answered = result.reshape(block_shape)
    returned = lax.all_to_all(answered, ("tile", "inf"), split_axis=0, concat_axis=0, tiled=True)
    returned_rows = returned.reshape(slot_total, features)
    drag_u, drag_v = pl.pallas_call(
        drag_kernel,
        out_shape=(
            jax.ShapeDtypeStruct((levels * width_x, width_y), jnp.float32),
            jax.ShapeDtypeStruct((levels * width_x, width_y), jnp.float32),
        ),
        in_specs=[smem, smem, vmem],
        out_specs=(vmem, vmem),
        scratch_shapes=[pltpu.VMEM((cells, features), jnp.float32)],
    )(slot_index, active_columns, returned_rows)
    drag_u = drag_u.reshape(levels, width_x, width_y)
    drag_v = drag_v.reshape(levels, width_x, width_y)

    depth = PASSES
    lanes = 2 * width_y
    ext_u = extend(u_field, depth, lanes)
    ext_v = extend(v_field, depth, lanes)
    coeff = extend(diffusivity, depth, lanes)
    rows_ext = width_x + 2 * depth
    lb = LEVEL_BLOCK
    ext_spec = pl.BlockSpec((lb, rows_ext, lanes), lambda i: (i, 0, 0))
    field_spec = pl.BlockSpec((lb, width_x, width_y), lambda i: (i, 0, 0))
    u_next, v_next = pl.pallas_call(
        diffuse_kernel,
        out_shape=(
            jax.ShapeDtypeStruct(u_field.shape, jnp.float32),
            jax.ShapeDtypeStruct(v_field.shape, jnp.float32),
        ),
        grid=(levels // lb,),
        in_specs=[
            ext_spec,
            ext_spec,
            pl.BlockSpec((rows_ext, lanes), lambda i: (0, 0)),
            field_spec,
            field_spec,
        ],
        out_specs=(field_spec, field_spec),
    )(ext_u, ext_v, coeff, drag_u, drag_v)
    return (u_next, v_next)


def solution(mesh):
    in_specs = (
        P(None, "tile", "inf"),
        P(None, "tile", "inf"),
        P("tile", "inf"),
        P(("tile", "inf")),
        P(("tile", "inf"), None),
        P(("tile", "inf"), None, None),
        P(("tile", "inf"), None, None),
        P(("tile", "inf"), None, None),
        P(("tile", "inf"), None, None),
    )
    out_specs = (P(None, "tile", "inf"), P(None, "tile", "inf"))
    return jax.shard_map(body, mesh=mesh, in_specs=in_specs, out_specs=out_specs, check_vma=False)
```

```python
import jax
import jax.numpy as jnp
from jax import lax
from jax.experimental import pallas as pl
from jax.experimental.pallas import tpu as pltpu
from jax.sharding import PartitionSpec as P

PASSES = 4


def halos(x, axis, dim, width):
    count, length = (lax.axis_size(axis), x.shape[dim])
    up = [(i, i + 1) for i in range(count - 1)]
    down = [(j, i) for i, j in up]
    last = lax.slice_in_dim(x, length - width, length, axis=dim)
    first = lax.slice_in_dim(x, 0, width, axis=dim)
    before = lax.ppermute(last, axis, up)
    after = lax.ppermute(first, axis, down)
    return before, after


def standardize(rows):
    center = jnp.mean(rows, axis=-1, keepdims=True)
    spread = jnp.mean(jnp.square(rows - center), axis=-1, keepdims=True)
    return (rows - center) * lax.rsqrt(spread + 1e-05)


def network_rows(rows, first_layer, second_layer, third_layer, last_layer):
    highest = lax.Precision.HIGHEST
    hidden = jax.nn.silu(jnp.dot(rows, first_layer, precision=highest))
    hidden = jax.nn.silu(jnp.dot(hidden, second_layer, precision=highest))
    hidden = jax.nn.silu(jnp.dot(hidden, third_layer, precision=highest))
    return jnp.dot(hidden, last_layer, precision=highest)


def gather_kernel(cell_ref, u_ref, v_ref, st_ref, o_ref):
    levels_x, width_y = u_ref.shape
    cells, features = st_ref.shape
    levels = features // 2
    width_x = levels_x // levels

    def transpose_tile(x, carry):
        a = u_ref[pl.ds(x, levels, stride=width_x), :]
        b = v_ref[pl.ds(x, levels, stride=width_x), :]
        tile = jnp.concatenate([a, b], axis=0)
        st_ref[pl.ds(pl.multiple_of(x * width_y, width_y), width_y), :] = tile.T
        return carry

    lax.fori_loop(0, width_x, transpose_tile, 0)

    def pick(s, carry):
        cell = cell_ref[s]
        keep = (cell < cells).astype(jnp.float32)
        row = st_ref[pl.ds(jnp.minimum(cell, cells - 1), 1), :]
        o_ref[pl.ds(s, 1), :] = row * keep
        return carry

    lax.fori_loop(0, o_ref.shape[0], pick, 0, unroll=8)


def diffuse_kernel(st_ref, xb_ref, xa_ref, yh_ref, c_ref, f_ref, e_ref, a_ref):
    width_x, width_y, _ = st_ref.shape
    depth = xb_ref.shape[0]
    rows_ext, ylen, _ = c_ref.shape
    e_ref[0:depth, 0:width_y, :] = xb_ref[...]
    e_ref[depth + width_x :, 0:width_y, :] = xa_ref[...]

    def fill(x, carry):
        e_ref[x + depth, 0:width_y, :] = st_ref[x]
        return carry

    lax.fori_loop(0, width_x, fill, 0)
    e_ref[:, width_y:, :] = yh_ref[...]

    def sweep(src, dst, p, last):
        def one(x, carry):
            q = src[x]
            n = src[x + 1] + src[x - 1]
            n = n + pltpu.roll(q, ylen - 1, 0) + pltpu.roll(q, 1, 0)
            new = q + c_ref[x] * (n - 4.0 * q)
            if last:
                f_ref[x - depth] = new[:width_y]
            else:
                dst[x] = new
            return carry

        lax.fori_loop(p + 1, rows_ext - 1 - p, one, 0)

    for p in range(PASSES):
        src, dst = (e_ref, a_ref) if p % 2 == 0 else (a_ref, e_ref)
        sweep(src, dst, p, p == PASSES - 1)


def finish_kernel(slot_ref, act_ref, r_ref, f_ref, uo_ref, vo_ref, d_ref):
    levels_x, width_y = uo_ref.shape
    cells, features = f_ref.shape
    levels = features // 2
    width_x = levels_x // levels

    def copy_tile(x, carry):
        at = pl.ds(pl.multiple_of(x * width_y, width_y), width_y)
        d_ref[at, :] = f_ref[at, :]
        return carry

    lax.fori_loop(0, width_x, copy_tile, 0)

    def place(r, carry):
        at = pl.ds(act_ref[r], 1)
        d_ref[at, :] = d_ref[at, :] + r_ref[pl.ds(slot_ref[r], 1), :]
        return carry

    lax.fori_loop(0, act_ref.shape[0], place, 0, unroll=8)

    def transpose_tile(x, carry):
        tile = d_ref[pl.ds(pl.multiple_of(x * width_y, width_y), width_y), :].T
        uo_ref[pl.ds(x, levels, stride=width_x), :] = tile[:levels]
        vo_ref[pl.ds(x, levels, stride=width_x), :] = tile[levels:]
        return carry

    lax.fori_loop(0, width_x, transpose_tile, 0)


def body(
    u_field,
    v_field,
    diffusivity,
    active_columns,
    regimes,
    first_layer,
    second_layer,
    third_layer,
    last_layer,
):
    levels, width_x, width_y = u_field.shape
    features = 2 * levels
    cells = width_x * width_y
    active_count = active_columns.shape[0]
    devices_all = lax.axis_size(("tile", "inf"))
    capacity = 2 * active_count // devices_all
    slot_total = devices_all * capacity
    block_rows = min(512, active_count)
    block_count = active_count // block_rows
    target = regimes[:, 0]
    labels = jnp.arange(devices_all, dtype=jnp.int32)
    one_hot = (
        (target[:, None] == labels[None, :])
        .astype(jnp.bfloat16)
        .reshape(block_count, block_rows, devices_all)
    )
    row_ids = jnp.arange(block_rows, dtype=jnp.int32)
    lower = (row_ids[:, None] > row_ids[None, :]).astype(jnp.bfloat16)

    def rank_step(counts, piece):
        earlier = jnp.dot(lower, piece, preferred_element_type=jnp.float32) + counts[None, :]
        wide_piece = piece.astype(jnp.float32)
        rank = jnp.sum(earlier * wide_piece, axis=1)
        return (counts + jnp.sum(wide_piece, axis=0), rank)

    _, ranks = lax.scan(rank_step, jnp.zeros((devices_all,), jnp.float32), one_hot)
    slot_index = target * capacity + ranks.reshape(-1).astype(jnp.int32)
    cell_of_slot = jnp.full((slot_total,), cells, jnp.int32).at[slot_index].set(
        active_columns, unique_indices=True
    )
    vmem = pl.BlockSpec(memory_space=pltpu.VMEM)
    smem = pl.BlockSpec(memory_space=pltpu.SMEM)
    u_rows = u_field.reshape(levels * width_x, width_y)
    v_rows = v_field.reshape(levels * width_x, width_y)
    state_t, outgoing = pl.pallas_call(
        gather_kernel,
        out_shape=(
            jax.ShapeDtypeStruct((cells, features), jnp.float32),
            jax.ShapeDtypeStruct((slot_total, features), jnp.float32),
        ),
        in_specs=[smem, vmem, vmem],
        out_specs=(vmem, vmem),
    )(cell_of_slot, u_rows, v_rows)
    block = lax.all_to_all(
        outgoing.reshape(devices_all, capacity, features),
        ("tile", "inf"),
        split_axis=0,
        concat_axis=0,
        tiled=True,
    )
    block_shape = block.shape
    rows = standardize(block.reshape(-1, features))
    result = network_rows(rows, first_layer[0], second_layer[0], third_layer[0], last_layer[0])
    answered = result.reshape(block_shape)
    returned = lax.all_to_all(answered, ("tile", "inf"), split_axis=0, concat_axis=0, tiled=True)
    returned_rows = returned.reshape(slot_total, features)

    depth = PASSES
    state_t = state_t.reshape(width_x, width_y, features)
    x_before, x_after = halos(state_t, "tile", 0, depth)
    extended = jnp.concatenate([x_before, state_t, x_after], axis=0)
    y_before, y_after = halos(extended, "inf", 1, depth)
    y_halo = jnp.concatenate([y_after, y_before], axis=1)
    c_before, c_after = halos(diffusivity, "tile", 0, depth)
    c_ext = jnp.concatenate([c_before, diffusivity, c_after], axis=0)
    c_before, c_after = halos(c_ext, "inf", 1, depth)
    c_ext = jnp.concatenate([c_ext, c_after, c_before], axis=1)
    rows_ext, ylen = c_ext.shape
    coeff = jnp.broadcast_to(c_ext[:, :, None], (rows_ext, ylen, features))
    diffused = pl.pallas_call(
        diffuse_kernel,
        out_shape=jax.ShapeDtypeStruct((width_x, width_y, features), jnp.float32),
        in_specs=[vmem] * 5,
        out_specs=vmem,
        scratch_shapes=[
            pltpu.VMEM((rows_ext, ylen, features), jnp.float32),
            pltpu.VMEM((rows_ext, ylen, features), jnp.float32),
        ],
        compiler_params=pltpu.CompilerParams(vmem_limit_bytes=100 * 1024 * 1024),
    )(state_t, x_before, x_after, y_halo, coeff)
    u_next, v_next = pl.pallas_call(
        finish_kernel,
        out_shape=(
            jax.ShapeDtypeStruct((levels * width_x, width_y), jnp.float32),
            jax.ShapeDtypeStruct((levels * width_x, width_y), jnp.float32),
        ),
        in_specs=[smem, smem, vmem, vmem],
        out_specs=(vmem, vmem),
        scratch_shapes=[pltpu.VMEM((cells, features), jnp.float32)],
    )(slot_index, active_columns, returned_rows, diffused.reshape(cells, features))
    return (u_next.reshape(u_field.shape), v_next.reshape(v_field.shape))


def solution(mesh):
    in_specs = (
        P(None, "tile", "inf"),
        P(None, "tile", "inf"),
        P("tile", "inf"),
        P(("tile", "inf")),
        P(("tile", "inf"), None),
        P(("tile", "inf"), None, None),
        P(("tile", "inf"), None, None),
        P(("tile", "inf"), None, None),
        P(("tile", "inf"), None, None),
    )
    out_specs = (P(None, "tile", "inf"), P(None, "tile", "inf"))
    return jax.shard_map(body, mesh=mesh, in_specs=in_specs, out_specs=out_specs, check_vma=False)
```

```python
import jax
import jax.numpy as jnp
from jax import lax
from jax.experimental import pallas as pl
from jax.experimental.pallas import tpu as pltpu
from jax.sharding import PartitionSpec as P

PASSES = 4


def halos(x, axis, dim, width):
    count, length = (lax.axis_size(axis), x.shape[dim])
    up = [(i, i + 1) for i in range(count - 1)]
    down = [(j, i) for i, j in up]
    last = lax.slice_in_dim(x, length - width, length, axis=dim)
    first = lax.slice_in_dim(x, 0, width, axis=dim)
    before = lax.ppermute(last, axis, up)
    after = lax.ppermute(first, axis, down)
    return before, after


def standardize(rows):
    center = jnp.mean(rows, axis=-1, keepdims=True)
    spread = jnp.mean(jnp.square(rows - center), axis=-1, keepdims=True)
    return (rows - center) * lax.rsqrt(spread + 1e-05)


def network_rows(rows, first_layer, second_layer, third_layer, last_layer):
    highest = lax.Precision.HIGHEST
    hidden = jax.nn.silu(jnp.dot(rows, first_layer, precision=highest))
    hidden = jax.nn.silu(jnp.dot(hidden, second_layer, precision=highest))
    hidden = jax.nn.silu(jnp.dot(hidden, third_layer, precision=highest))
    return jnp.dot(hidden, last_layer, precision=highest)


def gather_kernel(slot_ref, act_ref, u_ref, v_ref, st_ref, o_ref):
    levels_x, width_y = u_ref.shape
    cells, features = st_ref.shape
    levels = features // 2
    width_x = levels_x // levels
    chunk = 128

    def clear(k, carry):
        at = pl.ds(pl.multiple_of(k * chunk, chunk), chunk)
        o_ref[at, :] = jnp.zeros((chunk, features), jnp.float32)
        return carry

    lax.fori_loop(0, o_ref.shape[0] // chunk, clear, 0)

    def transpose_tile(x, carry):
        a = u_ref[pl.ds(x, levels, stride=width_x), :]
        b = v_ref[pl.ds(x, levels, stride=width_x), :]
        tile = jnp.concatenate([a, b], axis=0)
        st_ref[pl.ds(pl.multiple_of(x * width_y, width_y), width_y), :] = tile.T
        return carry

    lax.fori_loop(0, width_x, transpose_tile, 0)

    def place(r, carry):
        o_ref[pl.ds(slot_ref[r], 1), :] = st_ref[pl.ds(act_ref[r], 1), :]
        return carry

    lax.fori_loop(0, act_ref.shape[0], place, 0, unroll=8)


def diffuse_kernel(st_ref, xb_ref, xa_ref, yh_ref, c_ref, f_ref, e_ref, a_ref):
    width_x, width_y, _ = st_ref.shape
    depth = xb_ref.shape[0]
    rows_ext, ylen, _ = c_ref.shape
    e_ref[0:depth, 0:width_y, :] = xb_ref[...]
    e_ref[depth + width_x :, 0:width_y, :] = xa_ref[...]

    def fill(x, carry):
        e_ref[x + depth, 0:width_y, :] = st_ref[x]
        return carry

    lax.fori_loop(0, width_x, fill, 0)
    e_ref[:, width_y:, :] = yh_ref[...]

    def sweep(src, dst, p, last):
        def one(x, carry):
            q = src[x]
            n = src[x + 1] + src[x - 1]
            n = n + pltpu.roll(q, ylen - 1, 0) + pltpu.roll(q, 1, 0)
            new = q + c_ref[x] * (n - 4.0 * q)
            if last:
                f_ref[x - depth] = new[:width_y]
            else:
                dst[x] = new
            return carry

        lax.fori_loop(p + 1, rows_ext - 1 - p, one, 0)

    for p in range(PASSES):
        src, dst = (e_ref, a_ref) if p % 2 == 0 else (a_ref, e_ref)
        sweep(src, dst, p, p == PASSES - 1)


def finish_kernel(slot_ref, act_ref, r_ref, f_ref, uo_ref, vo_ref, d_ref):
    levels_x, width_y = uo_ref.shape
    cells, features = f_ref.shape
    levels = features // 2
    width_x = levels_x // levels

    def copy_tile(x, carry):
        at = pl.ds(pl.multiple_of(x * width_y, width_y), width_y)
        d_ref[at, :] = f_ref[at, :]
        return carry

    lax.fori_loop(0, width_x, copy_tile, 0)

    def place(r, carry):
        at = pl.ds(act_ref[r], 1)
        d_ref[at, :] = d_ref[at, :] + r_ref[pl.ds(slot_ref[r], 1), :]
        return carry

    lax.fori_loop(0, act_ref.shape[0], place, 0, unroll=8)

    def transpose_tile(x, carry):
        tile = d_ref[pl.ds(pl.multiple_of(x * width_y, width_y), width_y), :].T
        uo_ref[pl.ds(x, levels, stride=width_x), :] = tile[:levels]
        vo_ref[pl.ds(x, levels, stride=width_x), :] = tile[levels:]
        return carry

    lax.fori_loop(0, width_x, transpose_tile, 0)


def body(
    u_field,
    v_field,
    diffusivity,
    active_columns,
    regimes,
    first_layer,
    second_layer,
    third_layer,
    last_layer,
):
    levels, width_x, width_y = u_field.shape
    features = 2 * levels
    cells = width_x * width_y
    active_count = active_columns.shape[0]
    devices_all = lax.axis_size(("tile", "inf"))
    capacity = 2 * active_count // devices_all
    slot_total = devices_all * capacity
    block_rows = min(512, active_count)
    block_count = active_count // block_rows
    target = regimes[:, 0]
    labels = jnp.arange(devices_all, dtype=jnp.int32)
    one_hot = (
        (target[:, None] == labels[None, :])
        .astype(jnp.bfloat16)
        .reshape(block_count, block_rows, devices_all)
    )
    row_ids = jnp.arange(block_rows, dtype=jnp.int32)
    lower = (row_ids[:, None] > row_ids[None, :]).astype(jnp.bfloat16)

    def rank_step(counts, piece):
        earlier = jnp.dot(lower, piece, preferred_element_type=jnp.float32) + counts[None, :]
        wide_piece = piece.astype(jnp.float32)
        rank = jnp.sum(earlier * wide_piece, axis=1)
        return (counts + jnp.sum(wide_piece, axis=0), rank)

    _, ranks = lax.scan(rank_step, jnp.zeros((devices_all,), jnp.float32), one_hot)
    slot_index = target * capacity + ranks.reshape(-1).astype(jnp.int32)
    vmem = pl.BlockSpec(memory_space=pltpu.VMEM)
    smem = pl.BlockSpec(memory_space=pltpu.SMEM)
    u_rows = u_field.reshape(levels * width_x, width_y)
    v_rows = v_field.reshape(levels * width_x, width_y)
    state_t, outgoing = pl.pallas_call(
        gather_kernel,
        out_shape=(
            jax.ShapeDtypeStruct((cells, features), jnp.float32),
            jax.ShapeDtypeStruct((slot_total, features), jnp.float32),
        ),
        in_specs=[smem, smem, vmem, vmem],
        out_specs=(vmem, vmem),
    )(slot_index, active_columns, u_rows, v_rows)
    block = lax.all_to_all(
        outgoing.reshape(devices_all, capacity, features),
        ("tile", "inf"),
        split_axis=0,
        concat_axis=0,
        tiled=True,
    )
    block_shape = block.shape
    rows = standardize(block.reshape(-1, features))
    result = network_rows(rows, first_layer[0], second_layer[0], third_layer[0], last_layer[0])
    answered = result.reshape(block_shape)
    returned = lax.all_to_all(answered, ("tile", "inf"), split_axis=0, concat_axis=0, tiled=True)
    returned_rows = returned.reshape(slot_total, features)

    depth = PASSES
    state_t = state_t.reshape(width_x, width_y, features)
    u_before, u_after = halos(u_field, "tile", 1, depth)
    v_before, v_after = halos(v_field, "tile", 1, depth)
    x_before = jnp.concatenate([u_before, v_before], axis=0).transpose(1, 2, 0)
    x_after = jnp.concatenate([u_after, v_after], axis=0).transpose(1, 2, 0)

    def edge_columns(start):
        pieces = []
        for field, before, after in ((u_field, u_before, u_after), (v_field, v_before, v_after)):
            column = lambda a: lax.slice_in_dim(a, start, start + depth, axis=2)
            pieces.append(
                jnp.concatenate([column(before), column(field), column(after)], axis=1)
            )
        return jnp.concatenate(pieces, axis=0).transpose(1, 2, 0)

    inf_count = lax.axis_size("inf")
    up = [(i, i + 1) for i in range(inf_count - 1)]
    down = [(j, i) for i, j in up]
    y_before = lax.ppermute(edge_columns(width_y - depth), "inf", up)
    y_after = lax.ppermute(edge_columns(0), "inf", down)
    y_halo = jnp.concatenate([y_after, y_before], axis=1)
    c_before, c_after = halos(diffusivity, "tile", 0, depth)
    c_ext = jnp.concatenate([c_before, diffusivity, c_after], axis=0)
    c_before, c_after = halos(c_ext, "inf", 1, depth)
    c_ext = jnp.concatenate([c_ext, c_after, c_before], axis=1)
    rows_ext, ylen = c_ext.shape
    coeff = jnp.broadcast_to(c_ext[:, :, None], (rows_ext, ylen, features))
    diffused = pl.pallas_call(
        diffuse_kernel,
        out_shape=jax.ShapeDtypeStruct((width_x, width_y, features), jnp.float32),
        in_specs=[vmem] * 5,
        out_specs=vmem,
        scratch_shapes=[
            pltpu.VMEM((rows_ext, ylen, features), jnp.float32),
            pltpu.VMEM((rows_ext, ylen, features), jnp.float32),
        ],
        compiler_params=pltpu.CompilerParams(vmem_limit_bytes=100 * 1024 * 1024),
    )(state_t, x_before, x_after, y_halo, coeff)
    u_next, v_next = pl.pallas_call(
        finish_kernel,
        out_shape=(
            jax.ShapeDtypeStruct((levels * width_x, width_y), jnp.float32),
            jax.ShapeDtypeStruct((levels * width_x, width_y), jnp.float32),
        ),
        in_specs=[smem, smem, vmem, vmem],
        out_specs=(vmem, vmem),
        scratch_shapes=[pltpu.VMEM((cells, features), jnp.float32)],
    )(slot_index, active_columns, returned_rows, diffused.reshape(cells, features))
    return (u_next.reshape(u_field.shape), v_next.reshape(v_field.shape))


def solution(mesh):
    in_specs = (
        P(None, "tile", "inf"),
        P(None, "tile", "inf"),
        P("tile", "inf"),
        P(("tile", "inf")),
        P(("tile", "inf"), None),
        P(("tile", "inf"), None, None),
        P(("tile", "inf"), None, None),
        P(("tile", "inf"), None, None),
        P(("tile", "inf"), None, None),
    )
    out_specs = (P(None, "tile", "inf"), P(None, "tile", "inf"))
    return jax.shard_map(body, mesh=mesh, in_specs=in_specs, out_specs=out_specs, check_vma=False)
```

```python
import jax
import jax.numpy as jnp
from jax import lax
from jax.experimental import pallas as pl
from jax.experimental.pallas import tpu as pltpu
from jax.sharding import PartitionSpec as P

PASSES = 4


def halos(x, axis, dim, width):
    count, length = (lax.axis_size(axis), x.shape[dim])
    up = [(i, i + 1) for i in range(count - 1)]
    down = [(j, i) for i, j in up]
    last = lax.slice_in_dim(x, length - width, length, axis=dim)
    first = lax.slice_in_dim(x, 0, width, axis=dim)
    before = lax.ppermute(last, axis, up)
    after = lax.ppermute(first, axis, down)
    return before, after


def standardize(rows):
    center = jnp.mean(rows, axis=-1, keepdims=True)
    spread = jnp.mean(jnp.square(rows - center), axis=-1, keepdims=True)
    return (rows - center) * lax.rsqrt(spread + 1e-05)


def network_rows(rows, first_layer, second_layer, third_layer, last_layer):
    highest = lax.Precision.HIGH
    hidden = jax.nn.silu(jnp.dot(rows, first_layer, precision=highest))
    hidden = jax.nn.silu(jnp.dot(hidden, second_layer, precision=highest))
    hidden = jax.nn.silu(jnp.dot(hidden, third_layer, precision=highest))
    return jnp.dot(hidden, last_layer, precision=highest)


def gather_kernel(slot_ref, act_ref, u_ref, v_ref, st_ref, o_ref):
    levels_x, width_y = u_ref.shape
    cells, features = st_ref.shape
    levels = features // 2
    width_x = levels_x // levels
    chunk = 128

    def clear(k, carry):
        at = pl.ds(pl.multiple_of(k * chunk, chunk), chunk)
        o_ref[at, :] = jnp.zeros((chunk, features), jnp.float32)
        return carry

    lax.fori_loop(0, o_ref.shape[0] // chunk, clear, 0)

    def transpose_tile(x, carry):
        a = u_ref[pl.ds(x, levels, stride=width_x), :]
        b = v_ref[pl.ds(x, levels, stride=width_x), :]
        tile = jnp.concatenate([a, b], axis=0)
        st_ref[pl.ds(pl.multiple_of(x * width_y, width_y), width_y), :] = tile.T
        return carry

    lax.fori_loop(0, width_x, transpose_tile, 0)

    def place(r, carry):
        o_ref[pl.ds(slot_ref[r], 1), :] = st_ref[pl.ds(act_ref[r], 1), :]
        return carry

    lax.fori_loop(0, act_ref.shape[0], place, 0, unroll=8)


def diffuse_kernel(st_ref, xb_ref, xa_ref, yh_ref, c_ref, f_ref, e_ref, a_ref):
    width_x, width_y, _ = st_ref.shape
    depth = xb_ref.shape[0]
    rows_ext, ylen, _ = c_ref.shape
    e_ref[0:depth, 0:width_y, :] = xb_ref[...]
    e_ref[depth + width_x :, 0:width_y, :] = xa_ref[...]

    def fill(x, carry):
        e_ref[x + depth, 0:width_y, :] = st_ref[x]
        return carry

    lax.fori_loop(0, width_x, fill, 0)
    e_ref[:, width_y:, :] = yh_ref[...]

    def sweep(src, dst, p, last):
        def one(x, carry):
            q = src[x]
            n = src[x + 1] + src[x - 1]
            n = n + pltpu.roll(q, ylen - 1, 0) + pltpu.roll(q, 1, 0)
            new = q + c_ref[x] * (n - 4.0 * q)
            if last:
                f_ref[x - depth] = new[:width_y]
            else:
                dst[x] = new
            return carry

        lax.fori_loop(p + 1, rows_ext - 1 - p, one, 0)

    for p in range(PASSES):
        src, dst = (e_ref, a_ref) if p % 2 == 0 else (a_ref, e_ref)
        sweep(src, dst, p, p == PASSES - 1)


def finish_kernel(slot_ref, act_ref, r_ref, f_ref, uo_ref, vo_ref, d_ref):
    levels_x, width_y = uo_ref.shape
    cells, features = f_ref.shape
    levels = features // 2
    width_x = levels_x // levels

    def copy_tile(x, carry):
        at = pl.ds(pl.multiple_of(x * width_y, width_y), width_y)
        d_ref[at, :] = f_ref[at, :]
        return carry

    lax.fori_loop(0, width_x, copy_tile, 0)

    def place(r, carry):
        at = pl.ds(act_ref[r], 1)
        d_ref[at, :] = d_ref[at, :] + r_ref[pl.ds(slot_ref[r], 1), :]
        return carry

    lax.fori_loop(0, act_ref.shape[0], place, 0, unroll=8)

    def transpose_tile(x, carry):
        tile = d_ref[pl.ds(pl.multiple_of(x * width_y, width_y), width_y), :].T
        uo_ref[pl.ds(x, levels, stride=width_x), :] = tile[:levels]
        vo_ref[pl.ds(x, levels, stride=width_x), :] = tile[levels:]
        return carry

    lax.fori_loop(0, width_x, transpose_tile, 0)


def body(
    u_field,
    v_field,
    diffusivity,
    active_columns,
    regimes,
    first_layer,
    second_layer,
    third_layer,
    last_layer,
):
    levels, width_x, width_y = u_field.shape
    features = 2 * levels
    cells = width_x * width_y
    active_count = active_columns.shape[0]
    devices_all = lax.axis_size(("tile", "inf"))
    capacity = 2 * active_count // devices_all
    slot_total = devices_all * capacity
    block_rows = min(512, active_count)
    block_count = active_count // block_rows
    target = regimes[:, 0]
    labels = jnp.arange(devices_all, dtype=jnp.int32)
    one_hot = (
        (target[:, None] == labels[None, :])
        .astype(jnp.bfloat16)
        .reshape(block_count, block_rows, devices_all)
    )
    row_ids = jnp.arange(block_rows, dtype=jnp.int32)
    lower = (row_ids[:, None] > row_ids[None, :]).astype(jnp.bfloat16)

    def rank_step(counts, piece):
        earlier = jnp.dot(lower, piece, preferred_element_type=jnp.float32) + counts[None, :]
        wide_piece = piece.astype(jnp.float32)
        rank = jnp.sum(earlier * wide_piece, axis=1)
        return (counts + jnp.sum(wide_piece, axis=0), rank)

    _, ranks = lax.scan(rank_step, jnp.zeros((devices_all,), jnp.float32), one_hot)
    slot_index = target * capacity + ranks.reshape(-1).astype(jnp.int32)
    vmem = pl.BlockSpec(memory_space=pltpu.VMEM)
    smem = pl.BlockSpec(memory_space=pltpu.SMEM)
    depth = PASSES
    u_before, u_after = halos(u_field, "tile", 1, depth)
    v_before, v_after = halos(v_field, "tile", 1, depth)
    x_before = jnp.concatenate([u_before, v_before], axis=0).transpose(1, 2, 0)
    x_after = jnp.concatenate([u_after, v_after], axis=0).transpose(1, 2, 0)

    def edge_columns(start):
        pieces = []
        for field, before, after in ((u_field, u_before, u_after), (v_field, v_before, v_after)):
            column = lambda a: lax.slice_in_dim(a, start, start + depth, axis=2)
            pieces.append(
                jnp.concatenate([column(before), column(field), column(after)], axis=1)
            )
        return jnp.concatenate(pieces, axis=0).transpose(1, 2, 0)

    inf_count = lax.axis_size("inf")
    up = [(i, i + 1) for i in range(inf_count - 1)]
    down = [(j, i) for i, j in up]
    y_before = lax.ppermute(edge_columns(width_y - depth), "inf", up)
    y_after = lax.ppermute(edge_columns(0), "inf", down)
    y_halo = jnp.concatenate([y_after, y_before], axis=1)
    c_before, c_after = halos(diffusivity, "tile", 0, depth)
    c_ext = jnp.concatenate([c_before, diffusivity, c_after], axis=0)
    c_before, c_after = halos(c_ext, "inf", 1, depth)
    c_ext = jnp.concatenate([c_ext, c_after, c_before], axis=1)
    rows_ext, ylen = c_ext.shape
    coeff = jnp.broadcast_to(c_ext[:, :, None], (rows_ext, ylen, features))
    u_rows = u_field.reshape(levels * width_x, width_y)
    v_rows = v_field.reshape(levels * width_x, width_y)
    state_t, outgoing = pl.pallas_call(
        gather_kernel,
        out_shape=(
            jax.ShapeDtypeStruct((cells, features), jnp.float32),
            jax.ShapeDtypeStruct((slot_total, features), jnp.float32),
        ),
        in_specs=[smem, smem, vmem, vmem],
        out_specs=(vmem, vmem),
    )(slot_index, active_columns, u_rows, v_rows)
    outgoing, x_before, x_after, y_halo, coeff = lax.optimization_barrier(
        (outgoing, x_before, x_after, y_halo, coeff)
    )
    state_t = state_t.reshape(width_x, width_y, features)
    block = lax.all_to_all(
        outgoing.reshape(devices_all, capacity, features),
        ("tile", "inf"),
        split_axis=0,
        concat_axis=0,
        tiled=True,
    )
    block_shape = block.shape
    rows = standardize(block.reshape(-1, features))
    result = network_rows(rows, first_layer[0], second_layer[0], third_layer[0], last_layer[0])
    answered = result.reshape(block_shape)
    returned = lax.all_to_all(answered, ("tile", "inf"), split_axis=0, concat_axis=0, tiled=True)
    returned_rows = returned.reshape(slot_total, features)

    diffused = pl.pallas_call(
        diffuse_kernel,
        out_shape=jax.ShapeDtypeStruct((width_x, width_y, features), jnp.float32),
        in_specs=[vmem] * 5,
        out_specs=vmem,
        scratch_shapes=[
            pltpu.VMEM((rows_ext, ylen, features), jnp.float32),
            pltpu.VMEM((rows_ext, ylen, features), jnp.float32),
        ],
        compiler_params=pltpu.CompilerParams(vmem_limit_bytes=100 * 1024 * 1024),
    )(state_t, x_before, x_after, y_halo, coeff)
    u_next, v_next = pl.pallas_call(
        finish_kernel,
        out_shape=(
            jax.ShapeDtypeStruct((levels * width_x, width_y), jnp.float32),
            jax.ShapeDtypeStruct((levels * width_x, width_y), jnp.float32),
        ),
        in_specs=[smem, smem, vmem, vmem],
        out_specs=(vmem, vmem),
        scratch_shapes=[pltpu.VMEM((cells, features), jnp.float32)],
    )(slot_index, active_columns, returned_rows, diffused.reshape(cells, features))
    return (u_next.reshape(u_field.shape), v_next.reshape(v_field.shape))


def solution(mesh):
    in_specs = (
        P(None, "tile", "inf"),
        P(None, "tile", "inf"),
        P("tile", "inf"),
        P(("tile", "inf")),
        P(("tile", "inf"), None),
        P(("tile", "inf"), None, None),
        P(("tile", "inf"), None, None),
        P(("tile", "inf"), None, None),
        P(("tile", "inf"), None, None),
    )
    out_specs = (P(None, "tile", "inf"), P(None, "tile", "inf"))
    return jax.shard_map(body, mesh=mesh, in_specs=in_specs, out_specs=out_specs, check_vma=False)
```

```python
import jax
import jax.numpy as jnp
from jax import lax
from jax.experimental import pallas as pl
from jax.experimental.pallas import tpu as pltpu
from jax.sharding import PartitionSpec as P

PASSES = 4


def halos(x, axis, dim, width):
    count, length = (lax.axis_size(axis), x.shape[dim])
    up = [(i, i + 1) for i in range(count - 1)]
    down = [(j, i) for i, j in up]
    last = lax.slice_in_dim(x, length - width, length, axis=dim)
    first = lax.slice_in_dim(x, 0, width, axis=dim)
    before = lax.ppermute(last, axis, up)
    after = lax.ppermute(first, axis, down)
    return before, after


def stencil_inputs(state_t, diffusivity, depth):
    width_x, width_y, features = state_t.shape
    pad_rows = lambda c: jnp.pad(c, ((0, width_y - c.shape[0]), (0, 0)))[None]

    def x_piece(start):
        rows = lax.slice_in_dim(diffusivity, start, start + depth, axis=0)
        return jnp.concatenate(
            [lax.slice_in_dim(state_t, start, start + depth, axis=0), pad_rows(rows)], axis=0
        )

    tile_count = lax.axis_size("tile")
    up = [(i, i + 1) for i in range(tile_count - 1)]
    down = [(j, i) for i, j in up]
    before = lax.ppermute(x_piece(width_x - depth), "tile", up)
    after = lax.ppermute(x_piece(0), "tile", down)
    x_before, x_after = before[:depth], after[:depth]
    c_rows = jnp.concatenate([before[depth, :depth], diffusivity, after[depth, :depth]], axis=0)
    extended = jnp.concatenate([x_before, state_t, x_after], axis=0)

    def y_piece(start):
        rows = lax.slice_in_dim(extended, start, start + depth, axis=1)
        cols = lax.slice_in_dim(c_rows, start, start + depth, axis=1).T
        cols = jnp.pad(cols, ((0, 0), (0, features - cols.shape[1])))
        return jnp.concatenate([rows, cols[None]], axis=0)

    inf_count = lax.axis_size("inf")
    up = [(i, i + 1) for i in range(inf_count - 1)]
    down = [(j, i) for i, j in up]
    before = lax.ppermute(y_piece(width_y - depth), "inf", up)
    after = lax.ppermute(y_piece(0), "inf", down)
    rows_ext = extended.shape[0]
    y_halo = jnp.concatenate([after[:rows_ext], before[:rows_ext]], axis=1)
    c_ext = jnp.concatenate(
        [c_rows, after[rows_ext, :, :rows_ext].T, before[rows_ext, :, :rows_ext].T], axis=1
    )
    ylen = c_ext.shape[1]
    coeff = jnp.broadcast_to(c_ext[:, :, None], (rows_ext, ylen, features))
    return x_before, x_after, y_halo, coeff


def standardize(rows):
    center = jnp.mean(rows, axis=-1, keepdims=True)
    spread = jnp.mean(jnp.square(rows - center), axis=-1, keepdims=True)
    return (rows - center) * lax.rsqrt(spread + 1e-05)


def network_rows(rows, first_layer, second_layer, third_layer, last_layer):
    highest = lax.Precision.HIGH
    hidden = jax.nn.silu(jnp.dot(rows, first_layer, precision=highest))
    hidden = jax.nn.silu(jnp.dot(hidden, second_layer, precision=highest))
    hidden = jax.nn.silu(jnp.dot(hidden, third_layer, precision=highest))
    return jnp.dot(hidden, last_layer, precision=highest)


def gather_kernel(slot_ref, act_ref, u_ref, v_ref, st_ref, o_ref):
    levels_x, width_y = u_ref.shape
    cells, features = st_ref.shape
    levels = features // 2
    width_x = levels_x // levels
    chunk = 128

    def clear(k, carry):
        at = pl.ds(pl.multiple_of(k * chunk, chunk), chunk)
        o_ref[at, :] = jnp.zeros((chunk, features), jnp.float32)
        return carry

    lax.fori_loop(0, o_ref.shape[0] // chunk, clear, 0)

    def transpose_tile(x, carry):
        a = u_ref[pl.ds(x, levels, stride=width_x), :]
        b = v_ref[pl.ds(x, levels, stride=width_x), :]
        tile = jnp.concatenate([a, b], axis=0)
        st_ref[pl.ds(pl.multiple_of(x * width_y, width_y), width_y), :] = tile.T
        return carry

    lax.fori_loop(0, width_x, transpose_tile, 0)

    def place(r, carry):
        o_ref[pl.ds(slot_ref[r], 1), :] = st_ref[pl.ds(act_ref[r], 1), :]
        return carry

    lax.fori_loop(0, act_ref.shape[0], place, 0, unroll=8)


def diffuse_kernel(st_ref, xb_ref, xa_ref, yh_ref, c_ref, f_ref, e_ref, a_ref):
    width_x, width_y, _ = st_ref.shape
    depth = xb_ref.shape[0]
    rows_ext, ylen, _ = c_ref.shape
    e_ref[0:depth, 0:width_y, :] = xb_ref[...]
    e_ref[depth + width_x :, 0:width_y, :] = xa_ref[...]

    def fill(x, carry):
        e_ref[x + depth, 0:width_y, :] = st_ref[x]
        return carry

    lax.fori_loop(0, width_x, fill, 0)
    e_ref[:, width_y:, :] = yh_ref[...]

    def sweep(src, dst, p, last):
        def one(x, carry):
            q = src[x]
            n = src[x + 1] + src[x - 1]
            n = n + pltpu.roll(q, ylen - 1, 0) + pltpu.roll(q, 1, 0)
            new = q + c_ref[x] * (n - 4.0 * q)
            if last:
                f_ref[x - depth] = new[:width_y]
            else:
                dst[x] = new
            return carry

        lax.fori_loop(p + 1, rows_ext - 1 - p, one, 0)

    for p in range(PASSES):
        src, dst = (e_ref, a_ref) if p % 2 == 0 else (a_ref, e_ref)
        sweep(src, dst, p, p == PASSES - 1)


def finish_kernel(slot_ref, act_ref, r_ref, f_ref, uo_ref, vo_ref, d_ref):
    levels_x, width_y = uo_ref.shape
    cells, features = f_ref.shape
    levels = features // 2
    width_x = levels_x // levels

    def copy_tile(x, carry):
        at = pl.ds(pl.multiple_of(x * width_y, width_y), width_y)
        d_ref[at, :] = f_ref[at, :]
        return carry

    lax.fori_loop(0, width_x, copy_tile, 0)

    def place(r, carry):
        at = pl.ds(act_ref[r], 1)
        d_ref[at, :] = d_ref[at, :] + r_ref[pl.ds(slot_ref[r], 1), :]
        return carry

    lax.fori_loop(0, act_ref.shape[0], place, 0, unroll=8)

    def transpose_tile(x, carry):
        tile = d_ref[pl.ds(pl.multiple_of(x * width_y, width_y), width_y), :].T
        uo_ref[pl.ds(x, levels, stride=width_x), :] = tile[:levels]
        vo_ref[pl.ds(x, levels, stride=width_x), :] = tile[levels:]
        return carry

    lax.fori_loop(0, width_x, transpose_tile, 0)


def body(
    u_field,
    v_field,
    diffusivity,
    active_columns,
    regimes,
    first_layer,
    second_layer,
    third_layer,
    last_layer,
):
    levels, width_x, width_y = u_field.shape
    features = 2 * levels
    cells = width_x * width_y
    active_count = active_columns.shape[0]
    devices_all = lax.axis_size(("tile", "inf"))
    capacity = 2 * active_count // devices_all
    slot_total = devices_all * capacity
    block_rows = min(512, active_count)
    block_count = active_count // block_rows
    target = regimes[:, 0]
    labels = jnp.arange(devices_all, dtype=jnp.int32)
    one_hot = (
        (target[:, None] == labels[None, :])
        .astype(jnp.bfloat16)
        .reshape(block_count, block_rows, devices_all)
    )
    row_ids = jnp.arange(block_rows, dtype=jnp.int32)
    lower = (row_ids[:, None] > row_ids[None, :]).astype(jnp.bfloat16)

    def rank_step(counts, piece):
        earlier = jnp.dot(lower, piece, preferred_element_type=jnp.float32) + counts[None, :]
        wide_piece = piece.astype(jnp.float32)
        rank = jnp.sum(earlier * wide_piece, axis=1)
        return (counts + jnp.sum(wide_piece, axis=0), rank)

    _, ranks = lax.scan(rank_step, jnp.zeros((devices_all,), jnp.float32), one_hot)
    slot_index = target * capacity + ranks.reshape(-1).astype(jnp.int32)
    vmem = pl.BlockSpec(memory_space=pltpu.VMEM)
    smem = pl.BlockSpec(memory_space=pltpu.SMEM)
    u_rows = u_field.reshape(levels * width_x, width_y)
    v_rows = v_field.reshape(levels * width_x, width_y)
    state_t, outgoing = pl.pallas_call(
        gather_kernel,
        out_shape=(
            jax.ShapeDtypeStruct((cells, features), jnp.float32),
            jax.ShapeDtypeStruct((slot_total, features), jnp.float32),
        ),
        in_specs=[smem, smem, vmem, vmem],
        out_specs=(vmem, vmem),
    )(slot_index, active_columns, u_rows, v_rows)
    block = lax.all_to_all(
        outgoing.reshape(devices_all, capacity, features),
        ("tile", "inf"),
        split_axis=0,
        concat_axis=0,
        tiled=True,
    )
    block_shape = block.shape
    block, state_t = lax.optimization_barrier((block, state_t))
    state_t = state_t.reshape(width_x, width_y, features)
    x_before, x_after, y_halo, coeff = stencil_inputs(state_t, diffusivity, PASSES)
    rows = standardize(block.reshape(-1, features))
    result = network_rows(rows, first_layer[0], second_layer[0], third_layer[0], last_layer[0])
    answered = result.reshape(block_shape)
    answered, x_before, x_after, y_halo, coeff = lax.optimization_barrier(
        (answered, x_before, x_after, y_halo, coeff)
    )
    returned = lax.all_to_all(answered, ("tile", "inf"), split_axis=0, concat_axis=0, tiled=True)
    returned_rows = returned.reshape(slot_total, features)

    rows_ext, ylen = coeff.shape[:2]
    diffused = pl.pallas_call(
        diffuse_kernel,
        out_shape=jax.ShapeDtypeStruct((width_x, width_y, features), jnp.float32),
        in_specs=[vmem] * 5,
        out_specs=vmem,
        scratch_shapes=[
            pltpu.VMEM((rows_ext, ylen, features), jnp.float32),
            pltpu.VMEM((rows_ext, ylen, features), jnp.float32),
        ],
        compiler_params=pltpu.CompilerParams(vmem_limit_bytes=100 * 1024 * 1024),
    )(state_t, x_before, x_after, y_halo, coeff)
    u_next, v_next = pl.pallas_call(
        finish_kernel,
        out_shape=(
            jax.ShapeDtypeStruct((levels * width_x, width_y), jnp.float32),
            jax.ShapeDtypeStruct((levels * width_x, width_y), jnp.float32),
        ),
        in_specs=[smem, smem, vmem, vmem],
        out_specs=(vmem, vmem),
        scratch_shapes=[pltpu.VMEM((cells, features), jnp.float32)],
    )(slot_index, active_columns, returned_rows, diffused.reshape(cells, features))
    return (u_next.reshape(u_field.shape), v_next.reshape(v_field.shape))


def solution(mesh):
    in_specs = (
        P(None, "tile", "inf"),
        P(None, "tile", "inf"),
        P("tile", "inf"),
        P(("tile", "inf")),
        P(("tile", "inf"), None),
        P(("tile", "inf"), None, None),
        P(("tile", "inf"), None, None),
        P(("tile", "inf"), None, None),
        P(("tile", "inf"), None, None),
    )
    out_specs = (P(None, "tile", "inf"), P(None, "tile", "inf"))
    return jax.shard_map(body, mesh=mesh, in_specs=in_specs, out_specs=out_specs, check_vma=False)
```

```python
import jax
import jax.numpy as jnp
from jax import lax
from jax.experimental import pallas as pl
from jax.experimental.pallas import tpu as pltpu
from jax.sharding import PartitionSpec as P

PASSES = 4


def halos(x, axis, dim, width):
    count, length = (lax.axis_size(axis), x.shape[dim])
    up = [(i, i + 1) for i in range(count - 1)]
    down = [(j, i) for i, j in up]
    last = lax.slice_in_dim(x, length - width, length, axis=dim)
    first = lax.slice_in_dim(x, 0, width, axis=dim)
    before = lax.ppermute(last, axis, up)
    after = lax.ppermute(first, axis, down)
    return before, after


def stencil_start(state_t, diffusivity, depth):
    width_x, width_y, features = state_t.shape
    pad_rows = lambda c: jnp.pad(c, ((0, width_y - c.shape[0]), (0, 0)))[None]

    def x_piece(start):
        rows = lax.slice_in_dim(diffusivity, start, start + depth, axis=0)
        return jnp.concatenate(
            [lax.slice_in_dim(state_t, start, start + depth, axis=0), pad_rows(rows)], axis=0
        )

    tile_count = lax.axis_size("tile")
    up = [(i, i + 1) for i in range(tile_count - 1)]
    down = [(j, i) for i, j in up]
    before = lax.ppermute(x_piece(width_x - depth), "tile", up)
    after = lax.ppermute(x_piece(0), "tile", down)
    return before, after


def stencil_finish(state_t, diffusivity, before, after, depth):
    width_x, width_y, features = state_t.shape
    x_before, x_after = before[:depth], after[:depth]
    c_rows = jnp.concatenate([before[depth, :depth], diffusivity, after[depth, :depth]], axis=0)
    extended = jnp.concatenate([x_before, state_t, x_after], axis=0)

    def y_piece(start):
        rows = lax.slice_in_dim(extended, start, start + depth, axis=1)
        cols = lax.slice_in_dim(c_rows, start, start + depth, axis=1).T
        cols = jnp.pad(cols, ((0, 0), (0, features - cols.shape[1])))
        return jnp.concatenate([rows, cols[None]], axis=0)

    inf_count = lax.axis_size("inf")
    up = [(i, i + 1) for i in range(inf_count - 1)]
    down = [(j, i) for i, j in up]
    before = lax.ppermute(y_piece(width_y - depth), "inf", up)
    after = lax.ppermute(y_piece(0), "inf", down)
    rows_ext = extended.shape[0]
    y_halo = jnp.concatenate([after[:rows_ext], before[:rows_ext]], axis=1)
    c_ext = jnp.concatenate(
        [c_rows, after[rows_ext, :, :rows_ext].T, before[rows_ext, :, :rows_ext].T], axis=1
    )
    ylen = c_ext.shape[1]
    coeff = jnp.broadcast_to(c_ext[:, :, None], (rows_ext, ylen, features))
    return x_before, x_after, y_halo, coeff


def standardize(rows):
    center = jnp.mean(rows, axis=-1, keepdims=True)
    spread = jnp.mean(jnp.square(rows - center), axis=-1, keepdims=True)
    return (rows - center) * lax.rsqrt(spread + 1e-05)


def network_rows(rows, first_layer, second_layer, third_layer, last_layer):
    highest = lax.Precision.HIGH
    hidden = jax.nn.silu(jnp.dot(rows, first_layer, precision=highest))
    hidden = jax.nn.silu(jnp.dot(hidden, second_layer, precision=highest))
    hidden = jax.nn.silu(jnp.dot(hidden, third_layer, precision=highest))
    return jnp.dot(hidden, last_layer, precision=highest)


def gather_kernel(slot_ref, act_ref, u_ref, v_ref, st_ref, o_ref):
    levels_x, width_y = u_ref.shape
    cells, features = st_ref.shape
    levels = features // 2
    width_x = levels_x // levels
    chunk = 128

    def clear(k, carry):
        at = pl.ds(pl.multiple_of(k * chunk, chunk), chunk)
        o_ref[at, :] = jnp.zeros((chunk, features), jnp.float32)
        return carry

    lax.fori_loop(0, o_ref.shape[0] // chunk, clear, 0)

    def transpose_tile(x, carry):
        a = u_ref[pl.ds(x, levels, stride=width_x), :]
        b = v_ref[pl.ds(x, levels, stride=width_x), :]
        tile = jnp.concatenate([a, b], axis=0)
        st_ref[pl.ds(pl.multiple_of(x * width_y, width_y), width_y), :] = tile.T
        return carry

    lax.fori_loop(0, width_x, transpose_tile, 0)

    def place(r, carry):
        o_ref[pl.ds(slot_ref[r], 1), :] = st_ref[pl.ds(act_ref[r], 1), :]
        return carry

    lax.fori_loop(0, act_ref.shape[0], place, 0, unroll=8)


def diffuse_kernel(st_ref, xb_ref, xa_ref, yh_ref, c_ref, f_ref, e_ref, a_ref):
    width_x, width_y, _ = st_ref.shape
    depth = xb_ref.shape[0]
    rows_ext, ylen, _ = c_ref.shape
    e_ref[0:depth, 0:width_y, :] = xb_ref[...]
    e_ref[depth + width_x :, 0:width_y, :] = xa_ref[...]

    def fill(x, carry):
        e_ref[x + depth, 0:width_y, :] = st_ref[x]
        return carry

    lax.fori_loop(0, width_x, fill, 0)
    e_ref[:, width_y:, :] = yh_ref[...]

    def sweep(src, dst, p, last):
        def one(x, carry):
            q = src[x]
            n = src[x + 1] + src[x - 1]
            n = n + pltpu.roll(q, ylen - 1, 0) + pltpu.roll(q, 1, 0)
            new = q + c_ref[x] * (n - 4.0 * q)
            if last:
                f_ref[x - depth] = new[:width_y]
            else:
                dst[x] = new
            return carry

        lax.fori_loop(p + 1, rows_ext - 1 - p, one, 0)

    for p in range(PASSES):
        src, dst = (e_ref, a_ref) if p % 2 == 0 else (a_ref, e_ref)
        sweep(src, dst, p, p == PASSES - 1)


def finish_kernel(slot_ref, act_ref, r_ref, f_ref, uo_ref, vo_ref, d_ref):
    levels_x, width_y = uo_ref.shape
    cells, features = f_ref.shape
    levels = features // 2
    width_x = levels_x // levels

    def copy_tile(x, carry):
        at = pl.ds(pl.multiple_of(x * width_y, width_y), width_y)
        d_ref[at, :] = f_ref[at, :]
        return carry

    lax.fori_loop(0, width_x, copy_tile, 0)

    def place(r, carry):
        at = pl.ds(act_ref[r], 1)
        d_ref[at, :] = d_ref[at, :] + r_ref[pl.ds(slot_ref[r], 1), :]
        return carry

    lax.fori_loop(0, act_ref.shape[0], place, 0, unroll=8)

    def transpose_tile(x, carry):
        tile = d_ref[pl.ds(pl.multiple_of(x * width_y, width_y), width_y), :].T
        uo_ref[pl.ds(x, levels, stride=width_x), :] = tile[:levels]
        vo_ref[pl.ds(x, levels, stride=width_x), :] = tile[levels:]
        return carry

    lax.fori_loop(0, width_x, transpose_tile, 0)


def body(
    u_field,
    v_field,
    diffusivity,
    active_columns,
    regimes,
    first_layer,
    second_layer,
    third_layer,
    last_layer,
):
    levels, width_x, width_y = u_field.shape
    features = 2 * levels
    cells = width_x * width_y
    active_count = active_columns.shape[0]
    devices_all = lax.axis_size(("tile", "inf"))
    capacity = 2 * active_count // devices_all
    slot_total = devices_all * capacity
    block_rows = min(512, active_count)
    block_count = active_count // block_rows
    target = regimes[:, 0]
    labels = jnp.arange(devices_all, dtype=jnp.int32)
    one_hot = (
        (target[:, None] == labels[None, :])
        .astype(jnp.bfloat16)
        .reshape(block_count, block_rows, devices_all)
    )
    row_ids = jnp.arange(block_rows, dtype=jnp.int32)
    lower = (row_ids[:, None] > row_ids[None, :]).astype(jnp.bfloat16)

    def rank_step(counts, piece):
        earlier = jnp.dot(lower, piece, preferred_element_type=jnp.float32) + counts[None, :]
        wide_piece = piece.astype(jnp.float32)
        rank = jnp.sum(earlier * wide_piece, axis=1)
        return (counts + jnp.sum(wide_piece, axis=0), rank)

    _, ranks = lax.scan(rank_step, jnp.zeros((devices_all,), jnp.float32), one_hot)
    slot_index = target * capacity + ranks.reshape(-1).astype(jnp.int32)
    vmem = pl.BlockSpec(memory_space=pltpu.VMEM)
    smem = pl.BlockSpec(memory_space=pltpu.SMEM)
    u_rows = u_field.reshape(levels * width_x, width_y)
    v_rows = v_field.reshape(levels * width_x, width_y)
    state_t, outgoing = pl.pallas_call(
        gather_kernel,
        out_shape=(
            jax.ShapeDtypeStruct((cells, features), jnp.float32),
            jax.ShapeDtypeStruct((slot_total, features), jnp.float32),
        ),
        in_specs=[smem, smem, vmem, vmem],
        out_specs=(vmem, vmem),
    )(slot_index, active_columns, u_rows, v_rows)
    state_t = state_t.reshape(width_x, width_y, features)
    x_from_before, x_from_after = stencil_start(state_t, diffusivity, PASSES)
    outgoing, x_from_before, x_from_after = lax.optimization_barrier(
        (outgoing, x_from_before, x_from_after)
    )
    block = lax.all_to_all(
        outgoing.reshape(devices_all, capacity, features),
        ("tile", "inf"),
        split_axis=0,
        concat_axis=0,
        tiled=True,
    )
    block_shape = block.shape
    x_before, x_after, y_halo, coeff = stencil_finish(
        state_t, diffusivity, x_from_before, x_from_after, PASSES
    )
    rows_ext, ylen = coeff.shape[:2]
    diffused = pl.pallas_call(
        diffuse_kernel,
        out_shape=jax.ShapeDtypeStruct((width_x, width_y, features), jnp.float32),
        in_specs=[vmem] * 5,
        out_specs=vmem,
        scratch_shapes=[
            pltpu.VMEM((rows_ext, ylen, features), jnp.float32),
            pltpu.VMEM((rows_ext, ylen, features), jnp.float32),
        ],
        compiler_params=pltpu.CompilerParams(vmem_limit_bytes=100 * 1024 * 1024),
    )(state_t, x_before, x_after, y_halo, coeff)
    block, diffused = lax.optimization_barrier((block, diffused))
    rows = standardize(block.reshape(-1, features))
    result = network_rows(rows, first_layer[0], second_layer[0], third_layer[0], last_layer[0])
    answered = result.reshape(block_shape)
    returned = lax.all_to_all(answered, ("tile", "inf"), split_axis=0, concat_axis=0, tiled=True)
    returned_rows = returned.reshape(slot_total, features)

    u_next, v_next = pl.pallas_call(
        finish_kernel,
        out_shape=(
            jax.ShapeDtypeStruct((levels * width_x, width_y), jnp.float32),
            jax.ShapeDtypeStruct((levels * width_x, width_y), jnp.float32),
        ),
        in_specs=[smem, smem, vmem, vmem],
        out_specs=(vmem, vmem),
        scratch_shapes=[pltpu.VMEM((cells, features), jnp.float32)],
    )(slot_index, active_columns, returned_rows, diffused.reshape(cells, features))
    return (u_next.reshape(u_field.shape), v_next.reshape(v_field.shape))


def solution(mesh):
    in_specs = (
        P(None, "tile", "inf"),
        P(None, "tile", "inf"),
        P("tile", "inf"),
        P(("tile", "inf")),
        P(("tile", "inf"), None),
        P(("tile", "inf"), None, None),
        P(("tile", "inf"), None, None),
        P(("tile", "inf"), None, None),
        P(("tile", "inf"), None, None),
    )
    out_specs = (P(None, "tile", "inf"), P(None, "tile", "inf"))
    return jax.shard_map(body, mesh=mesh, in_specs=in_specs, out_specs=out_specs, check_vma=False)
```

```python
import jax
import jax.numpy as jnp
from jax import lax
from jax.experimental import pallas as pl
from jax.experimental.pallas import tpu as pltpu
from jax.sharding import PartitionSpec as P

PASSES = 4


def halos(x, axis, dim, width):
    count, length = (lax.axis_size(axis), x.shape[dim])
    up = [(i, i + 1) for i in range(count - 1)]
    down = [(j, i) for i, j in up]
    last = lax.slice_in_dim(x, length - width, length, axis=dim)
    first = lax.slice_in_dim(x, 0, width, axis=dim)
    before = lax.ppermute(last, axis, up)
    after = lax.ppermute(first, axis, down)
    return before, after


def stencil_start(u_field, v_field, diffusivity, depth):
    width_x = u_field.shape[1]

    def x_piece(start):
        rows = lambda a: lax.slice_in_dim(a, start, start + depth, axis=a.ndim - 2)
        return jnp.concatenate([rows(u_field), rows(v_field), rows(diffusivity)[None]], axis=0)

    tile_count = lax.axis_size("tile")
    up = [(i, i + 1) for i in range(tile_count - 1)]
    down = [(j, i) for i, j in up]
    before = lax.ppermute(x_piece(width_x - depth), "tile", up)
    after = lax.ppermute(x_piece(0), "tile", down)
    return before, after


def stencil_finish(state_t, diffusivity, before, after, depth):
    width_x, width_y, features = state_t.shape
    x_before = before[:features].transpose(1, 2, 0)
    x_after = after[:features].transpose(1, 2, 0)
    c_rows = jnp.concatenate([before[features], diffusivity, after[features]], axis=0)
    extended = jnp.concatenate([x_before, state_t, x_after], axis=0)

    def y_piece(start):
        rows = lax.slice_in_dim(extended, start, start + depth, axis=1)
        cols = lax.slice_in_dim(c_rows, start, start + depth, axis=1).T
        cols = jnp.pad(cols, ((0, 0), (0, features - cols.shape[1])))
        return jnp.concatenate([rows, cols[None]], axis=0)

    inf_count = lax.axis_size("inf")
    up = [(i, i + 1) for i in range(inf_count - 1)]
    down = [(j, i) for i, j in up]
    before = lax.ppermute(y_piece(width_y - depth), "inf", up)
    after = lax.ppermute(y_piece(0), "inf", down)
    rows_ext = extended.shape[0]
    y_halo = jnp.concatenate([after[:rows_ext], before[:rows_ext]], axis=1)
    c_ext = jnp.concatenate(
        [c_rows, after[rows_ext, :, :rows_ext].T, before[rows_ext, :, :rows_ext].T], axis=1
    )
    ylen = c_ext.shape[1]
    coeff = jnp.broadcast_to(c_ext[:, :, None], (rows_ext, ylen, features))
    return x_before, x_after, y_halo, coeff


def standardize(rows):
    center = jnp.mean(rows, axis=-1, keepdims=True)
    spread = jnp.mean(jnp.square(rows - center), axis=-1, keepdims=True)
    return (rows - center) * lax.rsqrt(spread + 1e-05)


def network_rows(rows, first_layer, second_layer, third_layer, last_layer):
    highest = lax.Precision.HIGH
    hidden = jax.nn.silu(jnp.dot(rows, first_layer, precision=highest))
    hidden = jax.nn.silu(jnp.dot(hidden, second_layer, precision=highest))
    hidden = jax.nn.silu(jnp.dot(hidden, third_layer, precision=highest))
    return jnp.dot(hidden, last_layer, precision=highest)


def gather_kernel(slot_ref, act_ref, u_ref, v_ref, st_ref, o_ref):
    levels_x, width_y = u_ref.shape
    cells, features = st_ref.shape
    levels = features // 2
    width_x = levels_x // levels
    chunk = 128

    def clear(k, carry):
        at = pl.ds(pl.multiple_of(k * chunk, chunk), chunk)
        o_ref[at, :] = jnp.zeros((chunk, features), jnp.float32)
        return carry

    lax.fori_loop(0, o_ref.shape[0] // chunk, clear, 0)

    def transpose_tile(x, carry):
        a = u_ref[pl.ds(x, levels, stride=width_x), :]
        b = v_ref[pl.ds(x, levels, stride=width_x), :]
        tile = jnp.concatenate([a, b], axis=0)
        st_ref[pl.ds(pl.multiple_of(x * width_y, width_y), width_y), :] = tile.T
        return carry

    lax.fori_loop(0, width_x, transpose_tile, 0)

    def place(r, carry):
        o_ref[pl.ds(slot_ref[r], 1), :] = st_ref[pl.ds(act_ref[r], 1), :]
        return carry

    lax.fori_loop(0, act_ref.shape[0], place, 0, unroll=8)


def diffuse_kernel(st_ref, xb_ref, xa_ref, yh_ref, c_ref, f_ref, e_ref, a_ref):
    width_x, width_y, _ = st_ref.shape
    depth = xb_ref.shape[0]
    rows_ext, ylen, _ = c_ref.shape
    e_ref[0:depth, 0:width_y, :] = xb_ref[...]
    e_ref[depth + width_x :, 0:width_y, :] = xa_ref[...]

    def fill(x, carry):
        e_ref[x + depth, 0:width_y, :] = st_ref[x]
        return carry

    lax.fori_loop(0, width_x, fill, 0)
    e_ref[:, width_y:, :] = yh_ref[...]

    def sweep(src, dst, p, last):
        def one(x, carry):
            q = src[x]
            n = src[x + 1] + src[x - 1]
            n = n + pltpu.roll(q, ylen - 1, 0) + pltpu.roll(q, 1, 0)
            new = q + c_ref[x] * (n - 4.0 * q)
            if last:
                f_ref[x - depth] = new[:width_y]
            else:
                dst[x] = new
            return carry

        lax.fori_loop(p + 1, rows_ext - 1 - p, one, 0)

    for p in range(PASSES):
        src, dst = (e_ref, a_ref) if p % 2 == 0 else (a_ref, e_ref)
        sweep(src, dst, p, p == PASSES - 1)


def finish_kernel(slot_ref, act_ref, r_ref, f_ref, uo_ref, vo_ref, d_ref):
    levels_x, width_y = uo_ref.shape
    cells, features = f_ref.shape
    levels = features // 2
    width_x = levels_x // levels

    def copy_tile(x, carry):
        at = pl.ds(pl.multiple_of(x * width_y, width_y), width_y)
        d_ref[at, :] = f_ref[at, :]
        return carry

    lax.fori_loop(0, width_x, copy_tile, 0)

    def place(r, carry):
        at = pl.ds(act_ref[r], 1)
        d_ref[at, :] = d_ref[at, :] + r_ref[pl.ds(slot_ref[r], 1), :]
        return carry

    lax.fori_loop(0, act_ref.shape[0], place, 0, unroll=8)

    def transpose_tile(x, carry):
        tile = d_ref[pl.ds(pl.multiple_of(x * width_y, width_y), width_y), :].T
        uo_ref[pl.ds(x, levels, stride=width_x), :] = tile[:levels]
        vo_ref[pl.ds(x, levels, stride=width_x), :] = tile[levels:]
        return carry

    lax.fori_loop(0, width_x, transpose_tile, 0)


def body(
    u_field,
    v_field,
    diffusivity,
    active_columns,
    regimes,
    first_layer,
    second_layer,
    third_layer,
    last_layer,
):
    levels, width_x, width_y = u_field.shape
    features = 2 * levels
    cells = width_x * width_y
    active_count = active_columns.shape[0]
    devices_all = lax.axis_size(("tile", "inf"))
    capacity = 2 * active_count // devices_all
    slot_total = devices_all * capacity
    block_rows = min(512, active_count)
    block_count = active_count // block_rows
    target = regimes[:, 0]
    labels = jnp.arange(devices_all, dtype=jnp.int32)
    one_hot = (
        (target[:, None] == labels[None, :])
        .astype(jnp.bfloat16)
        .reshape(block_count, block_rows, devices_all)
    )
    row_ids = jnp.arange(block_rows, dtype=jnp.int32)
    lower = (row_ids[:, None] > row_ids[None, :]).astype(jnp.bfloat16)

    def rank_step(counts, piece):
        earlier = jnp.dot(lower, piece, preferred_element_type=jnp.float32) + counts[None, :]
        wide_piece = piece.astype(jnp.float32)
        rank = jnp.sum(earlier * wide_piece, axis=1)
        return (counts + jnp.sum(wide_piece, axis=0), rank)

    _, ranks = lax.scan(rank_step, jnp.zeros((devices_all,), jnp.float32), one_hot)
    slot_index = target * capacity + ranks.reshape(-1).astype(jnp.int32)
    vmem = pl.BlockSpec(memory_space=pltpu.VMEM)
    smem = pl.BlockSpec(memory_space=pltpu.SMEM)
    x_from_before, x_from_after = stencil_start(u_field, v_field, diffusivity, PASSES)
    u_rows = u_field.reshape(levels * width_x, width_y)
    v_rows = v_field.reshape(levels * width_x, width_y)
    state_t, outgoing = pl.pallas_call(
        gather_kernel,
        out_shape=(
            jax.ShapeDtypeStruct((cells, features), jnp.float32),
            jax.ShapeDtypeStruct((slot_total, features), jnp.float32),
        ),
        in_specs=[smem, smem, vmem, vmem],
        out_specs=(vmem, vmem),
    )(slot_index, active_columns, u_rows, v_rows)
    state_t = state_t.reshape(width_x, width_y, features)
    outgoing, x_from_before, x_from_after = lax.optimization_barrier(
        (outgoing, x_from_before, x_from_after)
    )
    block = lax.all_to_all(
        outgoing.reshape(devices_all, capacity, features),
        ("tile", "inf"),
        split_axis=0,
        concat_axis=0,
        tiled=True,
    )
    block_shape = block.shape
    x_before, x_after, y_halo, coeff = stencil_finish(
        state_t, diffusivity, x_from_before, x_from_after, PASSES
    )
    rows_ext, ylen = coeff.shape[:2]
    diffused = pl.pallas_call(
        diffuse_kernel,
        out_shape=jax.ShapeDtypeStruct((width_x, width_y, features), jnp.float32),
        in_specs=[vmem] * 5,
        out_specs=vmem,
        scratch_shapes=[
            pltpu.VMEM((rows_ext, ylen, features), jnp.float32),
            pltpu.VMEM((rows_ext, ylen, features), jnp.float32),
        ],
        compiler_params=pltpu.CompilerParams(vmem_limit_bytes=100 * 1024 * 1024),
    )(state_t, x_before, x_after, y_halo, coeff)
    block, diffused = lax.optimization_barrier((block, diffused))
    rows = standardize(block.reshape(-1, features))
    result = network_rows(rows, first_layer[0], second_layer[0], third_layer[0], last_layer[0])
    answered = result.reshape(block_shape)
    returned = lax.all_to_all(answered, ("tile", "inf"), split_axis=0, concat_axis=0, tiled=True)
    returned_rows = returned.reshape(slot_total, features)

    u_next, v_next = pl.pallas_call(
        finish_kernel,
        out_shape=(
            jax.ShapeDtypeStruct((levels * width_x, width_y), jnp.float32),
            jax.ShapeDtypeStruct((levels * width_x, width_y), jnp.float32),
        ),
        in_specs=[smem, smem, vmem, vmem],
        out_specs=(vmem, vmem),
        scratch_shapes=[pltpu.VMEM((cells, features), jnp.float32)],
    )(slot_index, active_columns, returned_rows, diffused.reshape(cells, features))
    return (u_next.reshape(u_field.shape), v_next.reshape(v_field.shape))


def solution(mesh):
    in_specs = (
        P(None, "tile", "inf"),
        P(None, "tile", "inf"),
        P("tile", "inf"),
        P(("tile", "inf")),
        P(("tile", "inf"), None),
        P(("tile", "inf"), None, None),
        P(("tile", "inf"), None, None),
        P(("tile", "inf"), None, None),
        P(("tile", "inf"), None, None),
    )
    out_specs = (P(None, "tile", "inf"), P(None, "tile", "inf"))
    return jax.shard_map(body, mesh=mesh, in_specs=in_specs, out_specs=out_specs, check_vma=False)
```

```python
import jax
import jax.numpy as jnp
from jax import lax
from jax.experimental import pallas as pl
from jax.experimental.pallas import tpu as pltpu
from jax.sharding import PartitionSpec as P

PASSES = 4


def halos(x, axis, dim, width):
    count, length = (lax.axis_size(axis), x.shape[dim])
    up = [(i, i + 1) for i in range(count - 1)]
    down = [(j, i) for i, j in up]
    last = lax.slice_in_dim(x, length - width, length, axis=dim)
    first = lax.slice_in_dim(x, 0, width, axis=dim)
    before = lax.ppermute(last, axis, up)
    after = lax.ppermute(first, axis, down)
    return before, after


def stencil_start(u_field, v_field, diffusivity, depth):
    width_x = u_field.shape[1]

    def x_piece(start):
        rows = lambda a: lax.slice_in_dim(a, start, start + depth, axis=a.ndim - 2)
        return jnp.concatenate([rows(u_field), rows(v_field), rows(diffusivity)[None]], axis=0)

    tile_count = lax.axis_size("tile")
    up = [(i, i + 1) for i in range(tile_count - 1)]
    down = [(j, i) for i, j in up]
    before = lax.ppermute(x_piece(width_x - depth), "tile", up)
    after = lax.ppermute(x_piece(0), "tile", down)
    return before, after


def stencil_finish(state_t, diffusivity, before, after, depth):
    width_x, width_y, features = state_t.shape
    x_before = before[:features].transpose(1, 2, 0)
    x_after = after[:features].transpose(1, 2, 0)
    c_rows = jnp.concatenate([before[features], diffusivity, after[features]], axis=0)
    extended = jnp.concatenate([x_before, state_t, x_after], axis=0)

    def y_piece(start):
        rows = lax.slice_in_dim(extended, start, start + depth, axis=1)
        cols = lax.slice_in_dim(c_rows, start, start + depth, axis=1).T
        cols = jnp.pad(cols, ((0, 0), (0, features - cols.shape[1])))
        return jnp.concatenate([rows, cols[None]], axis=0)

    inf_count = lax.axis_size("inf")
    up = [(i, i + 1) for i in range(inf_count - 1)]
    down = [(j, i) for i, j in up]
    before = lax.ppermute(y_piece(width_y - depth), "inf", up)
    after = lax.ppermute(y_piece(0), "inf", down)
    rows_ext = extended.shape[0]
    y_halo = jnp.concatenate([after[:rows_ext], before[:rows_ext]], axis=1)
    c_ext = jnp.concatenate(
        [c_rows, after[rows_ext, :, :rows_ext].T, before[rows_ext, :, :rows_ext].T], axis=1
    )
    ylen = c_ext.shape[1]
    coeff = jnp.broadcast_to(c_ext[:, :, None], (rows_ext, ylen, features))
    return x_before, x_after, y_halo, coeff


def standardize(rows):
    center = jnp.mean(rows, axis=-1, keepdims=True)
    spread = jnp.mean(jnp.square(rows - center), axis=-1, keepdims=True)
    return (rows - center) * lax.rsqrt(spread + 1e-05)


def network_rows(rows, first_layer, second_layer, third_layer, last_layer):
    highest = lax.Precision.HIGH
    hidden = jax.nn.silu(jnp.dot(rows, first_layer, precision=highest))
    hidden = jax.nn.silu(jnp.dot(hidden, second_layer, precision=highest))
    hidden = jax.nn.silu(jnp.dot(hidden, third_layer, precision=highest))
    return jnp.dot(hidden, last_layer, precision=highest)


def gather_kernel(slot_ref, act_ref, u_ref, v_ref, st_ref, o_ref):
    levels_x, width_y = u_ref.shape
    cells, features = st_ref.shape
    levels = features // 2
    width_x = levels_x // levels
    chunk = 128

    def clear(k, carry):
        at = pl.ds(pl.multiple_of(k * chunk, chunk), chunk)
        o_ref[at, :] = jnp.zeros((chunk, features), jnp.float32)
        return carry

    lax.fori_loop(0, o_ref.shape[0] // chunk, clear, 0)

    def transpose_tile(x, carry):
        a = u_ref[pl.ds(x, levels, stride=width_x), :]
        b = v_ref[pl.ds(x, levels, stride=width_x), :]
        tile = jnp.concatenate([a, b], axis=0)
        st_ref[pl.ds(pl.multiple_of(x * width_y, width_y), width_y), :] = tile.T
        return carry

    lax.fori_loop(0, width_x, transpose_tile, 0)

    def place(r, carry):
        o_ref[pl.ds(slot_ref[r], 1), :] = st_ref[pl.ds(act_ref[r], 1), :]
        return carry

    lax.fori_loop(0, act_ref.shape[0], place, 0, unroll=8)


def diffuse_kernel(st_ref, xb_ref, xa_ref, yh_ref, c_ref, f_ref, e_ref, a_ref):
    width_x, width_y, _ = st_ref.shape
    depth = xb_ref.shape[0]
    rows_ext, ylen, _ = c_ref.shape
    e_ref[0:depth, 0:width_y, :] = xb_ref[...]
    e_ref[depth + width_x :, 0:width_y, :] = xa_ref[...]

    def fill(x, carry):
        e_ref[x + depth, 0:width_y, :] = st_ref[x]
        return carry

    lax.fori_loop(0, width_x, fill, 0)
    e_ref[:, width_y:, :] = yh_ref[...]

    def sweep(src, dst, p, last):
        def one(x, carry):
            q = src[x]
            n = src[x + 1] + src[x - 1]
            n = n + pltpu.roll(q, ylen - 1, 0) + pltpu.roll(q, 1, 0)
            new = q + c_ref[x] * (n - 4.0 * q)
            if last:
                f_ref[x - depth] = new[:width_y]
            else:
                dst[x] = new
            return carry

        lax.fori_loop(p + 1, rows_ext - 1 - p, one, 0)

    for p in range(PASSES):
        src, dst = (e_ref, a_ref) if p % 2 == 0 else (a_ref, e_ref)
        sweep(src, dst, p, p == PASSES - 1)


def finish_kernel(slot_ref, act_ref, r_ref, f_ref, uo_ref, vo_ref, d_ref):
    levels_x, width_y = uo_ref.shape
    cells, features = f_ref.shape
    levels = features // 2
    width_x = levels_x // levels

    def copy_tile(x, carry):
        at = pl.ds(pl.multiple_of(x * width_y, width_y), width_y)
        d_ref[at, :] = f_ref[at, :]
        return carry

    lax.fori_loop(0, width_x, copy_tile, 0)

    def place(r, carry):
        at = pl.ds(act_ref[r], 1)
        d_ref[at, :] = d_ref[at, :] + r_ref[pl.ds(slot_ref[r], 1), :]
        return carry

    lax.fori_loop(0, act_ref.shape[0], place, 0, unroll=8)

    def transpose_tile(x, carry):
        tile = d_ref[pl.ds(pl.multiple_of(x * width_y, width_y), width_y), :].T
        uo_ref[pl.ds(x, levels, stride=width_x), :] = tile[:levels]
        vo_ref[pl.ds(x, levels, stride=width_x), :] = tile[levels:]
        return carry

    lax.fori_loop(0, width_x, transpose_tile, 0)


def body(
    u_field,
    v_field,
    diffusivity,
    active_columns,
    regimes,
    first_layer,
    second_layer,
    third_layer,
    last_layer,
):
    levels, width_x, width_y = u_field.shape
    features = 2 * levels
    cells = width_x * width_y
    active_count = active_columns.shape[0]
    devices_all = lax.axis_size(("tile", "inf"))
    capacity = 2 * active_count // devices_all
    slot_total = devices_all * capacity
    block_rows = min(512, active_count)
    block_count = active_count // block_rows
    target = regimes[:, 0]
    labels = jnp.arange(devices_all, dtype=jnp.int32)
    one_hot = (
        (target[:, None] == labels[None, :])
        .astype(jnp.bfloat16)
        .reshape(block_count, block_rows, devices_all)
    )
    row_ids = jnp.arange(block_rows, dtype=jnp.int32)
    lower = (row_ids[:, None] > row_ids[None, :]).astype(jnp.bfloat16)

    def rank_step(counts, piece):
        earlier = jnp.dot(lower, piece, preferred_element_type=jnp.float32) + counts[None, :]
        wide_piece = piece.astype(jnp.float32)
        rank = jnp.sum(earlier * wide_piece, axis=1)
        return (counts + jnp.sum(wide_piece, axis=0), rank)

    _, ranks = lax.scan(rank_step, jnp.zeros((devices_all,), jnp.float32), one_hot)
    tile_count, inf_count = lax.axis_size("tile"), lax.axis_size("inf")
    half_tiles = tile_count // 2
    my_half = lax.axis_index("tile") // half_tiles
    target_tile = target // inf_count
    place = (target_tile % half_tiles) * inf_count + target % inf_count
    kind = (target_tile // half_tiles != my_half).astype(jnp.int32)
    pair_slots = 2 * capacity
    slot_index = place * pair_slots + kind * capacity + ranks.reshape(-1).astype(jnp.int32)
    groups = [
        [t * inf_count + i for t in range(h * half_tiles, (h + 1) * half_tiles) for i in range(inf_count)]
        for h in range(2)
    ]
    group_size = half_tiles * inf_count
    swap = [(t, (t + half_tiles) % tile_count) for t in range(tile_count)]
    mirrored = [
        lax.ppermute(w[0], "tile", swap) for w in (first_layer, second_layer, third_layer, last_layer)
    ]
    vmem = pl.BlockSpec(memory_space=pltpu.VMEM)
    smem = pl.BlockSpec(memory_space=pltpu.SMEM)
    x_from_before, x_from_after = stencil_start(u_field, v_field, diffusivity, PASSES)
    u_rows = u_field.reshape(levels * width_x, width_y)
    v_rows = v_field.reshape(levels * width_x, width_y)
    state_t, outgoing = pl.pallas_call(
        gather_kernel,
        out_shape=(
            jax.ShapeDtypeStruct((cells, features), jnp.float32),
            jax.ShapeDtypeStruct((slot_total, features), jnp.float32),
        ),
        in_specs=[smem, smem, vmem, vmem],
        out_specs=(vmem, vmem),
    )(slot_index, active_columns, u_rows, v_rows)
    state_t = state_t.reshape(width_x, width_y, features)
    outgoing, x_from_before, x_from_after, mirrored = lax.optimization_barrier(
        (outgoing, x_from_before, x_from_after, mirrored)
    )
    block = lax.all_to_all(
        outgoing.reshape(group_size, pair_slots, features),
        ("tile", "inf"),
        split_axis=0,
        concat_axis=0,
        tiled=True,
        axis_index_groups=groups,
    )
    block_shape = block.shape
    x_before, x_after, y_halo, coeff = stencil_finish(
        state_t, diffusivity, x_from_before, x_from_after, PASSES
    )
    rows_ext, ylen = coeff.shape[:2]
    diffused = pl.pallas_call(
        diffuse_kernel,
        out_shape=jax.ShapeDtypeStruct((width_x, width_y, features), jnp.float32),
        in_specs=[vmem] * 5,
        out_specs=vmem,
        scratch_shapes=[
            pltpu.VMEM((rows_ext, ylen, features), jnp.float32),
            pltpu.VMEM((rows_ext, ylen, features), jnp.float32),
        ],
        compiler_params=pltpu.CompilerParams(vmem_limit_bytes=100 * 1024 * 1024),
    )(state_t, x_before, x_after, y_halo, coeff)
    block, diffused = lax.optimization_barrier((block, diffused))
    own_rows = standardize(block[:, :capacity].reshape(-1, features))
    own = network_rows(own_rows, first_layer[0], second_layer[0], third_layer[0], last_layer[0])
    other_rows = standardize(block[:, capacity:].reshape(-1, features))
    other = network_rows(other_rows, *mirrored)
    answered = jnp.concatenate(
        [own.reshape(group_size, capacity, features), other.reshape(group_size, capacity, features)],
        axis=1,
    )
    returned = lax.all_to_all(
        answered,
        ("tile", "inf"),
        split_axis=0,
        concat_axis=0,
        tiled=True,
        axis_index_groups=groups,
    )
    returned_rows = returned.reshape(slot_total, features)

    u_next, v_next = pl.pallas_call(
        finish_kernel,
        out_shape=(
            jax.ShapeDtypeStruct((levels * width_x, width_y), jnp.float32),
            jax.ShapeDtypeStruct((levels * width_x, width_y), jnp.float32),
        ),
        in_specs=[smem, smem, vmem, vmem],
        out_specs=(vmem, vmem),
        scratch_shapes=[pltpu.VMEM((cells, features), jnp.float32)],
    )(slot_index, active_columns, returned_rows, diffused.reshape(cells, features))
    return (u_next.reshape(u_field.shape), v_next.reshape(v_field.shape))


def solution(mesh):
    in_specs = (
        P(None, "tile", "inf"),
        P(None, "tile", "inf"),
        P("tile", "inf"),
        P(("tile", "inf")),
        P(("tile", "inf"), None),
        P(("tile", "inf"), None, None),
        P(("tile", "inf"), None, None),
        P(("tile", "inf"), None, None),
        P(("tile", "inf"), None, None),
    )
    out_specs = (P(None, "tile", "inf"), P(None, "tile", "inf"))
    return jax.shard_map(body, mesh=mesh, in_specs=in_specs, out_specs=out_specs, check_vma=False)
```

```python
import jax
import jax.numpy as jnp
from jax import lax
from jax.experimental import pallas as pl
from jax.experimental.pallas import tpu as pltpu
from jax.sharding import PartitionSpec as P

PASSES = 4


def halos(x, axis, dim, width):
    count, length = (lax.axis_size(axis), x.shape[dim])
    up = [(i, i + 1) for i in range(count - 1)]
    down = [(j, i) for i, j in up]
    last = lax.slice_in_dim(x, length - width, length, axis=dim)
    first = lax.slice_in_dim(x, 0, width, axis=dim)
    before = lax.ppermute(last, axis, up)
    after = lax.ppermute(first, axis, down)
    return before, after


def stencil_start(u_field, v_field, diffusivity, depth):
    width_x = u_field.shape[1]

    def x_piece(start):
        rows = lambda a: lax.slice_in_dim(a, start, start + depth, axis=a.ndim - 2)
        return jnp.concatenate([rows(u_field), rows(v_field), rows(diffusivity)[None]], axis=0)

    tile_count = lax.axis_size("tile")
    up = [(i, i + 1) for i in range(tile_count - 1)]
    down = [(j, i) for i, j in up]
    before = lax.ppermute(x_piece(width_x - depth), "tile", up)
    after = lax.ppermute(x_piece(0), "tile", down)
    return before, after


def stencil_finish(state_t, diffusivity, before, after, depth):
    width_x, width_y, features = state_t.shape
    x_before = before[:features].transpose(1, 2, 0)
    x_after = after[:features].transpose(1, 2, 0)
    c_rows = jnp.concatenate([before[features], diffusivity, after[features]], axis=0)
    extended = jnp.concatenate([x_before, state_t, x_after], axis=0)

    def y_piece(start):
        rows = lax.slice_in_dim(extended, start, start + depth, axis=1)
        cols = lax.slice_in_dim(c_rows, start, start + depth, axis=1).T
        cols = jnp.pad(cols, ((0, 0), (0, features - cols.shape[1])))
        return jnp.concatenate([rows, cols[None]], axis=0)

    inf_count = lax.axis_size("inf")
    up = [(i, i + 1) for i in range(inf_count - 1)]
    down = [(j, i) for i, j in up]
    before = lax.ppermute(y_piece(width_y - depth), "inf", up)
    after = lax.ppermute(y_piece(0), "inf", down)
    rows_ext = extended.shape[0]
    y_halo = jnp.concatenate([after[:rows_ext], before[:rows_ext]], axis=1)
    c_ext = jnp.concatenate(
        [c_rows, after[rows_ext, :, :rows_ext].T, before[rows_ext, :, :rows_ext].T], axis=1
    )
    ylen = c_ext.shape[1]
    coeff = jnp.broadcast_to(c_ext[:, :, None], (rows_ext, ylen, features))
    return x_before, x_after, y_halo, coeff


def standardize(rows):
    center = jnp.mean(rows, axis=-1, keepdims=True)
    spread = jnp.mean(jnp.square(rows - center), axis=-1, keepdims=True)
    return (rows - center) * lax.rsqrt(spread + 1e-05)


def network_rows(rows, first_layer, second_layer, third_layer, last_layer):
    highest = lax.Precision.HIGH
    hidden = jax.nn.silu(jnp.dot(rows, first_layer, precision=highest))
    hidden = jax.nn.silu(jnp.dot(hidden, second_layer, precision=highest))
    hidden = jax.nn.silu(jnp.dot(hidden, third_layer, precision=highest))
    return jnp.dot(hidden, last_layer, precision=highest)


def gather_kernel(slot_ref, act_ref, u_ref, v_ref, st_ref, o_ref):
    levels_x, width_y = u_ref.shape
    cells, features = st_ref.shape
    levels = features // 2
    width_x = levels_x // levels
    chunk = 128

    def clear(k, carry):
        at = pl.ds(pl.multiple_of(k * chunk, chunk), chunk)
        o_ref[at, :] = jnp.zeros((chunk, features), jnp.float32)
        return carry

    lax.fori_loop(0, o_ref.shape[0] // chunk, clear, 0)

    def transpose_tile(x, carry):
        a = u_ref[pl.ds(x, levels, stride=width_x), :]
        b = v_ref[pl.ds(x, levels, stride=width_x), :]
        tile = jnp.concatenate([a, b], axis=0)
        st_ref[pl.ds(pl.multiple_of(x * width_y, width_y), width_y), :] = tile.T
        return carry

    lax.fori_loop(0, width_x, transpose_tile, 0)

    def place(r, carry):
        o_ref[pl.ds(slot_ref[r], 1), :] = st_ref[pl.ds(act_ref[r], 1), :]
        return carry

    lax.fori_loop(0, act_ref.shape[0], place, 0, unroll=8)


def diffuse_kernel(st_ref, xb_ref, xa_ref, yh_ref, c_ref, f_ref, e_ref, a_ref):
    width_x, width_y, _ = st_ref.shape
    depth = xb_ref.shape[0]
    rows_ext, ylen, _ = c_ref.shape
    e_ref[0:depth, 0:width_y, :] = xb_ref[...]
    e_ref[depth + width_x :, 0:width_y, :] = xa_ref[...]

    def fill(x, carry):
        e_ref[x + depth, 0:width_y, :] = st_ref[x]
        return carry

    lax.fori_loop(0, width_x, fill, 0)
    e_ref[:, width_y:, :] = yh_ref[...]

    def sweep(src, dst, p, last):
        def one(x, carry):
            q = src[x]
            n = src[x + 1] + src[x - 1]
            n = n + pltpu.roll(q, ylen - 1, 0) + pltpu.roll(q, 1, 0)
            new = q + c_ref[x] * (n - 4.0 * q)
            if last:
                f_ref[x - depth] = new[:width_y]
            else:
                dst[x] = new
            return carry

        lax.fori_loop(p + 1, rows_ext - 1 - p, one, 0)

    for p in range(PASSES):
        src, dst = (e_ref, a_ref) if p % 2 == 0 else (a_ref, e_ref)
        sweep(src, dst, p, p == PASSES - 1)


def finish_kernel(slot_ref, act_ref, r_ref, f_ref, uo_ref, vo_ref, d_ref):
    levels_x, width_y = uo_ref.shape
    cells, features = f_ref.shape
    levels = features // 2
    width_x = levels_x // levels

    def copy_tile(x, carry):
        at = pl.ds(pl.multiple_of(x * width_y, width_y), width_y)
        d_ref[at, :] = f_ref[at, :]
        return carry

    lax.fori_loop(0, width_x, copy_tile, 0)

    def place(r, carry):
        at = pl.ds(act_ref[r], 1)
        d_ref[at, :] = d_ref[at, :] + r_ref[pl.ds(slot_ref[r], 1), :]
        return carry

    lax.fori_loop(0, act_ref.shape[0], place, 0, unroll=8)

    def transpose_tile(x, carry):
        tile = d_ref[pl.ds(pl.multiple_of(x * width_y, width_y), width_y), :].T
        uo_ref[pl.ds(x, levels, stride=width_x), :] = tile[:levels]
        vo_ref[pl.ds(x, levels, stride=width_x), :] = tile[levels:]
        return carry

    lax.fori_loop(0, width_x, transpose_tile, 0)


def body(
    u_field,
    v_field,
    diffusivity,
    active_columns,
    regimes,
    first_layer,
    second_layer,
    third_layer,
    last_layer,
):
    levels, width_x, width_y = u_field.shape
    features = 2 * levels
    cells = width_x * width_y
    active_count = active_columns.shape[0]
    devices_all = lax.axis_size(("tile", "inf"))
    capacity = 2 * active_count // devices_all
    slot_total = devices_all * capacity
    block_rows = min(512, active_count)
    block_count = active_count // block_rows
    target = regimes[:, 0]
    labels = jnp.arange(devices_all, dtype=jnp.int32)
    one_hot = (
        (target[:, None] == labels[None, :])
        .astype(jnp.bfloat16)
        .reshape(block_count, block_rows, devices_all)
    )
    row_ids = jnp.arange(block_rows, dtype=jnp.int32)
    lower = (row_ids[:, None] > row_ids[None, :]).astype(jnp.bfloat16)

    def rank_step(counts, piece):
        earlier = jnp.dot(lower, piece, preferred_element_type=jnp.float32) + counts[None, :]
        wide_piece = piece.astype(jnp.float32)
        rank = jnp.sum(earlier * wide_piece, axis=1)
        return (counts + jnp.sum(wide_piece, axis=0), rank)

    _, ranks = lax.scan(rank_step, jnp.zeros((devices_all,), jnp.float32), one_hot)
    tile_count, inf_count = lax.axis_size("tile"), lax.axis_size("inf")
    half_tiles = tile_count // 2
    my_half = lax.axis_index("tile") // half_tiles
    target_tile = target // inf_count
    place = (target_tile % half_tiles) * inf_count + target % inf_count
    kind = (target_tile // half_tiles != my_half).astype(jnp.int32)
    pair_slots = 2 * capacity
    slot_index = place * pair_slots + kind * capacity + ranks.reshape(-1).astype(jnp.int32)
    groups = [
        [t * inf_count + i for t in range(h * half_tiles, (h + 1) * half_tiles) for i in range(inf_count)]
        for h in range(2)
    ]
    group_size = half_tiles * inf_count
    swap = [(t, (t + half_tiles) % tile_count) for t in range(tile_count)]
    mirrored = [
        lax.ppermute(w[0], "tile", swap) for w in (first_layer, second_layer, third_layer, last_layer)
    ]
    vmem = pl.BlockSpec(memory_space=pltpu.VMEM)
    smem = pl.BlockSpec(memory_space=pltpu.SMEM)
    x_from_before, x_from_after = stencil_start(u_field, v_field, diffusivity, PASSES)
    u_rows = u_field.reshape(levels * width_x, width_y)
    v_rows = v_field.reshape(levels * width_x, width_y)
    state_t, outgoing = pl.pallas_call(
        gather_kernel,
        out_shape=(
            jax.ShapeDtypeStruct((cells, features), jnp.float32),
            jax.ShapeDtypeStruct((slot_total, features), jnp.float32),
        ),
        in_specs=[smem, smem, vmem, vmem],
        out_specs=(vmem, vmem),
    )(slot_index, active_columns, u_rows, v_rows)
    state_t = state_t.reshape(width_x, width_y, features)
    outgoing, x_from_before, x_from_after = lax.optimization_barrier(
        (outgoing, x_from_before, x_from_after)
    )
    block = lax.all_to_all(
        outgoing.reshape(group_size, pair_slots, features),
        ("tile", "inf"),
        split_axis=0,
        concat_axis=0,
        tiled=True,
        axis_index_groups=groups,
    )
    block_shape = block.shape
    x_before, x_after, y_halo, coeff = stencil_finish(
        state_t, diffusivity, x_from_before, x_from_after, PASSES
    )
    block, mirrored, x_before, x_after, y_halo, coeff = lax.optimization_barrier(
        (block, mirrored, x_before, x_after, y_halo, coeff)
    )
    own_rows = standardize(block[:, :capacity].reshape(-1, features))
    own = network_rows(own_rows, first_layer[0], second_layer[0], third_layer[0], last_layer[0])
    other_rows = standardize(block[:, capacity:].reshape(-1, features))
    other = network_rows(other_rows, *mirrored)
    answered = jnp.concatenate(
        [own.reshape(group_size, capacity, features), other.reshape(group_size, capacity, features)],
        axis=1,
    )
    returned = lax.all_to_all(
        answered,
        ("tile", "inf"),
        split_axis=0,
        concat_axis=0,
        tiled=True,
        axis_index_groups=groups,
    )
    returned_rows = returned.reshape(slot_total, features)

    rows_ext, ylen = coeff.shape[:2]
    diffused = pl.pallas_call(
        diffuse_kernel,
        out_shape=jax.ShapeDtypeStruct((width_x, width_y, features), jnp.float32),
        in_specs=[vmem] * 5,
        out_specs=vmem,
        scratch_shapes=[
            pltpu.VMEM((rows_ext, ylen, features), jnp.float32),
            pltpu.VMEM((rows_ext, ylen, features), jnp.float32),
        ],
        compiler_params=pltpu.CompilerParams(vmem_limit_bytes=100 * 1024 * 1024),
    )(state_t, x_before, x_after, y_halo, coeff)
    u_next, v_next = pl.pallas_call(
        finish_kernel,
        out_shape=(
            jax.ShapeDtypeStruct((levels * width_x, width_y), jnp.float32),
            jax.ShapeDtypeStruct((levels * width_x, width_y), jnp.float32),
        ),
        in_specs=[smem, smem, vmem, vmem],
        out_specs=(vmem, vmem),
        scratch_shapes=[pltpu.VMEM((cells, features), jnp.float32)],
    )(slot_index, active_columns, returned_rows, diffused.reshape(cells, features))
    return (u_next.reshape(u_field.shape), v_next.reshape(v_field.shape))


def solution(mesh):
    in_specs = (
        P(None, "tile", "inf"),
        P(None, "tile", "inf"),
        P("tile", "inf"),
        P(("tile", "inf")),
        P(("tile", "inf"), None),
        P(("tile", "inf"), None, None),
        P(("tile", "inf"), None, None),
        P(("tile", "inf"), None, None),
        P(("tile", "inf"), None, None),
    )
    out_specs = (P(None, "tile", "inf"), P(None, "tile", "inf"))
    return jax.shard_map(body, mesh=mesh, in_specs=in_specs, out_specs=out_specs, check_vma=False)
```

```python
import jax
import jax.numpy as jnp
from jax import lax
from jax.experimental import pallas as pl
from jax.experimental.pallas import tpu as pltpu
from jax.sharding import PartitionSpec as P


PASSES = 4


def stencil_start(u_field, v_field, diffusivity, depth):
    width_x = u_field.shape[1]

    def x_piece(start):
        rows = lambda a: lax.slice_in_dim(a, start, start + depth, axis=a.ndim - 2)
        return jnp.concatenate([rows(u_field), rows(v_field), rows(diffusivity)[None]], axis=0)

    tile_count = lax.axis_size("tile")
    up = [(i, i + 1) for i in range(tile_count - 1)]
    down = [(j, i) for i, j in up]
    before = lax.ppermute(x_piece(width_x - depth), "tile", up)
    after = lax.ppermute(x_piece(0), "tile", down)
    return before, after


def stencil_finish(state_t, diffusivity, before, after, depth):
    _, width_y, features = state_t.shape
    x_before = before[:features].transpose(1, 2, 0)
    x_after = after[:features].transpose(1, 2, 0)
    c_rows = jnp.concatenate([before[features], diffusivity, after[features]], axis=0)
    extended = jnp.concatenate([x_before, state_t, x_after], axis=0)

    def y_piece(start):
        rows = lax.slice_in_dim(extended, start, start + depth, axis=1)
        cols = lax.slice_in_dim(c_rows, start, start + depth, axis=1).T
        cols = jnp.pad(cols, ((0, 0), (0, features - cols.shape[1])))
        return jnp.concatenate([rows, cols[None]], axis=0)

    inf_count = lax.axis_size("inf")
    up = [(i, i + 1) for i in range(inf_count - 1)]
    down = [(j, i) for i, j in up]
    before = lax.ppermute(y_piece(width_y - depth), "inf", up)
    after = lax.ppermute(y_piece(0), "inf", down)
    rows_ext = extended.shape[0]
    y_halo = jnp.concatenate([after[:rows_ext], before[:rows_ext]], axis=1)
    c_ext = jnp.concatenate(
        [c_rows, after[rows_ext, :, :rows_ext].T, before[rows_ext, :, :rows_ext].T], axis=1
    )
    ylen = c_ext.shape[1]
    coeff = jnp.broadcast_to(c_ext[:, :, None], (rows_ext, ylen, features))
    return x_before, x_after, y_halo, coeff


def standardize(rows):
    center = jnp.mean(rows, axis=-1, keepdims=True)
    spread = jnp.mean(jnp.square(rows - center), axis=-1, keepdims=True)
    return (rows - center) * lax.rsqrt(spread + 1e-05)


def network_rows(rows, first_layer, second_layer, third_layer, last_layer):
    highest = lax.Precision.HIGH
    hidden = jax.nn.silu(jnp.dot(rows, first_layer, precision=highest))
    hidden = jax.nn.silu(jnp.dot(hidden, second_layer, precision=highest))
    hidden = jax.nn.silu(jnp.dot(hidden, third_layer, precision=highest))
    return jnp.dot(hidden, last_layer, precision=highest)


def gather_kernel(slot_ref, act_ref, u_ref, v_ref, st_ref, o_ref):
    levels_x, width_y = u_ref.shape
    _, features = st_ref.shape
    levels = features // 2
    width_x = levels_x // levels
    chunk = 128

    def clear(k, carry):
        at = pl.ds(pl.multiple_of(k * chunk, chunk), chunk)
        o_ref[at, :] = jnp.zeros((chunk, features), jnp.float32)
        return carry

    lax.fori_loop(0, o_ref.shape[0] // chunk, clear, 0)

    def transpose_tile(x, carry):
        a = u_ref[pl.ds(x, levels, stride=width_x), :]
        b = v_ref[pl.ds(x, levels, stride=width_x), :]
        tile = jnp.concatenate([a, b], axis=0)
        st_ref[pl.ds(pl.multiple_of(x * width_y, width_y), width_y), :] = tile.T
        return carry

    lax.fori_loop(0, width_x, transpose_tile, 0)

    def place(r, carry):
        o_ref[pl.ds(slot_ref[r], 1), :] = st_ref[pl.ds(act_ref[r], 1), :]
        return carry

    lax.fori_loop(0, act_ref.shape[0], place, 0, unroll=8)


def diffuse_kernel(st_ref, xb_ref, xa_ref, yh_ref, c_ref, f_ref, e_ref, a_ref):
    width_x, width_y, _ = st_ref.shape
    depth = xb_ref.shape[0]
    rows_ext, ylen, _ = c_ref.shape
    e_ref[0:depth, 0:width_y, :] = xb_ref[...]
    e_ref[depth + width_x :, 0:width_y, :] = xa_ref[...]

    def fill(x, carry):
        e_ref[x + depth, 0:width_y, :] = st_ref[x]
        return carry

    lax.fori_loop(0, width_x, fill, 0)
    e_ref[:, width_y:, :] = yh_ref[...]

    def sweep(src, dst, p, last):
        def one(x, carry):
            q = src[x]
            n = src[x + 1] + src[x - 1]
            n = n + pltpu.roll(q, ylen - 1, 0) + pltpu.roll(q, 1, 0)
            new = q + c_ref[x] * (n - 4.0 * q)
            if last:
                f_ref[x - depth] = new[:width_y]
            else:
                dst[x] = new
            return carry

        lax.fori_loop(p + 1, rows_ext - 1 - p, one, 0)

    for p in range(PASSES):
        src, dst = (e_ref, a_ref) if p % 2 == 0 else (a_ref, e_ref)
        sweep(src, dst, p, p == PASSES - 1)


def finish_kernel(slot_ref, act_ref, r_ref, f_ref, uo_ref, vo_ref, d_ref):
    levels_x, width_y = uo_ref.shape
    _, features = f_ref.shape
    levels = features // 2
    width_x = levels_x // levels

    def copy_tile(x, carry):
        at = pl.ds(pl.multiple_of(x * width_y, width_y), width_y)
        d_ref[at, :] = f_ref[at, :]
        return carry

    lax.fori_loop(0, width_x, copy_tile, 0)

    def place(r, carry):
        at = pl.ds(act_ref[r], 1)
        d_ref[at, :] = d_ref[at, :] + r_ref[pl.ds(slot_ref[r], 1), :]
        return carry

    lax.fori_loop(0, act_ref.shape[0], place, 0, unroll=8)

    def transpose_tile(x, carry):
        tile = d_ref[pl.ds(pl.multiple_of(x * width_y, width_y), width_y), :].T
        uo_ref[pl.ds(x, levels, stride=width_x), :] = tile[:levels]
        vo_ref[pl.ds(x, levels, stride=width_x), :] = tile[levels:]
        return carry

    lax.fori_loop(0, width_x, transpose_tile, 0)


def step(
    u_field,
    v_field,
    diffusivity,
    active_columns,
    regimes,
    first_layer,
    second_layer,
    third_layer,
    last_layer,
):
    levels, width_x, width_y = u_field.shape
    features = 2 * levels
    cells = width_x * width_y
    active_count = active_columns.shape[0]
    devices_all = lax.axis_size(("tile", "inf"))
    capacity = 2 * active_count // devices_all
    slot_total = devices_all * capacity
    block_rows = min(512, active_count)
    block_count = active_count // block_rows
    target = regimes[:, 0]
    labels = jnp.arange(devices_all, dtype=jnp.int32)
    one_hot = (
        (target[:, None] == labels[None, :])
        .astype(jnp.bfloat16)
        .reshape(block_count, block_rows, devices_all)
    )
    row_ids = jnp.arange(block_rows, dtype=jnp.int32)
    lower = (row_ids[:, None] > row_ids[None, :]).astype(jnp.bfloat16)

    def rank_step(counts, piece):
        earlier = jnp.dot(lower, piece, preferred_element_type=jnp.float32) + counts[None, :]
        wide_piece = piece.astype(jnp.float32)
        rank = jnp.sum(earlier * wide_piece, axis=1)
        return (counts + jnp.sum(wide_piece, axis=0), rank)

    _, ranks = lax.scan(rank_step, jnp.zeros((devices_all,), jnp.float32), one_hot)
    tile_count, inf_count = lax.axis_size("tile"), lax.axis_size("inf")
    half_tiles = tile_count // 2
    my_half = lax.axis_index("tile") // half_tiles
    target_tile = target // inf_count
    place = (target_tile % half_tiles) * inf_count + target % inf_count
    kind = (target_tile // half_tiles != my_half).astype(jnp.int32)
    pair_slots = 2 * capacity
    slot_index = place * pair_slots + kind * capacity + ranks.reshape(-1).astype(jnp.int32)
    groups = [
        [t * inf_count + i for t in range(h * half_tiles, (h + 1) * half_tiles) for i in range(inf_count)]
        for h in range(2)
    ]
    group_size = half_tiles * inf_count
    swap = [(t, (t + half_tiles) % tile_count) for t in range(tile_count)]
    mirrored = [
        lax.ppermute(w[0], "tile", swap)
        for w in (first_layer, second_layer, third_layer, last_layer)
    ]
    vmem = pl.BlockSpec(memory_space=pltpu.VMEM)
    smem = pl.BlockSpec(memory_space=pltpu.SMEM)
    x_from_before, x_from_after = stencil_start(u_field, v_field, diffusivity, PASSES)
    u_rows = u_field.reshape(levels * width_x, width_y)
    v_rows = v_field.reshape(levels * width_x, width_y)
    state_t, outgoing = pl.pallas_call(
        gather_kernel,
        out_shape=(
            jax.ShapeDtypeStruct((cells, features), jnp.float32),
            jax.ShapeDtypeStruct((slot_total, features), jnp.float32),
        ),
        in_specs=[smem, smem, vmem, vmem],
        out_specs=(vmem, vmem),
    )(slot_index, active_columns, u_rows, v_rows)
    state_t = state_t.reshape(width_x, width_y, features)
    outgoing, x_from_before, x_from_after = lax.optimization_barrier(
        (outgoing, x_from_before, x_from_after)
    )
    block = lax.all_to_all(
        outgoing.reshape(group_size, pair_slots, features),
        ("tile", "inf"),
        split_axis=0,
        concat_axis=0,
        tiled=True,
        axis_index_groups=groups,
    )
    x_before, x_after, y_halo, coeff = stencil_finish(
        state_t, diffusivity, x_from_before, x_from_after, PASSES
    )
    block, mirrored, x_before, x_after, y_halo, coeff = lax.optimization_barrier(
        (block, mirrored, x_before, x_after, y_halo, coeff)
    )
    own_rows = standardize(block[:, :capacity].reshape(-1, features))
    own = network_rows(own_rows, first_layer[0], second_layer[0], third_layer[0], last_layer[0])
    other_rows = standardize(block[:, capacity:].reshape(-1, features))
    other = network_rows(other_rows, *mirrored)
    answered = jnp.concatenate(
        [own.reshape(group_size, capacity, features), other.reshape(group_size, capacity, features)],
        axis=1,
    )
    returned = lax.all_to_all(
        answered,
        ("tile", "inf"),
        split_axis=0,
        concat_axis=0,
        tiled=True,
        axis_index_groups=groups,
    )
    returned_rows = returned.reshape(slot_total, features)

    rows_ext, ylen = coeff.shape[:2]
    diffused = pl.pallas_call(
        diffuse_kernel,
        out_shape=jax.ShapeDtypeStruct((width_x, width_y, features), jnp.float32),
        in_specs=[vmem] * 5,
        out_specs=vmem,
        scratch_shapes=[
            pltpu.VMEM((rows_ext, ylen, features), jnp.float32),
            pltpu.VMEM((rows_ext, ylen, features), jnp.float32),
        ],
        compiler_params=pltpu.CompilerParams(vmem_limit_bytes=100 * 1024 * 1024),
    )(state_t, x_before, x_after, y_halo, coeff)
    u_next, v_next = pl.pallas_call(
        finish_kernel,
        out_shape=(
            jax.ShapeDtypeStruct((levels * width_x, width_y), jnp.float32),
            jax.ShapeDtypeStruct((levels * width_x, width_y), jnp.float32),
        ),
        in_specs=[smem, smem, vmem, vmem],
        out_specs=(vmem, vmem),
        scratch_shapes=[pltpu.VMEM((cells, features), jnp.float32)],
    )(slot_index, active_columns, returned_rows, diffused.reshape(cells, features))
    return (u_next.reshape(u_field.shape), v_next.reshape(v_field.shape))


def solution(mesh):
    in_specs = (
        P(None, "tile", "inf"),
        P(None, "tile", "inf"),
        P("tile", "inf"),
        P(("tile", "inf")),
        P(("tile", "inf"), None),
        P(("tile", "inf"), None, None),
        P(("tile", "inf"), None, None),
        P(("tile", "inf"), None, None),
        P(("tile", "inf"), None, None),
    )
    out_specs = (P(None, "tile", "inf"), P(None, "tile", "inf"))
    return jax.shard_map(step, mesh=mesh, in_specs=in_specs, out_specs=out_specs, check_vma=False)
```

```python
import jax
import jax.numpy as jnp
from jax import lax
from jax.experimental import pallas as pl
from jax.experimental.pallas import tpu as pltpu
from jax.sharding import PartitionSpec as P

PASSES = 4


def halos(x, axis, dim, width):
    count, length = (lax.axis_size(axis), x.shape[dim])
    up = [(i, i + 1) for i in range(count - 1)]
    down = [(j, i) for i, j in up]
    last = lax.slice_in_dim(x, length - width, length, axis=dim)
    first = lax.slice_in_dim(x, 0, width, axis=dim)
    before = lax.ppermute(last, axis, up)
    after = lax.ppermute(first, axis, down)
    return before, after


def stencil_start(u_field, v_field, diffusivity, depth):
    width_x = u_field.shape[1]

    def x_piece(start):
        rows = lambda a: lax.slice_in_dim(a, start, start + depth, axis=a.ndim - 2)
        return jnp.concatenate([rows(u_field), rows(v_field), rows(diffusivity)[None]], axis=0)

    tile_count = lax.axis_size("tile")
    up = [(i, i + 1) for i in range(tile_count - 1)]
    down = [(j, i) for i, j in up]
    before = lax.ppermute(x_piece(width_x - depth), "tile", up)
    after = lax.ppermute(x_piece(0), "tile", down)
    return before, after


def stencil_finish(state_t, diffusivity, before, after, depth):
    width_x, width_y, features = state_t.shape
    x_before = before[:features].transpose(1, 2, 0)
    x_after = after[:features].transpose(1, 2, 0)
    c_rows = jnp.concatenate([before[features], diffusivity, after[features]], axis=0)
    extended = jnp.concatenate([x_before, state_t, x_after], axis=0)

    def y_piece(start):
        rows = lax.slice_in_dim(extended, start, start + depth, axis=1)
        cols = lax.slice_in_dim(c_rows, start, start + depth, axis=1).T
        cols = jnp.pad(cols, ((0, 0), (0, features - cols.shape[1])))
        return jnp.concatenate([rows, cols[None]], axis=0)

    inf_count = lax.axis_size("inf")
    up = [(i, i + 1) for i in range(inf_count - 1)]
    down = [(j, i) for i, j in up]
    before = lax.ppermute(y_piece(width_y - depth), "inf", up)
    after = lax.ppermute(y_piece(0), "inf", down)
    rows_ext = extended.shape[0]
    y_halo = jnp.concatenate([after[:rows_ext], before[:rows_ext]], axis=1)
    c_ext = jnp.concatenate(
        [c_rows, after[rows_ext, :, :rows_ext].T, before[rows_ext, :, :rows_ext].T], axis=1
    )
    ylen = c_ext.shape[1]
    coeff = jnp.broadcast_to(c_ext[:, :, None], (rows_ext, ylen, features))
    return x_before, x_after, y_halo, coeff


def standardize(rows):
    center = jnp.mean(rows, axis=-1, keepdims=True)
    spread = jnp.mean(jnp.square(rows - center), axis=-1, keepdims=True)
    return (rows - center) * lax.rsqrt(spread + 1e-05)


def network_rows(rows, first_layer, second_layer, third_layer, last_layer):
    highest = lax.Precision.HIGH
    hidden = jax.nn.silu(jnp.dot(rows, first_layer, precision=highest))
    hidden = jax.nn.silu(jnp.dot(hidden, second_layer, precision=highest))
    hidden = jax.nn.silu(jnp.dot(hidden, third_layer, precision=highest))
    return jnp.dot(hidden, last_layer, precision=highest)


def gather_kernel(slot_ref, act_ref, u_ref, v_ref, st_ref, o_ref):
    levels_x, width_y = u_ref.shape
    cells, features = st_ref.shape
    levels = features // 2
    width_x = levels_x // levels
    chunk = 128

    def clear(k, carry):
        at = pl.ds(pl.multiple_of(k * chunk, chunk), chunk)
        o_ref[at, :] = jnp.zeros((chunk, features), jnp.float32)
        return carry

    lax.fori_loop(0, o_ref.shape[0] // chunk, clear, 0)

    def transpose_tile(x, carry):
        a = u_ref[pl.ds(x, levels, stride=width_x), :]
        b = v_ref[pl.ds(x, levels, stride=width_x), :]
        tile = jnp.concatenate([a, b], axis=0)
        st_ref[pl.ds(pl.multiple_of(x * width_y, width_y), width_y), :] = tile.T
        return carry

    lax.fori_loop(0, width_x, transpose_tile, 0)

    def place(r, carry):
        o_ref[pl.ds(slot_ref[r], 1), :] = st_ref[pl.ds(act_ref[r], 1), :]
        return carry

    lax.fori_loop(0, act_ref.shape[0], place, 0, unroll=8)


def diffuse_kernel(st_ref, xb_ref, xa_ref, yh_ref, c_ref, f_ref, e_ref, a_ref):
    width_x, width_y, _ = st_ref.shape
    depth = xb_ref.shape[0]
    rows_ext, ylen, _ = c_ref.shape
    e_ref[0:depth, 0:width_y, :] = xb_ref[...]
    e_ref[depth + width_x :, 0:width_y, :] = xa_ref[...]

    def fill(x, carry):
        e_ref[x + depth, 0:width_y, :] = st_ref[x]
        return carry

    lax.fori_loop(0, width_x, fill, 0)
    e_ref[:, width_y:, :] = yh_ref[...]

    def sweep(src, dst, p, last):
        def one(x, carry):
            q = src[x]
            n = src[x + 1] + src[x - 1]
            n = n + pltpu.roll(q, ylen - 1, 0) + pltpu.roll(q, 1, 0)
            new = q + c_ref[x] * (n - 4.0 * q)
            if last:
                f_ref[x - depth] = new[:width_y]
            else:
                dst[x] = new
            return carry

        lax.fori_loop(p + 1, rows_ext - 1 - p, one, 0)

    for p in range(PASSES):
        src, dst = (e_ref, a_ref) if p % 2 == 0 else (a_ref, e_ref)
        sweep(src, dst, p, p == PASSES - 1)


def finish_kernel(slot_ref, act_ref, r_ref, f_ref, uo_ref, vo_ref, d_ref):
    levels_x, width_y = uo_ref.shape
    cells, features = f_ref.shape
    levels = features // 2
    width_x = levels_x // levels

    def copy_tile(x, carry):
        at = pl.ds(pl.multiple_of(x * width_y, width_y), width_y)
        d_ref[at, :] = f_ref[at, :]
        return carry

    lax.fori_loop(0, width_x, copy_tile, 0)

    def place(r, carry):
        at = pl.ds(act_ref[r], 1)
        d_ref[at, :] = d_ref[at, :] + r_ref[pl.ds(slot_ref[r], 1), :]
        return carry

    lax.fori_loop(0, act_ref.shape[0], place, 0, unroll=8)

    def transpose_tile(x, carry):
        tile = d_ref[pl.ds(pl.multiple_of(x * width_y, width_y), width_y), :].T
        uo_ref[pl.ds(x, levels, stride=width_x), :] = tile[:levels]
        vo_ref[pl.ds(x, levels, stride=width_x), :] = tile[levels:]
        return carry

    lax.fori_loop(0, width_x, transpose_tile, 0)


def body(
    u_field,
    v_field,
    diffusivity,
    active_columns,
    regimes,
    first_layer,
    second_layer,
    third_layer,
    last_layer,
):
    levels, width_x, width_y = u_field.shape
    features = 2 * levels
    cells = width_x * width_y
    active_count = active_columns.shape[0]
    devices_all = lax.axis_size(("tile", "inf"))
    capacity = 2 * active_count // devices_all
    slot_total = devices_all * capacity
    block_rows = min(512, active_count)
    block_count = active_count // block_rows
    target = regimes[:, 0]
    labels = jnp.arange(devices_all, dtype=jnp.int32)
    one_hot = (
        (target[:, None] == labels[None, :])
        .astype(jnp.bfloat16)
        .reshape(block_count, block_rows, devices_all)
    )
    row_ids = jnp.arange(block_rows, dtype=jnp.int32)
    lower = (row_ids[:, None] > row_ids[None, :]).astype(jnp.bfloat16)

    def rank_step(counts, piece):
        earlier = jnp.dot(lower, piece, preferred_element_type=jnp.float32) + counts[None, :]
        wide_piece = piece.astype(jnp.float32)
        rank = jnp.sum(earlier * wide_piece, axis=1)
        return (counts + jnp.sum(wide_piece, axis=0), rank)

    _, ranks = lax.scan(rank_step, jnp.zeros((devices_all,), jnp.float32), one_hot)
    tile_count, inf_count = lax.axis_size("tile"), lax.axis_size("inf")
    half_tiles = tile_count // 2
    my_half = lax.axis_index("tile") // half_tiles
    target_tile = target // inf_count
    place = (target_tile % half_tiles) * inf_count + target % inf_count
    kind = (target_tile // half_tiles != my_half).astype(jnp.int32)
    pair_slots = 2 * capacity
    slot_index = place * pair_slots + kind * capacity + ranks.reshape(-1).astype(jnp.int32)
    groups = [
        [t * inf_count + i for t in range(h * half_tiles, (h + 1) * half_tiles) for i in range(inf_count)]
        for h in range(2)
    ]
    group_size = half_tiles * inf_count
    swap = [(t, (t + half_tiles) % tile_count) for t in range(tile_count)]
    mirrored = [
        lax.ppermute(w[0], "tile", swap) for w in (first_layer, second_layer, third_layer, last_layer)
    ]
    vmem = pl.BlockSpec(memory_space=pltpu.VMEM)
    smem = pl.BlockSpec(memory_space=pltpu.SMEM)
    x_from_before, x_from_after = stencil_start(u_field, v_field, diffusivity, PASSES)
    u_rows = u_field.reshape(levels * width_x, width_y)
    v_rows = v_field.reshape(levels * width_x, width_y)
    state_t, outgoing = pl.pallas_call(
        gather_kernel,
        out_shape=(
            jax.ShapeDtypeStruct((cells, features), jnp.float32),
            jax.ShapeDtypeStruct((slot_total, features), jnp.float32),
        ),
        in_specs=[smem, smem, vmem, vmem],
        out_specs=(vmem, vmem),
    )(slot_index, active_columns, u_rows, v_rows)
    state_t = state_t.reshape(width_x, width_y, features)
    outgoing, x_from_before, x_from_after = lax.optimization_barrier(
        (outgoing, x_from_before, x_from_after)
    )
    block = lax.all_to_all(
        outgoing.reshape(group_size, pair_slots, features),
        ("tile", "inf"),
        split_axis=0,
        concat_axis=0,
        tiled=True,
        axis_index_groups=groups,
    )
    block_shape = block.shape
    x_before, x_after, y_halo, coeff = stencil_finish(
        state_t, diffusivity, x_from_before, x_from_after, PASSES
    )
    block, x_before, x_after, y_halo = lax.optimization_barrier(
        (block, x_before, x_after, y_halo)
    )
    own_rows = standardize(block[:, :capacity].reshape(-1, features))
    own = network_rows(own_rows, first_layer[0], second_layer[0], third_layer[0], last_layer[0])
    other_rows = standardize(block[:, capacity:].reshape(-1, features))
    other = network_rows(other_rows, *mirrored)
    answered = jnp.concatenate(
        [own.reshape(group_size, capacity, features), other.reshape(group_size, capacity, features)],
        axis=1,
    )
    returned = lax.all_to_all(
        answered,
        ("tile", "inf"),
        split_axis=0,
        concat_axis=0,
        tiled=True,
        axis_index_groups=groups,
    )
    returned_rows = returned.reshape(slot_total, features)

    rows_ext, ylen = coeff.shape[:2]
    diffused = pl.pallas_call(
        diffuse_kernel,
        out_shape=jax.ShapeDtypeStruct((width_x, width_y, features), jnp.float32),
        in_specs=[vmem] * 5,
        out_specs=vmem,
        scratch_shapes=[
            pltpu.VMEM((rows_ext, ylen, features), jnp.float32),
            pltpu.VMEM((rows_ext, ylen, features), jnp.float32),
        ],
        compiler_params=pltpu.CompilerParams(vmem_limit_bytes=100 * 1024 * 1024),
    )(state_t, x_before, x_after, y_halo, coeff)
    u_next, v_next = pl.pallas_call(
        finish_kernel,
        out_shape=(
            jax.ShapeDtypeStruct((levels * width_x, width_y), jnp.float32),
            jax.ShapeDtypeStruct((levels * width_x, width_y), jnp.float32),
        ),
        in_specs=[smem, smem, vmem, vmem],
        out_specs=(vmem, vmem),
        scratch_shapes=[pltpu.VMEM((cells, features), jnp.float32)],
    )(slot_index, active_columns, returned_rows, diffused.reshape(cells, features))
    return (u_next.reshape(u_field.shape), v_next.reshape(v_field.shape))


def solution(mesh):
    in_specs = (
        P(None, "tile", "inf"),
        P(None, "tile", "inf"),
        P("tile", "inf"),
        P(("tile", "inf")),
        P(("tile", "inf"), None),
        P(("tile", "inf"), None, None),
        P(("tile", "inf"), None, None),
        P(("tile", "inf"), None, None),
        P(("tile", "inf"), None, None),
    )
    out_specs = (P(None, "tile", "inf"), P(None, "tile", "inf"))
    return jax.shard_map(body, mesh=mesh, in_specs=in_specs, out_specs=out_specs, check_vma=False)
```

```python
import jax
import jax.numpy as jnp
from jax import lax
from jax.experimental import pallas as pl
from jax.experimental.pallas import tpu as pltpu
from jax.sharding import PartitionSpec as P

PASSES = 4


def halos(x, axis, dim, width):
    count, length = (lax.axis_size(axis), x.shape[dim])
    up = [(i, i + 1) for i in range(count - 1)]
    down = [(j, i) for i, j in up]
    last = lax.slice_in_dim(x, length - width, length, axis=dim)
    first = lax.slice_in_dim(x, 0, width, axis=dim)
    before = lax.ppermute(last, axis, up)
    after = lax.ppermute(first, axis, down)
    return before, after


def stencil_start(u_field, v_field, diffusivity, depth):
    width_x = u_field.shape[1]

    def x_piece(start):
        rows = lambda a: lax.slice_in_dim(a, start, start + depth, axis=a.ndim - 2)
        return jnp.concatenate([rows(u_field), rows(v_field), rows(diffusivity)[None]], axis=0)

    tile_count = lax.axis_size("tile")
    up = [(i, i + 1) for i in range(tile_count - 1)]
    down = [(j, i) for i, j in up]
    before = lax.ppermute(x_piece(width_x - depth), "tile", up)
    after = lax.ppermute(x_piece(0), "tile", down)
    return before, after


def stencil_finish(state_t, diffusivity, before, after, depth):
    width_x, width_y, features = state_t.shape
    x_before = before[:features].transpose(1, 2, 0)
    x_after = after[:features].transpose(1, 2, 0)
    c_rows = jnp.concatenate([before[features], diffusivity, after[features]], axis=0)
    extended = jnp.concatenate([x_before, state_t, x_after], axis=0)

    def y_piece(start):
        rows = lax.slice_in_dim(extended, start, start + depth, axis=1)
        cols = lax.slice_in_dim(c_rows, start, start + depth, axis=1).T
        cols = jnp.pad(cols, ((0, 0), (0, features - cols.shape[1])))
        return jnp.concatenate([rows, cols[None]], axis=0)

    inf_count = lax.axis_size("inf")
    up = [(i, i + 1) for i in range(inf_count - 1)]
    down = [(j, i) for i, j in up]
    before = lax.ppermute(y_piece(width_y - depth), "inf", up)
    after = lax.ppermute(y_piece(0), "inf", down)
    rows_ext = extended.shape[0]
    y_halo = jnp.concatenate([after[:rows_ext], before[:rows_ext]], axis=1)
    c_ext = jnp.concatenate(
        [c_rows, after[rows_ext, :, :rows_ext].T, before[rows_ext, :, :rows_ext].T], axis=1
    )
    ylen = c_ext.shape[1]
    coeff = jnp.broadcast_to(c_ext[:, :, None], (rows_ext, ylen, features))
    return x_before, x_after, y_halo, coeff


def standardize(rows):
    center = jnp.mean(rows, axis=-1, keepdims=True)
    spread = jnp.mean(jnp.square(rows - center), axis=-1, keepdims=True)
    return (rows - center) * lax.rsqrt(spread + 1e-05)


def network_rows(rows, first_layer, second_layer, third_layer, last_layer):
    highest = lax.Precision.HIGH
    hidden = jax.nn.silu(jnp.dot(rows, first_layer, precision=highest))
    hidden = jax.nn.silu(jnp.dot(hidden, second_layer, precision=highest))
    hidden = jax.nn.silu(jnp.dot(hidden, third_layer, precision=highest))
    return jnp.dot(hidden, last_layer, precision=highest)


def gather_kernel(slot_ref, act_ref, u_hbm, v_hbm, st_ref, o_ref, buf, sems):
    levels = u_hbm.shape[0]
    width_x, features, width_y = buf.shape
    chunk = 128

    def copies(x):
        at = pl.ds(pl.multiple_of(x * width_y, width_y), width_y)
        return (
            pltpu.make_async_copy(u_hbm.at[:, at], buf.at[x, pl.ds(0, levels), :], sems.at[0, x]),
            pltpu.make_async_copy(v_hbm.at[:, at], buf.at[x, pl.ds(levels, levels), :], sems.at[1, x]),
        )

    def start(x, carry):
        for copy in copies(x):
            copy.start()
        return carry

    lax.fori_loop(0, width_x, start, 0)

    def clear(k, carry):
        at = pl.ds(pl.multiple_of(k * chunk, chunk), chunk)
        o_ref[at, :] = jnp.zeros((chunk, features), jnp.float32)
        return carry

    lax.fori_loop(0, o_ref.shape[0] // chunk, clear, 0)

    def transpose_tile(x, carry):
        for copy in copies(x):
            copy.wait()
        st_ref[pl.ds(pl.multiple_of(x * width_y, width_y), width_y), :] = buf[x].T
        return carry

    lax.fori_loop(0, width_x, transpose_tile, 0)

    def place(r, carry):
        o_ref[pl.ds(slot_ref[r], 1), :] = st_ref[pl.ds(act_ref[r], 1), :]
        return carry

    lax.fori_loop(0, act_ref.shape[0], place, 0, unroll=8)


def diffuse_kernel(st_ref, xb_ref, xa_ref, yh_ref, c_ref, f_ref, e_ref, a_ref):
    width_x, width_y, _ = st_ref.shape
    depth = xb_ref.shape[0]
    rows_ext, ylen, _ = c_ref.shape
    e_ref[0:depth, 0:width_y, :] = xb_ref[...]
    e_ref[depth + width_x :, 0:width_y, :] = xa_ref[...]

    def fill(x, carry):
        e_ref[x + depth, 0:width_y, :] = st_ref[x]
        return carry

    lax.fori_loop(0, width_x, fill, 0)
    e_ref[:, width_y:, :] = yh_ref[...]

    def sweep(src, dst, p, last):
        def one(x, carry):
            q = src[x]
            n = src[x + 1] + src[x - 1]
            n = n + pltpu.roll(q, ylen - 1, 0) + pltpu.roll(q, 1, 0)
            new = q + c_ref[x] * (n - 4.0 * q)
            if last:
                f_ref[x - depth] = new[:width_y]
            else:
                dst[x] = new
            return carry

        lax.fori_loop(p + 1, rows_ext - 1 - p, one, 0)

    for p in range(PASSES):
        src, dst = (e_ref, a_ref) if p % 2 == 0 else (a_ref, e_ref)
        sweep(src, dst, p, p == PASSES - 1)


def finish_kernel(slot_ref, act_ref, r_ref, f_ref, uo_hbm, vo_hbm, d_ref, obuf, sems):
    levels = uo_hbm.shape[0]
    width_x, features, width_y = obuf.shape

    def clear(x, carry):
        at = pl.ds(pl.multiple_of(x * width_y, width_y), width_y)
        d_ref[at, :] = jnp.zeros((width_y, features), jnp.float32)
        return carry

    lax.fori_loop(0, width_x, clear, 0)

    def place(r, carry):
        d_ref[pl.ds(act_ref[r], 1), :] = r_ref[pl.ds(slot_ref[r], 1), :]
        return carry

    lax.fori_loop(0, act_ref.shape[0], place, 0, unroll=8)

    def copies(x):
        at = pl.ds(pl.multiple_of(x * width_y, width_y), width_y)
        return (
            pltpu.make_async_copy(obuf.at[x, pl.ds(0, levels), :], uo_hbm.at[:, at], sems.at[0, x]),
            pltpu.make_async_copy(obuf.at[x, pl.ds(levels, levels), :], vo_hbm.at[:, at], sems.at[1, x]),
        )

    def transpose_tile(x, carry):
        at = pl.ds(pl.multiple_of(x * width_y, width_y), width_y)
        obuf[x] = (f_ref[at, :] + d_ref[at, :]).T
        for copy in copies(x):
            copy.start()
        return carry

    lax.fori_loop(0, width_x, transpose_tile, 0)

    def finish(x, carry):
        for copy in copies(x):
            copy.wait()
        return carry

    lax.fori_loop(0, width_x, finish, 0)


def body(
    u_field,
    v_field,
    diffusivity,
    active_columns,
    regimes,
    first_layer,
    second_layer,
    third_layer,
    last_layer,
):
    levels, width_x, width_y = u_field.shape
    features = 2 * levels
    cells = width_x * width_y
    active_count = active_columns.shape[0]
    devices_all = lax.axis_size(("tile", "inf"))
    capacity = 2 * active_count // devices_all
    slot_total = devices_all * capacity
    block_rows = min(512, active_count)
    block_count = active_count // block_rows
    target = regimes[:, 0]
    labels = jnp.arange(devices_all, dtype=jnp.int32)
    one_hot = (
        (target[:, None] == labels[None, :])
        .astype(jnp.bfloat16)
        .reshape(block_count, block_rows, devices_all)
    )
    row_ids = jnp.arange(block_rows, dtype=jnp.int32)
    lower = (row_ids[:, None] > row_ids[None, :]).astype(jnp.bfloat16)

    def rank_step(counts, piece):
        earlier = jnp.dot(lower, piece, preferred_element_type=jnp.float32) + counts[None, :]
        wide_piece = piece.astype(jnp.float32)
        rank = jnp.sum(earlier * wide_piece, axis=1)
        return (counts + jnp.sum(wide_piece, axis=0), rank)

    _, ranks = lax.scan(rank_step, jnp.zeros((devices_all,), jnp.float32), one_hot)
    tile_count, inf_count = lax.axis_size("tile"), lax.axis_size("inf")
    half_tiles = tile_count // 2
    my_half = lax.axis_index("tile") // half_tiles
    target_tile = target // inf_count
    place = (target_tile % half_tiles) * inf_count + target % inf_count
    kind = (target_tile // half_tiles != my_half).astype(jnp.int32)
    pair_slots = 2 * capacity
    slot_index = place * pair_slots + kind * capacity + ranks.reshape(-1).astype(jnp.int32)
    groups = [
        [t * inf_count + i for t in range(h * half_tiles, (h + 1) * half_tiles) for i in range(inf_count)]
        for h in range(2)
    ]
    group_size = half_tiles * inf_count
    swap = [(t, (t + half_tiles) % tile_count) for t in range(tile_count)]
    mirrored = [
        lax.ppermute(w[0], "tile", swap) for w in (first_layer, second_layer, third_layer, last_layer)
    ]
    vmem = pl.BlockSpec(memory_space=pltpu.VMEM)
    smem = pl.BlockSpec(memory_space=pltpu.SMEM)
    x_from_before, x_from_after = stencil_start(u_field, v_field, diffusivity, PASSES)
    u_rows = u_field.reshape(levels, cells)
    v_rows = v_field.reshape(levels, cells)
    hbm = pl.BlockSpec(memory_space=pl.ANY)
    state_t, outgoing = pl.pallas_call(
        gather_kernel,
        out_shape=(
            jax.ShapeDtypeStruct((cells, features), jnp.float32),
            jax.ShapeDtypeStruct((slot_total, features), jnp.float32),
        ),
        in_specs=[smem, smem, hbm, hbm],
        out_specs=(vmem, vmem),
        scratch_shapes=[
            pltpu.VMEM((width_x, features, width_y), jnp.float32),
            pltpu.SemaphoreType.DMA((2, width_x)),
        ],
    )(slot_index, active_columns, u_rows, v_rows)
    state_t = state_t.reshape(width_x, width_y, features)
    outgoing, x_from_before, x_from_after = lax.optimization_barrier(
        (outgoing, x_from_before, x_from_after)
    )
    block = lax.all_to_all(
        outgoing.reshape(group_size, pair_slots, features),
        ("tile", "inf"),
        split_axis=0,
        concat_axis=0,
        tiled=True,
        axis_index_groups=groups,
    )
    block_shape = block.shape
    x_before, x_after, y_halo, coeff = stencil_finish(
        state_t, diffusivity, x_from_before, x_from_after, PASSES
    )
    block, x_before, x_after, y_halo = lax.optimization_barrier(
        (block, x_before, x_after, y_halo)
    )
    own_rows = standardize(block[:, :capacity].reshape(-1, features))
    own = network_rows(own_rows, first_layer[0], second_layer[0], third_layer[0], last_layer[0])
    other_rows = standardize(block[:, capacity:].reshape(-1, features))
    other = network_rows(other_rows, *mirrored)
    answered = jnp.concatenate(
        [own.reshape(group_size, capacity, features), other.reshape(group_size, capacity, features)],
        axis=1,
    )
    returned = lax.all_to_all(
        answered,
        ("tile", "inf"),
        split_axis=0,
        concat_axis=0,
        tiled=True,
        axis_index_groups=groups,
    )
    returned_rows = returned.reshape(slot_total, features)

    rows_ext, ylen = coeff.shape[:2]
    diffused = pl.pallas_call(
        diffuse_kernel,
        out_shape=jax.ShapeDtypeStruct((width_x, width_y, features), jnp.float32),
        in_specs=[vmem] * 5,
        out_specs=vmem,
        scratch_shapes=[
            pltpu.VMEM((rows_ext, ylen, features), jnp.float32),
            pltpu.VMEM((rows_ext, ylen, features), jnp.float32),
        ],
        compiler_params=pltpu.CompilerParams(vmem_limit_bytes=100 * 1024 * 1024),
    )(state_t, x_before, x_after, y_halo, coeff)
    u_next, v_next = pl.pallas_call(
        finish_kernel,
        out_shape=(
            jax.ShapeDtypeStruct((levels, cells), jnp.float32),
            jax.ShapeDtypeStruct((levels, cells), jnp.float32),
        ),
        in_specs=[smem, smem, vmem, vmem],
        out_specs=(hbm, hbm),
        scratch_shapes=[
            pltpu.VMEM((cells, features), jnp.float32),
            pltpu.VMEM((width_x, features, width_y), jnp.float32),
            pltpu.SemaphoreType.DMA((2, width_x)),
        ],
    )(slot_index, active_columns, returned_rows, diffused.reshape(cells, features))
    return (u_next.reshape(u_field.shape), v_next.reshape(v_field.shape))


def solution(mesh):
    in_specs = (
        P(None, "tile", "inf"),
        P(None, "tile", "inf"),
        P("tile", "inf"),
        P(("tile", "inf")),
        P(("tile", "inf"), None),
        P(("tile", "inf"), None, None),
        P(("tile", "inf"), None, None),
        P(("tile", "inf"), None, None),
        P(("tile", "inf"), None, None),
    )
    out_specs = (P(None, "tile", "inf"), P(None, "tile", "inf"))
    return jax.shard_map(body, mesh=mesh, in_specs=in_specs, out_specs=out_specs, check_vma=False)
```

```python
import jax
import jax.numpy as jnp
from jax import lax
from jax.experimental import pallas as pl
from jax.experimental.pallas import tpu as pltpu
from jax.sharding import PartitionSpec as P

PASSES = 4


def halos(x, axis, dim, width):
    count, length = (lax.axis_size(axis), x.shape[dim])
    up = [(i, i + 1) for i in range(count - 1)]
    down = [(j, i) for i, j in up]
    last = lax.slice_in_dim(x, length - width, length, axis=dim)
    first = lax.slice_in_dim(x, 0, width, axis=dim)
    before = lax.ppermute(last, axis, up)
    after = lax.ppermute(first, axis, down)
    return before, after


def stencil_start(u_field, v_field, diffusivity, depth):
    width_x = u_field.shape[1]

    def x_piece(start):
        rows = lambda a: lax.slice_in_dim(a, start, start + depth, axis=a.ndim - 2)
        return jnp.concatenate([rows(u_field), rows(v_field), rows(diffusivity)[None]], axis=0)

    tile_count = lax.axis_size("tile")
    up = [(i, i + 1) for i in range(tile_count - 1)]
    down = [(j, i) for i, j in up]
    before = lax.ppermute(x_piece(width_x - depth), "tile", up)
    after = lax.ppermute(x_piece(0), "tile", down)
    return before, after


def stencil_finish(state_t, diffusivity, before, after, depth):
    width_x, width_y, features = state_t.shape
    x_before = before[:features].transpose(1, 2, 0)
    x_after = after[:features].transpose(1, 2, 0)
    c_rows = jnp.concatenate([before[features], diffusivity, after[features]], axis=0)
    extended = jnp.concatenate([x_before, state_t, x_after], axis=0)

    def y_piece(start):
        rows = lax.slice_in_dim(extended, start, start + depth, axis=1)
        cols = lax.slice_in_dim(c_rows, start, start + depth, axis=1).T
        cols = jnp.pad(cols, ((0, 0), (0, features - cols.shape[1])))
        return jnp.concatenate([rows, cols[None]], axis=0)

    inf_count = lax.axis_size("inf")
    up = [(i, i + 1) for i in range(inf_count - 1)]
    down = [(j, i) for i, j in up]
    before = lax.ppermute(y_piece(width_y - depth), "inf", up)
    after = lax.ppermute(y_piece(0), "inf", down)
    rows_ext = extended.shape[0]
    y_halo = jnp.concatenate([after[:rows_ext], before[:rows_ext]], axis=1)
    c_ext = jnp.concatenate(
        [c_rows, after[rows_ext, :, :rows_ext].T, before[rows_ext, :, :rows_ext].T], axis=1
    )
    ylen = c_ext.shape[1]
    coeff = jnp.broadcast_to(c_ext[:, :, None], (rows_ext, ylen, features))
    return x_before, x_after, y_halo, coeff


def standardize(rows):
    center = jnp.mean(rows, axis=-1, keepdims=True)
    spread = jnp.mean(jnp.square(rows - center), axis=-1, keepdims=True)
    return (rows - center) * lax.rsqrt(spread + 1e-05)


def network_rows(rows, first_layer, second_layer, third_layer, last_layer):
    highest = lax.Precision.HIGH
    hidden = jax.nn.silu(jnp.dot(rows, first_layer, precision=highest))
    hidden = jax.nn.silu(jnp.dot(hidden, second_layer, precision=highest))
    hidden = jax.nn.silu(jnp.dot(hidden, third_layer, precision=highest))
    return jnp.dot(hidden, last_layer, precision=highest)


def gather_kernel(slot_ref, act_ref, u_hbm, v_hbm, st_ref, o_ref, buf, sems):
    levels = u_hbm.shape[0]
    width_x, features, width_y = buf.shape
    chunk = 128

    def copies(x):
        return (
            pltpu.make_async_copy(u_hbm.at[:, x, :], buf.at[x, pl.ds(0, levels), :], sems.at[0, x]),
            pltpu.make_async_copy(v_hbm.at[:, x, :], buf.at[x, pl.ds(levels, levels), :], sems.at[1, x]),
        )

    def start(x, carry):
        for copy in copies(x):
            copy.start()
        return carry

    lax.fori_loop(0, width_x, start, 0)

    def clear(k, carry):
        at = pl.ds(pl.multiple_of(k * chunk, chunk), chunk)
        o_ref[at, :] = jnp.zeros((chunk, features), jnp.float32)
        return carry

    lax.fori_loop(0, o_ref.shape[0] // chunk, clear, 0)

    def transpose_tile(x, carry):
        for copy in copies(x):
            copy.wait()
        st_ref[pl.ds(pl.multiple_of(x * width_y, width_y), width_y), :] = buf[x].T
        return carry

    lax.fori_loop(0, width_x, transpose_tile, 0)

    def place(r, carry):
        o_ref[pl.ds(slot_ref[r], 1), :] = st_ref[pl.ds(act_ref[r], 1), :]
        return carry

    lax.fori_loop(0, act_ref.shape[0], place, 0, unroll=8)


def diffuse_kernel(st_ref, xb_ref, xa_ref, yh_ref, c_ref, f_ref, e_ref, a_ref):
    width_x, width_y, _ = st_ref.shape
    depth = xb_ref.shape[0]
    rows_ext, ylen, _ = c_ref.shape
    e_ref[0:depth, 0:width_y, :] = xb_ref[...]
    e_ref[depth + width_x :, 0:width_y, :] = xa_ref[...]

    def fill(x, carry):
        e_ref[x + depth, 0:width_y, :] = st_ref[x]
        return carry

    lax.fori_loop(0, width_x, fill, 0)
    e_ref[:, width_y:, :] = yh_ref[...]

    def sweep(src, dst, p, last):
        def one(x, carry):
            q = src[x]
            n = src[x + 1] + src[x - 1]
            n = n + pltpu.roll(q, ylen - 1, 0) + pltpu.roll(q, 1, 0)
            new = q + c_ref[x] * (n - 4.0 * q)
            if last:
                f_ref[x - depth] = new[:width_y]
            else:
                dst[x] = new
            return carry

        lax.fori_loop(p + 1, rows_ext - 1 - p, one, 0)

    for p in range(PASSES):
        src, dst = (e_ref, a_ref) if p % 2 == 0 else (a_ref, e_ref)
        sweep(src, dst, p, p == PASSES - 1)


def finish_kernel(slot_ref, act_ref, r_ref, f_ref, uo_hbm, vo_hbm, d_ref, obuf, sems):
    levels = uo_hbm.shape[0]
    width_x, features, width_y = obuf.shape

    def clear(x, carry):
        at = pl.ds(pl.multiple_of(x * width_y, width_y), width_y)
        d_ref[at, :] = jnp.zeros((width_y, features), jnp.float32)
        return carry

    lax.fori_loop(0, width_x, clear, 0)

    def place(r, carry):
        d_ref[pl.ds(act_ref[r], 1), :] = r_ref[pl.ds(slot_ref[r], 1), :]
        return carry

    lax.fori_loop(0, act_ref.shape[0], place, 0, unroll=8)

    def copies(x):
        return (
            pltpu.make_async_copy(obuf.at[x, pl.ds(0, levels), :], uo_hbm.at[:, x, :], sems.at[0, x]),
            pltpu.make_async_copy(obuf.at[x, pl.ds(levels, levels), :], vo_hbm.at[:, x, :], sems.at[1, x]),
        )

    def transpose_tile(x, carry):
        at = pl.ds(pl.multiple_of(x * width_y, width_y), width_y)
        obuf[x] = (f_ref[at, :] + d_ref[at, :]).T
        for copy in copies(x):
            copy.start()
        return carry

    lax.fori_loop(0, width_x, transpose_tile, 0)

    def finish(x, carry):
        for copy in copies(x):
            copy.wait()
        return carry

    lax.fori_loop(0, width_x, finish, 0)


def body(
    u_field,
    v_field,
    diffusivity,
    active_columns,
    regimes,
    first_layer,
    second_layer,
    third_layer,
    last_layer,
):
    levels, width_x, width_y = u_field.shape
    features = 2 * levels
    cells = width_x * width_y
    active_count = active_columns.shape[0]
    devices_all = lax.axis_size(("tile", "inf"))
    capacity = 2 * active_count // devices_all
    slot_total = devices_all * capacity
    block_rows = min(512, active_count)
    block_count = active_count // block_rows
    target = regimes[:, 0]
    labels = jnp.arange(devices_all, dtype=jnp.int32)
    one_hot = (
        (target[:, None] == labels[None, :])
        .astype(jnp.bfloat16)
        .reshape(block_count, block_rows, devices_all)
    )
    row_ids = jnp.arange(block_rows, dtype=jnp.int32)
    lower = (row_ids[:, None] > row_ids[None, :]).astype(jnp.bfloat16)

    def rank_step(counts, piece):
        earlier = jnp.dot(lower, piece, preferred_element_type=jnp.float32) + counts[None, :]
        wide_piece = piece.astype(jnp.float32)
        rank = jnp.sum(earlier * wide_piece, axis=1)
        return (counts + jnp.sum(wide_piece, axis=0), rank)

    _, ranks = lax.scan(rank_step, jnp.zeros((devices_all,), jnp.float32), one_hot)
    tile_count, inf_count = lax.axis_size("tile"), lax.axis_size("inf")
    half_tiles = tile_count // 2
    my_half = lax.axis_index("tile") // half_tiles
    target_tile = target // inf_count
    place = (target_tile % half_tiles) * inf_count + target % inf_count
    kind = (target_tile // half_tiles != my_half).astype(jnp.int32)
    pair_slots = 2 * capacity
    slot_index = place * pair_slots + kind * capacity + ranks.reshape(-1).astype(jnp.int32)
    groups = [
        [t * inf_count + i for t in range(h * half_tiles, (h + 1) * half_tiles) for i in range(inf_count)]
        for h in range(2)
    ]
    group_size = half_tiles * inf_count
    swap = [(t, (t + half_tiles) % tile_count) for t in range(tile_count)]
    mirrored = [
        lax.ppermute(w[0], "tile", swap) for w in (first_layer, second_layer, third_layer, last_layer)
    ]
    vmem = pl.BlockSpec(memory_space=pltpu.VMEM)
    smem = pl.BlockSpec(memory_space=pltpu.SMEM)
    x_from_before, x_from_after = stencil_start(u_field, v_field, diffusivity, PASSES)
    hbm = pl.BlockSpec(memory_space=pl.ANY)
    state_t, outgoing = pl.pallas_call(
        gather_kernel,
        out_shape=(
            jax.ShapeDtypeStruct((cells, features), jnp.float32),
            jax.ShapeDtypeStruct((slot_total, features), jnp.float32),
        ),
        in_specs=[smem, smem, hbm, hbm],
        out_specs=(vmem, vmem),
        scratch_shapes=[
            pltpu.VMEM((width_x, features, width_y), jnp.float32),
            pltpu.SemaphoreType.DMA((2, width_x)),
        ],
    )(slot_index, active_columns, u_field, v_field)
    state_t = state_t.reshape(width_x, width_y, features)
    outgoing, x_from_before, x_from_after = lax.optimization_barrier(
        (outgoing, x_from_before, x_from_after)
    )
    block = lax.all_to_all(
        outgoing.reshape(group_size, pair_slots, features),
        ("tile", "inf"),
        split_axis=0,
        concat_axis=0,
        tiled=True,
        axis_index_groups=groups,
    )
    block_shape = block.shape
    x_before, x_after, y_halo, coeff = stencil_finish(
        state_t, diffusivity, x_from_before, x_from_after, PASSES
    )
    block, x_before, x_after, y_halo = lax.optimization_barrier(
        (block, x_before, x_after, y_halo)
    )
    own_rows = standardize(block[:, :capacity].reshape(-1, features))
    own = network_rows(own_rows, first_layer[0], second_layer[0], third_layer[0], last_layer[0])
    other_rows = standardize(block[:, capacity:].reshape(-1, features))
    other = network_rows(other_rows, *mirrored)
    answered = jnp.concatenate(
        [own.reshape(group_size, capacity, features), other.reshape(group_size, capacity, features)],
        axis=1,
    )
    returned = lax.all_to_all(
        answered,
        ("tile", "inf"),
        split_axis=0,
        concat_axis=0,
        tiled=True,
        axis_index_groups=groups,
    )
    returned_rows = returned.reshape(slot_total, features)

    rows_ext, ylen = coeff.shape[:2]
    diffused = pl.pallas_call(
        diffuse_kernel,
        out_shape=jax.ShapeDtypeStruct((width_x, width_y, features), jnp.float32),
        in_specs=[vmem] * 5,
        out_specs=vmem,
        scratch_shapes=[
            pltpu.VMEM((rows_ext, ylen, features), jnp.float32),
            pltpu.VMEM((rows_ext, ylen, features), jnp.float32),
        ],
        compiler_params=pltpu.CompilerParams(vmem_limit_bytes=100 * 1024 * 1024),
    )(state_t, x_before, x_after, y_halo, coeff)
    u_next, v_next = pl.pallas_call(
        finish_kernel,
        out_shape=(
            jax.ShapeDtypeStruct(u_field.shape, jnp.float32),
            jax.ShapeDtypeStruct(v_field.shape, jnp.float32),
        ),
        in_specs=[smem, smem, vmem, vmem],
        out_specs=(hbm, hbm),
        scratch_shapes=[
            pltpu.VMEM((cells, features), jnp.float32),
            pltpu.VMEM((width_x, features, width_y), jnp.float32),
            pltpu.SemaphoreType.DMA((2, width_x)),
        ],
    )(slot_index, active_columns, returned_rows, diffused.reshape(cells, features))
    return (u_next, v_next)


def solution(mesh):
    in_specs = (
        P(None, "tile", "inf"),
        P(None, "tile", "inf"),
        P("tile", "inf"),
        P(("tile", "inf")),
        P(("tile", "inf"), None),
        P(("tile", "inf"), None, None),
        P(("tile", "inf"), None, None),
        P(("tile", "inf"), None, None),
        P(("tile", "inf"), None, None),
    )
    out_specs = (P(None, "tile", "inf"), P(None, "tile", "inf"))
    return jax.shard_map(body, mesh=mesh, in_specs=in_specs, out_specs=out_specs, check_vma=False)
```

```python
import jax
import jax.numpy as jnp
from jax import lax
from jax.experimental import pallas as pl
from jax.experimental.pallas import tpu as pltpu
from jax.sharding import PartitionSpec as P

PASSES = 4


def halos(x, axis, dim, width):
    count, length = (lax.axis_size(axis), x.shape[dim])
    up = [(i, i + 1) for i in range(count - 1)]
    down = [(j, i) for i, j in up]
    last = lax.slice_in_dim(x, length - width, length, axis=dim)
    first = lax.slice_in_dim(x, 0, width, axis=dim)
    before = lax.ppermute(last, axis, up)
    after = lax.ppermute(first, axis, down)
    return before, after


def stencil_start(u_field, v_field, diffusivity, depth):
    width_x = u_field.shape[1]

    def x_piece(start):
        rows = lambda a: lax.slice_in_dim(a, start, start + depth, axis=a.ndim - 2)
        return jnp.concatenate([rows(u_field), rows(v_field), rows(diffusivity)[None]], axis=0)

    tile_count = lax.axis_size("tile")
    up = [(i, i + 1) for i in range(tile_count - 1)]
    down = [(j, i) for i, j in up]
    before = lax.ppermute(x_piece(width_x - depth), "tile", up)
    after = lax.ppermute(x_piece(0), "tile", down)
    return before, after


def stencil_finish(state_t, diffusivity, before, after, depth):
    width_x, width_y, features = state_t.shape
    x_before = before[:features].transpose(1, 2, 0)
    x_after = after[:features].transpose(1, 2, 0)
    c_rows = jnp.concatenate([before[features], diffusivity, after[features]], axis=0)
    extended = jnp.concatenate([x_before, state_t, x_after], axis=0)

    def y_piece(start):
        rows = lax.slice_in_dim(extended, start, start + depth, axis=1)
        cols = lax.slice_in_dim(c_rows, start, start + depth, axis=1).T
        cols = jnp.pad(cols, ((0, 0), (0, features - cols.shape[1])))
        return jnp.concatenate([rows, cols[None]], axis=0)

    inf_count = lax.axis_size("inf")
    up = [(i, i + 1) for i in range(inf_count - 1)]
    down = [(j, i) for i, j in up]
    before = lax.ppermute(y_piece(width_y - depth), "inf", up)
    after = lax.ppermute(y_piece(0), "inf", down)
    rows_ext = extended.shape[0]
    y_halo = jnp.concatenate([after[:rows_ext], before[:rows_ext]], axis=1)
    c_ext = jnp.concatenate(
        [c_rows, after[rows_ext, :, :rows_ext].T, before[rows_ext, :, :rows_ext].T], axis=1
    )
    ylen = c_ext.shape[1]
    coeff = jnp.broadcast_to(c_ext[:, :, None], (rows_ext, ylen, features))
    return x_before, x_after, y_halo, coeff


def standardize(rows):
    center = jnp.mean(rows, axis=-1, keepdims=True)
    spread = jnp.mean(jnp.square(rows - center), axis=-1, keepdims=True)
    return (rows - center) * lax.rsqrt(spread + 1e-05)


def network_rows(rows, first_layer, second_layer, third_layer, last_layer):
    highest = lax.Precision.HIGH
    hidden = jax.nn.silu(jnp.dot(rows, first_layer, precision=highest))
    hidden = jax.nn.silu(jnp.dot(hidden, second_layer, precision=highest))
    hidden = jax.nn.silu(jnp.dot(hidden, third_layer, precision=highest))
    return jnp.dot(hidden, last_layer, precision=highest)


def gather_kernel(slot_ref, act_ref, u_hbm, v_hbm, st_ref, o_ref, buf, sems):
    levels = u_hbm.shape[0]
    width_x, features, width_y = buf.shape
    chunk = 128

    def copies(x):
        return (
            pltpu.make_async_copy(u_hbm.at[:, x, :], buf.at[x, pl.ds(0, levels), :], sems.at[0, x]),
            pltpu.make_async_copy(v_hbm.at[:, x, :], buf.at[x, pl.ds(levels, levels), :], sems.at[1, x]),
        )

    def start(x, carry):
        for copy in copies(x):
            copy.start()
        return carry

    lax.fori_loop(0, width_x, start, 0)

    def clear(k, carry):
        at = pl.ds(pl.multiple_of(k * chunk, chunk), chunk)
        o_ref[at, :] = jnp.zeros((chunk, features), jnp.float32)
        return carry

    lax.fori_loop(0, o_ref.shape[0] // chunk, clear, 0)

    def transpose_tile(x, carry):
        for copy in copies(x):
            copy.wait()
        st_ref[pl.ds(pl.multiple_of(x * width_y, width_y), width_y), :] = buf[x].T
        return carry

    lax.fori_loop(0, width_x, transpose_tile, 0)

    def place(r, carry):
        o_ref[pl.ds(slot_ref[r], 1), :] = st_ref[pl.ds(act_ref[r], 1), :]
        return carry

    lax.fori_loop(0, act_ref.shape[0], place, 0, unroll=8)


def diffuse_kernel(st_ref, xb_ref, xa_ref, yh_ref, c_ref, f_ref, e_ref, a_ref):
    width_x, width_y, _ = st_ref.shape
    depth = xb_ref.shape[0]
    rows_ext, ylen, _ = c_ref.shape
    e_ref[0:depth, 0:width_y, :] = xb_ref[...]
    e_ref[depth + width_x :, 0:width_y, :] = xa_ref[...]

    def fill(x, carry):
        e_ref[x + depth, 0:width_y, :] = st_ref[x]
        return carry

    lax.fori_loop(0, width_x, fill, 0)
    e_ref[:, width_y:, :] = yh_ref[...]

    def sweep(src, dst, p, last):
        def one(x, carry):
            q = src[x]
            n = src[x + 1] + src[x - 1]
            n = n + pltpu.roll(q, ylen - 1, 0) + pltpu.roll(q, 1, 0)
            new = q + c_ref[x] * (n - 4.0 * q)
            if last:
                f_ref[x - depth] = new[:width_y]
            else:
                dst[x] = new
            return carry

        lax.fori_loop(p + 1, rows_ext - 1 - p, one, 0)

    for p in range(PASSES):
        src, dst = (e_ref, a_ref) if p % 2 == 0 else (a_ref, e_ref)
        sweep(src, dst, p, p == PASSES - 1)


def finish_kernel(slot_ref, act_ref, r_ref, f_ref, uo_hbm, vo_hbm, d_ref, obuf, sems):
    levels = uo_hbm.shape[0]
    width_x, features, width_y = obuf.shape

    def clear(x, carry):
        at = pl.ds(pl.multiple_of(x * width_y, width_y), width_y)
        d_ref[at, :] = jnp.zeros((width_y, features), jnp.float32)
        return carry

    lax.fori_loop(0, width_x, clear, 0)

    def place(r, carry):
        d_ref[pl.ds(act_ref[r], 1), :] = r_ref[pl.ds(slot_ref[r], 1), :]
        return carry

    lax.fori_loop(0, act_ref.shape[0], place, 0, unroll=8)

    def copies(x):
        return (
            pltpu.make_async_copy(obuf.at[x, pl.ds(0, levels), :], uo_hbm.at[:, x, :], sems.at[0, x]),
            pltpu.make_async_copy(obuf.at[x, pl.ds(levels, levels), :], vo_hbm.at[:, x, :], sems.at[1, x]),
        )

    def transpose_tile(x, carry):
        at = pl.ds(pl.multiple_of(x * width_y, width_y), width_y)
        obuf[x] = (f_ref[at, :] + d_ref[at, :]).T
        for copy in copies(x):
            copy.start()
        return carry

    lax.fori_loop(0, width_x, transpose_tile, 0)

    def finish(x, carry):
        for copy in copies(x):
            copy.wait()
        return carry

    lax.fori_loop(0, width_x, finish, 0)


def body(
    u_field,
    v_field,
    diffusivity,
    active_columns,
    regimes,
    first_layer,
    second_layer,
    third_layer,
    last_layer,
):
    levels, width_x, width_y = u_field.shape
    features = 2 * levels
    cells = width_x * width_y
    active_count = active_columns.shape[0]
    devices_all = lax.axis_size(("tile", "inf"))
    capacity = 2 * active_count // devices_all
    slot_total = devices_all * capacity
    block_rows = min(512, active_count)
    block_count = active_count // block_rows
    target = regimes[:, 0]
    labels = jnp.arange(devices_all, dtype=jnp.int32)
    one_hot = (
        (target[:, None] == labels[None, :])
        .astype(jnp.bfloat16)
        .reshape(block_count, block_rows, devices_all)
    )
    row_ids = jnp.arange(block_rows, dtype=jnp.int32)
    lower = (row_ids[:, None] > row_ids[None, :]).astype(jnp.bfloat16)

    def rank_step(counts, piece):
        earlier = jnp.dot(lower, piece, preferred_element_type=jnp.float32) + counts[None, :]
        wide_piece = piece.astype(jnp.float32)
        rank = jnp.sum(earlier * wide_piece, axis=1)
        return (counts + jnp.sum(wide_piece, axis=0), rank)

    _, ranks = lax.scan(rank_step, jnp.zeros((devices_all,), jnp.float32), one_hot)
    tile_count, inf_count = lax.axis_size("tile"), lax.axis_size("inf")
    half_tiles = tile_count // 2
    my_half = lax.axis_index("tile") // half_tiles
    target_tile = target // inf_count
    place = (target_tile % half_tiles) * inf_count + target % inf_count
    kind = (target_tile // half_tiles != my_half).astype(jnp.int32)
    pair_slots = 2 * capacity
    group_size = half_tiles * inf_count
    slot_index = (kind * group_size + place) * capacity + ranks.reshape(-1).astype(jnp.int32)
    groups = [
        [t * inf_count + i for t in range(h * half_tiles, (h + 1) * half_tiles) for i in range(inf_count)]
        for h in range(2)
    ]
    group_size = half_tiles * inf_count
    swap = [(t, (t + half_tiles) % tile_count) for t in range(tile_count)]
    mirrored = [
        lax.ppermute(w[0], "tile", swap) for w in (first_layer, second_layer, third_layer, last_layer)
    ]
    vmem = pl.BlockSpec(memory_space=pltpu.VMEM)
    smem = pl.BlockSpec(memory_space=pltpu.SMEM)
    x_from_before, x_from_after = stencil_start(u_field, v_field, diffusivity, PASSES)
    hbm = pl.BlockSpec(memory_space=pl.ANY)
    state_t, outgoing = pl.pallas_call(
        gather_kernel,
        out_shape=(
            jax.ShapeDtypeStruct((cells, features), jnp.float32),
            jax.ShapeDtypeStruct((slot_total, features), jnp.float32),
        ),
        in_specs=[smem, smem, hbm, hbm],
        out_specs=(vmem, vmem),
        scratch_shapes=[
            pltpu.VMEM((width_x, features, width_y), jnp.float32),
            pltpu.SemaphoreType.DMA((2, width_x)),
        ],
    )(slot_index, active_columns, u_field, v_field)
    state_t = state_t.reshape(width_x, width_y, features)
    outgoing, x_from_before, x_from_after = lax.optimization_barrier(
        (outgoing, x_from_before, x_from_after)
    )
    exchange = lambda a: lax.all_to_all(
        a, ("tile", "inf"), split_axis=0, concat_axis=0, tiled=True, axis_index_groups=groups
    )
    halves = outgoing.reshape(2, group_size, capacity, features)
    block_own = exchange(halves[0])
    block_other = exchange(halves[1])
    x_before, x_after, y_halo, coeff = stencil_finish(
        state_t, diffusivity, x_from_before, x_from_after, PASSES
    )
    block_own, x_before, x_after, y_halo = lax.optimization_barrier(
        (block_own, x_before, x_after, y_halo)
    )
    own_rows = standardize(block_own.reshape(-1, features))
    own = network_rows(own_rows, first_layer[0], second_layer[0], third_layer[0], last_layer[0])
    returned_own = exchange(own.reshape(group_size, capacity, features))
    other_rows = standardize(block_other.reshape(-1, features))
    other = network_rows(other_rows, *mirrored)
    returned_other = exchange(other.reshape(group_size, capacity, features))
    returned = jnp.concatenate([returned_own, returned_other], axis=0)
    returned_rows = returned.reshape(slot_total, features)

    rows_ext, ylen = coeff.shape[:2]
    diffused = pl.pallas_call(
        diffuse_kernel,
        out_shape=jax.ShapeDtypeStruct((width_x, width_y, features), jnp.float32),
        in_specs=[vmem] * 5,
        out_specs=vmem,
        scratch_shapes=[
            pltpu.VMEM((rows_ext, ylen, features), jnp.float32),
            pltpu.VMEM((rows_ext, ylen, features), jnp.float32),
        ],
        compiler_params=pltpu.CompilerParams(vmem_limit_bytes=100 * 1024 * 1024),
    )(state_t, x_before, x_after, y_halo, coeff)
    u_next, v_next = pl.pallas_call(
        finish_kernel,
        out_shape=(
            jax.ShapeDtypeStruct(u_field.shape, jnp.float32),
            jax.ShapeDtypeStruct(v_field.shape, jnp.float32),
        ),
        in_specs=[smem, smem, vmem, vmem],
        out_specs=(hbm, hbm),
        scratch_shapes=[
            pltpu.VMEM((cells, features), jnp.float32),
            pltpu.VMEM((width_x, features, width_y), jnp.float32),
            pltpu.SemaphoreType.DMA((2, width_x)),
        ],
    )(slot_index, active_columns, returned_rows, diffused.reshape(cells, features))
    return (u_next, v_next)


def solution(mesh):
    in_specs = (
        P(None, "tile", "inf"),
        P(None, "tile", "inf"),
        P("tile", "inf"),
        P(("tile", "inf")),
        P(("tile", "inf"), None),
        P(("tile", "inf"), None, None),
        P(("tile", "inf"), None, None),
        P(("tile", "inf"), None, None),
        P(("tile", "inf"), None, None),
    )
    out_specs = (P(None, "tile", "inf"), P(None, "tile", "inf"))
    return jax.shard_map(body, mesh=mesh, in_specs=in_specs, out_specs=out_specs, check_vma=False)
```

```python
import jax
import jax.numpy as jnp
from jax import lax
from jax.experimental import pallas as pl
from jax.experimental.pallas import tpu as pltpu
from jax.sharding import PartitionSpec as P

PASSES = 4


def halos(x, axis, dim, width):
    count, length = (lax.axis_size(axis), x.shape[dim])
    up = [(i, i + 1) for i in range(count - 1)]
    down = [(j, i) for i, j in up]
    last = lax.slice_in_dim(x, length - width, length, axis=dim)
    first = lax.slice_in_dim(x, 0, width, axis=dim)
    before = lax.ppermute(last, axis, up)
    after = lax.ppermute(first, axis, down)
    return before, after


def stencil_start(u_field, v_field, diffusivity, depth):
    width_x = u_field.shape[1]

    def x_piece(start):
        rows = lambda a: lax.slice_in_dim(a, start, start + depth, axis=a.ndim - 2)
        return jnp.concatenate([rows(u_field), rows(v_field), rows(diffusivity)[None]], axis=0)

    tile_count = lax.axis_size("tile")
    up = [(i, i + 1) for i in range(tile_count - 1)]
    down = [(j, i) for i, j in up]
    before = lax.ppermute(x_piece(width_x - depth), "tile", up)
    after = lax.ppermute(x_piece(0), "tile", down)
    return before, after


def stencil_finish(state_t, diffusivity, before, after, depth):
    width_x, width_y, features = state_t.shape
    x_before = before[:features].transpose(1, 2, 0)
    x_after = after[:features].transpose(1, 2, 0)
    c_rows = jnp.concatenate([before[features], diffusivity, after[features]], axis=0)
    extended = jnp.concatenate([x_before, state_t, x_after], axis=0)

    def y_piece(start):
        rows = lax.slice_in_dim(extended, start, start + depth, axis=1)
        cols = lax.slice_in_dim(c_rows, start, start + depth, axis=1).T
        cols = jnp.pad(cols, ((0, 0), (0, features - cols.shape[1])))
        return jnp.concatenate([rows, cols[None]], axis=0)

    inf_count = lax.axis_size("inf")
    up = [(i, i + 1) for i in range(inf_count - 1)]
    down = [(j, i) for i, j in up]
    before = lax.ppermute(y_piece(width_y - depth), "inf", up)
    after = lax.ppermute(y_piece(0), "inf", down)
    rows_ext = extended.shape[0]
    y_halo = jnp.concatenate([after[:rows_ext], before[:rows_ext]], axis=1)
    c_ext = jnp.concatenate(
        [c_rows, after[rows_ext, :, :rows_ext].T, before[rows_ext, :, :rows_ext].T], axis=1
    )
    ylen = c_ext.shape[1]
    coeff = jnp.broadcast_to(c_ext[:, :, None], (rows_ext, ylen, features))
    return x_before, x_after, y_halo, coeff


def standardize(rows):
    center = jnp.mean(rows, axis=-1, keepdims=True)
    spread = jnp.mean(jnp.square(rows - center), axis=-1, keepdims=True)
    return (rows - center) * lax.rsqrt(spread + 1e-05)


def network_rows(rows, first_layer, second_layer, third_layer, last_layer):
    highest = lax.Precision.HIGH
    hidden = jax.nn.silu(jnp.dot(rows, first_layer, precision=highest))
    hidden = jax.nn.silu(jnp.dot(hidden, second_layer, precision=highest))
    hidden = jax.nn.silu(jnp.dot(hidden, third_layer, precision=highest))
    return jnp.dot(hidden, last_layer, precision=highest)


def gather_kernel(slot_ref, act_ref, u_hbm, v_hbm, st_ref, o_ref, buf, sems):
    levels = u_hbm.shape[0]
    width_x, features, width_y = buf.shape
    chunk = 128

    def copies(x):
        return (
            pltpu.make_async_copy(u_hbm.at[:, x, :], buf.at[x, pl.ds(0, levels), :], sems.at[0, x]),
            pltpu.make_async_copy(v_hbm.at[:, x, :], buf.at[x, pl.ds(levels, levels), :], sems.at[1, x]),
        )

    def start(x, carry):
        for copy in copies(x):
            copy.start()
        return carry

    lax.fori_loop(0, width_x, start, 0)

    def clear(k, carry):
        at = pl.ds(pl.multiple_of(k * chunk, chunk), chunk)
        o_ref[at, :] = jnp.zeros((chunk, features), jnp.float32)
        return carry

    lax.fori_loop(0, o_ref.shape[0] // chunk, clear, 0)

    def transpose_tile(x, carry):
        for copy in copies(x):
            copy.wait()
        st_ref[pl.ds(pl.multiple_of(x * width_y, width_y), width_y), :] = buf[x].T
        return carry

    lax.fori_loop(0, width_x, transpose_tile, 0)

    def place(r, carry):
        o_ref[pl.ds(slot_ref[r], 1), :] = st_ref[pl.ds(act_ref[r], 1), :]
        return carry

    lax.fori_loop(0, act_ref.shape[0], place, 0, unroll=8)

    def normalize(k, carry):
        at = pl.ds(pl.multiple_of(k * chunk, chunk), chunk)
        o_ref[at, :] = standardize(o_ref[at, :])
        return carry

    lax.fori_loop(0, o_ref.shape[0] // chunk, normalize, 0)


def diffuse_kernel(st_ref, xb_ref, xa_ref, yh_ref, c_ref, f_ref, e_ref, a_ref):
    width_x, width_y, _ = st_ref.shape
    depth = xb_ref.shape[0]
    rows_ext, ylen, _ = c_ref.shape
    e_ref[0:depth, 0:width_y, :] = xb_ref[...]
    e_ref[depth + width_x :, 0:width_y, :] = xa_ref[...]

    def fill(x, carry):
        e_ref[x + depth, 0:width_y, :] = st_ref[x]
        return carry

    lax.fori_loop(0, width_x, fill, 0)
    e_ref[:, width_y:, :] = yh_ref[...]

    def sweep(src, dst, p, last):
        def one(x, carry):
            q = src[x]
            n = src[x + 1] + src[x - 1]
            n = n + pltpu.roll(q, ylen - 1, 0) + pltpu.roll(q, 1, 0)
            new = q + c_ref[x] * (n - 4.0 * q)
            if last:
                f_ref[x - depth] = new[:width_y]
            else:
                dst[x] = new
            return carry

        lax.fori_loop(p + 1, rows_ext - 1 - p, one, 0)

    for p in range(PASSES):
        src, dst = (e_ref, a_ref) if p % 2 == 0 else (a_ref, e_ref)
        sweep(src, dst, p, p == PASSES - 1)


def finish_kernel(slot_ref, act_ref, r_ref, f_ref, uo_hbm, vo_hbm, d_ref, obuf, sems):
    levels = uo_hbm.shape[0]
    width_x, features, width_y = obuf.shape

    def clear(x, carry):
        at = pl.ds(pl.multiple_of(x * width_y, width_y), width_y)
        d_ref[at, :] = jnp.zeros((width_y, features), jnp.float32)
        return carry

    lax.fori_loop(0, width_x, clear, 0)

    def place(r, carry):
        d_ref[pl.ds(act_ref[r], 1), :] = r_ref[pl.ds(slot_ref[r], 1), :]
        return carry

    lax.fori_loop(0, act_ref.shape[0], place, 0, unroll=8)

    def copies(x):
        return (
            pltpu.make_async_copy(obuf.at[x, pl.ds(0, levels), :], uo_hbm.at[:, x, :], sems.at[0, x]),
            pltpu.make_async_copy(obuf.at[x, pl.ds(levels, levels), :], vo_hbm.at[:, x, :], sems.at[1, x]),
        )

    def transpose_tile(x, carry):
        at = pl.ds(pl.multiple_of(x * width_y, width_y), width_y)
        obuf[x] = (f_ref[at, :] + d_ref[at, :]).T
        for copy in copies(x):
            copy.start()
        return carry

    lax.fori_loop(0, width_x, transpose_tile, 0)

    def finish(x, carry):
        for copy in copies(x):
            copy.wait()
        return carry

    lax.fori_loop(0, width_x, finish, 0)


def body(
    u_field,
    v_field,
    diffusivity,
    active_columns,
    regimes,
    first_layer,
    second_layer,
    third_layer,
    last_layer,
):
    levels, width_x, width_y = u_field.shape
    features = 2 * levels
    cells = width_x * width_y
    active_count = active_columns.shape[0]
    devices_all = lax.axis_size(("tile", "inf"))
    capacity = 2 * active_count // devices_all
    slot_total = devices_all * capacity
    block_rows = min(512, active_count)
    block_count = active_count // block_rows
    target = regimes[:, 0]
    labels = jnp.arange(devices_all, dtype=jnp.int32)
    one_hot = (
        (target[:, None] == labels[None, :])
        .astype(jnp.bfloat16)
        .reshape(block_count, block_rows, devices_all)
    )
    row_ids = jnp.arange(block_rows, dtype=jnp.int32)
    lower = (row_ids[:, None] > row_ids[None, :]).astype(jnp.bfloat16)

    def rank_step(counts, piece):
        earlier = jnp.dot(lower, piece, preferred_element_type=jnp.float32) + counts[None, :]
        wide_piece = piece.astype(jnp.float32)
        rank = jnp.sum(earlier * wide_piece, axis=1)
        return (counts + jnp.sum(wide_piece, axis=0), rank)

    _, ranks = lax.scan(rank_step, jnp.zeros((devices_all,), jnp.float32), one_hot)
    tile_count, inf_count = lax.axis_size("tile"), lax.axis_size("inf")
    half_tiles = tile_count // 2
    my_half = lax.axis_index("tile") // half_tiles
    target_tile = target // inf_count
    place = (target_tile % half_tiles) * inf_count + target % inf_count
    kind = (target_tile // half_tiles != my_half).astype(jnp.int32)
    pair_slots = 2 * capacity
    slot_index = place * pair_slots + kind * capacity + ranks.reshape(-1).astype(jnp.int32)
    groups = [
        [t * inf_count + i for t in range(h * half_tiles, (h + 1) * half_tiles) for i in range(inf_count)]
        for h in range(2)
    ]
    group_size = half_tiles * inf_count
    swap = [(t, (t + half_tiles) % tile_count) for t in range(tile_count)]
    mirrored = [
        lax.ppermute(w[0], "tile", swap) for w in (first_layer, second_layer, third_layer, last_layer)
    ]
    vmem = pl.BlockSpec(memory_space=pltpu.VMEM)
    smem = pl.BlockSpec(memory_space=pltpu.SMEM)
    x_from_before, x_from_after = stencil_start(u_field, v_field, diffusivity, PASSES)
    hbm = pl.BlockSpec(memory_space=pl.ANY)
    state_t, outgoing = pl.pallas_call(
        gather_kernel,
        out_shape=(
            jax.ShapeDtypeStruct((cells, features), jnp.float32),
            jax.ShapeDtypeStruct((slot_total, features), jnp.float32),
        ),
        in_specs=[smem, smem, hbm, hbm],
        out_specs=(vmem, vmem),
        scratch_shapes=[
            pltpu.VMEM((width_x, features, width_y), jnp.float32),
            pltpu.SemaphoreType.DMA((2, width_x)),
        ],
    )(slot_index, active_columns, u_field, v_field)
    state_t = state_t.reshape(width_x, width_y, features)
    outgoing, x_from_before, x_from_after = lax.optimization_barrier(
        (outgoing, x_from_before, x_from_after)
    )
    block = lax.all_to_all(
        outgoing.reshape(group_size, pair_slots, features),
        ("tile", "inf"),
        split_axis=0,
        concat_axis=0,
        tiled=True,
        axis_index_groups=groups,
    )
    block_shape = block.shape
    x_before, x_after, y_halo, coeff = stencil_finish(
        state_t, diffusivity, x_from_before, x_from_after, PASSES
    )
    block, x_before, x_after, y_halo = lax.optimization_barrier(
        (block, x_before, x_after, y_halo)
    )
    own_rows = block[:, :capacity].reshape(-1, features)
    own = network_rows(own_rows, first_layer[0], second_layer[0], third_layer[0], last_layer[0])
    other_rows = block[:, capacity:].reshape(-1, features)
    other = network_rows(other_rows, *mirrored)
    answered = jnp.concatenate(
        [own.reshape(group_size, capacity, features), other.reshape(group_size, capacity, features)],
        axis=1,
    )
    returned = lax.all_to_all(
        answered,
        ("tile", "inf"),
        split_axis=0,
        concat_axis=0,
        tiled=True,
        axis_index_groups=groups,
    )
    returned_rows = returned.reshape(slot_total, features)

    rows_ext, ylen = coeff.shape[:2]
    diffused = pl.pallas_call(
        diffuse_kernel,
        out_shape=jax.ShapeDtypeStruct((width_x, width_y, features), jnp.float32),
        in_specs=[vmem] * 5,
        out_specs=vmem,
        scratch_shapes=[
            pltpu.VMEM((rows_ext, ylen, features), jnp.float32),
            pltpu.VMEM((rows_ext, ylen, features), jnp.float32),
        ],
        compiler_params=pltpu.CompilerParams(vmem_limit_bytes=100 * 1024 * 1024),
    )(state_t, x_before, x_after, y_halo, coeff)
    u_next, v_next = pl.pallas_call(
        finish_kernel,
        out_shape=(
            jax.ShapeDtypeStruct(u_field.shape, jnp.float32),
            jax.ShapeDtypeStruct(v_field.shape, jnp.float32),
        ),
        in_specs=[smem, smem, vmem, vmem],
        out_specs=(hbm, hbm),
        scratch_shapes=[
            pltpu.VMEM((cells, features), jnp.float32),
            pltpu.VMEM((width_x, features, width_y), jnp.float32),
            pltpu.SemaphoreType.DMA((2, width_x)),
        ],
    )(slot_index, active_columns, returned_rows, diffused.reshape(cells, features))
    return (u_next, v_next)


def solution(mesh):
    in_specs = (
        P(None, "tile", "inf"),
        P(None, "tile", "inf"),
        P("tile", "inf"),
        P(("tile", "inf")),
        P(("tile", "inf"), None),
        P(("tile", "inf"), None, None),
        P(("tile", "inf"), None, None),
        P(("tile", "inf"), None, None),
        P(("tile", "inf"), None, None),
    )
    out_specs = (P(None, "tile", "inf"), P(None, "tile", "inf"))
    return jax.shard_map(body, mesh=mesh, in_specs=in_specs, out_specs=out_specs, check_vma=False)
```

```python
import jax
import jax.numpy as jnp
from jax import lax
from jax.experimental import pallas as pl
from jax.experimental.pallas import tpu as pltpu
from jax.sharding import PartitionSpec as P

PASSES = 4


def halos(x, axis, dim, width):
    count, length = (lax.axis_size(axis), x.shape[dim])
    up = [(i, i + 1) for i in range(count - 1)]
    down = [(j, i) for i, j in up]
    last = lax.slice_in_dim(x, length - width, length, axis=dim)
    first = lax.slice_in_dim(x, 0, width, axis=dim)
    before = lax.ppermute(last, axis, up)
    after = lax.ppermute(first, axis, down)
    return before, after


def stencil_start(u_field, v_field, diffusivity, depth, after_this):
    width_x = u_field.shape[1]

    def x_piece(start):
        rows = lambda a: lax.slice_in_dim(a, start, start + depth, axis=a.ndim - 2)
        return jnp.concatenate([rows(u_field), rows(v_field), rows(diffusivity)[None]], axis=0)

    tile_count = lax.axis_size("tile")
    up = [(i, i + 1) for i in range(tile_count - 1)]
    down = [(j, i) for i, j in up]
    after_this, last, first = lax.optimization_barrier(
        (after_this, x_piece(width_x - depth), x_piece(0))
    )
    before = lax.ppermute(last, "tile", up)
    after = lax.ppermute(first, "tile", down)
    return after_this, before, after


def stencil_finish(state_t, diffusivity, before, after, depth):
    width_x, width_y, features = state_t.shape
    x_before = before[:features].transpose(1, 2, 0)
    x_after = after[:features].transpose(1, 2, 0)
    c_rows = jnp.concatenate([before[features], diffusivity, after[features]], axis=0)
    extended = jnp.concatenate([x_before, state_t, x_after], axis=0)

    def y_piece(start):
        rows = lax.slice_in_dim(extended, start, start + depth, axis=1)
        cols = lax.slice_in_dim(c_rows, start, start + depth, axis=1).T
        cols = jnp.pad(cols, ((0, 0), (0, features - cols.shape[1])))
        return jnp.concatenate([rows, cols[None]], axis=0)

    inf_count = lax.axis_size("inf")
    up = [(i, i + 1) for i in range(inf_count - 1)]
    down = [(j, i) for i, j in up]
    before = lax.ppermute(y_piece(width_y - depth), "inf", up)
    after = lax.ppermute(y_piece(0), "inf", down)
    rows_ext = extended.shape[0]
    y_halo = jnp.concatenate([after[:rows_ext], before[:rows_ext]], axis=1)
    c_ext = jnp.concatenate(
        [c_rows, after[rows_ext, :, :rows_ext].T, before[rows_ext, :, :rows_ext].T], axis=1
    )
    ylen = c_ext.shape[1]
    coeff = jnp.broadcast_to(c_ext[:, :, None], (rows_ext, ylen, features))
    return x_before, x_after, y_halo, coeff


def standardize(rows):
    center = jnp.mean(rows, axis=-1, keepdims=True)
    spread = jnp.mean(jnp.square(rows - center), axis=-1, keepdims=True)
    return (rows - center) * lax.rsqrt(spread + 1e-05)


def network_rows(rows, first_layer, second_layer, third_layer, last_layer):
    highest = lax.Precision.HIGH
    hidden = jax.nn.silu(jnp.dot(rows, first_layer, precision=highest))
    hidden = jax.nn.silu(jnp.dot(hidden, second_layer, precision=highest))
    hidden = jax.nn.silu(jnp.dot(hidden, third_layer, precision=highest))
    return jnp.dot(hidden, last_layer, precision=highest)


def gather_kernel(slot_ref, act_ref, u_hbm, v_hbm, st_ref, o_ref, buf, sems):
    levels = u_hbm.shape[0]
    width_x, features, width_y = buf.shape
    chunk = 128

    def copies(x):
        return (
            pltpu.make_async_copy(u_hbm.at[:, x, :], buf.at[x, pl.ds(0, levels), :], sems.at[0, x]),
            pltpu.make_async_copy(v_hbm.at[:, x, :], buf.at[x, pl.ds(levels, levels), :], sems.at[1, x]),
        )

    def start(x, carry):
        for copy in copies(x):
            copy.start()
        return carry

    lax.fori_loop(0, width_x, start, 0)

    def clear(k, carry):
        at = pl.ds(pl.multiple_of(k * chunk, chunk), chunk)
        o_ref[at, :] = jnp.zeros((chunk, features), jnp.float32)
        return carry

    lax.fori_loop(0, o_ref.shape[0] // chunk, clear, 0)

    def transpose_tile(x, carry):
        for copy in copies(x):
            copy.wait()
        st_ref[pl.ds(pl.multiple_of(x * width_y, width_y), width_y), :] = buf[x].T
        return carry

    lax.fori_loop(0, width_x, transpose_tile, 0)

    def place(r, carry):
        o_ref[pl.ds(slot_ref[r], 1), :] = st_ref[pl.ds(act_ref[r], 1), :]
        return carry

    lax.fori_loop(0, act_ref.shape[0], place, 0, unroll=8)


def diffuse_kernel(st_ref, xb_ref, xa_ref, yh_ref, c_ref, f_ref, e_ref, a_ref):
    width_x, width_y, _ = st_ref.shape
    depth = xb_ref.shape[0]
    rows_ext, ylen, _ = c_ref.shape
    e_ref[0:depth, 0:width_y, :] = xb_ref[...]
    e_ref[depth + width_x :, 0:width_y, :] = xa_ref[...]

    def fill(x, carry):
        e_ref[x + depth, 0:width_y, :] = st_ref[x]
        return carry

    lax.fori_loop(0, width_x, fill, 0)
    e_ref[:, width_y:, :] = yh_ref[...]

    def sweep(src, dst, p, last):
        def one(x, carry):
            q = src[x]
            n = src[x + 1] + src[x - 1]
            n = n + pltpu.roll(q, ylen - 1, 0) + pltpu.roll(q, 1, 0)
            new = q + c_ref[x] * (n - 4.0 * q)
            if last:
                f_ref[x - depth] = new[:width_y]
            else:
                dst[x] = new
            return carry

        lax.fori_loop(p + 1, rows_ext - 1 - p, one, 0)

    for p in range(PASSES):
        src, dst = (e_ref, a_ref) if p % 2 == 0 else (a_ref, e_ref)
        sweep(src, dst, p, p == PASSES - 1)


def finish_kernel(slot_ref, act_ref, r_ref, f_ref, uo_hbm, vo_hbm, d_ref, obuf, sems):
    levels = uo_hbm.shape[0]
    width_x, features, width_y = obuf.shape

    def clear(x, carry):
        at = pl.ds(pl.multiple_of(x * width_y, width_y), width_y)
        d_ref[at, :] = jnp.zeros((width_y, features), jnp.float32)
        return carry

    lax.fori_loop(0, width_x, clear, 0)

    def place(r, carry):
        d_ref[pl.ds(act_ref[r], 1), :] = r_ref[pl.ds(slot_ref[r], 1), :]
        return carry

    lax.fori_loop(0, act_ref.shape[0], place, 0, unroll=8)

    def copies(x):
        return (
            pltpu.make_async_copy(obuf.at[x, pl.ds(0, levels), :], uo_hbm.at[:, x, :], sems.at[0, x]),
            pltpu.make_async_copy(obuf.at[x, pl.ds(levels, levels), :], vo_hbm.at[:, x, :], sems.at[1, x]),
        )

    def transpose_tile(x, carry):
        at = pl.ds(pl.multiple_of(x * width_y, width_y), width_y)
        obuf[x] = (f_ref[at, :] + d_ref[at, :]).T
        for copy in copies(x):
            copy.start()
        return carry

    lax.fori_loop(0, width_x, transpose_tile, 0)

    def finish(x, carry):
        for copy in copies(x):
            copy.wait()
        return carry

    lax.fori_loop(0, width_x, finish, 0)


def body(
    u_field,
    v_field,
    diffusivity,
    active_columns,
    regimes,
    first_layer,
    second_layer,
    third_layer,
    last_layer,
):
    levels, width_x, width_y = u_field.shape
    features = 2 * levels
    cells = width_x * width_y
    active_count = active_columns.shape[0]
    devices_all = lax.axis_size(("tile", "inf"))
    capacity = 2 * active_count // devices_all
    slot_total = devices_all * capacity
    block_rows = min(512, active_count)
    block_count = active_count // block_rows
    target = regimes[:, 0]
    labels = jnp.arange(devices_all, dtype=jnp.int32)
    one_hot = (
        (target[:, None] == labels[None, :])
        .astype(jnp.bfloat16)
        .reshape(block_count, block_rows, devices_all)
    )
    row_ids = jnp.arange(block_rows, dtype=jnp.int32)
    lower = (row_ids[:, None] > row_ids[None, :]).astype(jnp.bfloat16)

    def rank_step(counts, piece):
        earlier = jnp.dot(lower, piece, preferred_element_type=jnp.float32) + counts[None, :]
        wide_piece = piece.astype(jnp.float32)
        rank = jnp.sum(earlier * wide_piece, axis=1)
        return (counts + jnp.sum(wide_piece, axis=0), rank)

    _, ranks = lax.scan(rank_step, jnp.zeros((devices_all,), jnp.float32), one_hot)
    tile_count, inf_count = lax.axis_size("tile"), lax.axis_size("inf")
    half_tiles = tile_count // 2
    my_half = lax.axis_index("tile") // half_tiles
    target_tile = target // inf_count
    place = (target_tile % half_tiles) * inf_count + target % inf_count
    kind = (target_tile // half_tiles != my_half).astype(jnp.int32)
    pair_slots = 2 * capacity
    slot_index = place * pair_slots + kind * capacity + ranks.reshape(-1).astype(jnp.int32)
    groups = [
        [t * inf_count + i for t in range(h * half_tiles, (h + 1) * half_tiles) for i in range(inf_count)]
        for h in range(2)
    ]
    group_size = half_tiles * inf_count
    swap = [(t, (t + half_tiles) % tile_count) for t in range(tile_count)]
    mirrored = [
        lax.ppermute(w[0], "tile", swap) for w in (first_layer, second_layer, third_layer, last_layer)
    ]
    vmem = pl.BlockSpec(memory_space=pltpu.VMEM)
    smem = pl.BlockSpec(memory_space=pltpu.SMEM)
    hbm = pl.BlockSpec(memory_space=pl.ANY)
    state_t, outgoing = pl.pallas_call(
        gather_kernel,
        out_shape=(
            jax.ShapeDtypeStruct((cells, features), jnp.float32),
            jax.ShapeDtypeStruct((slot_total, features), jnp.float32),
        ),
        in_specs=[smem, smem, hbm, hbm],
        out_specs=(vmem, vmem),
        scratch_shapes=[
            pltpu.VMEM((width_x, features, width_y), jnp.float32),
            pltpu.SemaphoreType.DMA((2, width_x)),
        ],
    )(slot_index, active_columns, u_field, v_field)
    state_t = state_t.reshape(width_x, width_y, features)
    outgoing, x_from_before, x_from_after = stencil_start(
        u_field, v_field, diffusivity, PASSES, outgoing
    )
    block = lax.all_to_all(
        outgoing.reshape(group_size, pair_slots, features),
        ("tile", "inf"),
        split_axis=0,
        concat_axis=0,
        tiled=True,
        axis_index_groups=groups,
    )
    block_shape = block.shape
    x_before, x_after, y_halo, coeff = stencil_finish(
        state_t, diffusivity, x_from_before, x_from_after, PASSES
    )
    block, x_before, x_after, y_halo = lax.optimization_barrier(
        (block, x_before, x_after, y_halo)
    )
    own_rows = standardize(block[:, :capacity].reshape(-1, features))
    own = network_rows(own_rows, first_layer[0], second_layer[0], third_layer[0], last_layer[0])
    other_rows = standardize(block[:, capacity:].reshape(-1, features))
    other = network_rows(other_rows, *mirrored)
    answered = jnp.concatenate(
        [own.reshape(group_size, capacity, features), other.reshape(group_size, capacity, features)],
        axis=1,
    )
    returned = lax.all_to_all(
        answered,
        ("tile", "inf"),
        split_axis=0,
        concat_axis=0,
        tiled=True,
        axis_index_groups=groups,
    )
    returned_rows = returned.reshape(slot_total, features)

    rows_ext, ylen = coeff.shape[:2]
    diffused = pl.pallas_call(
        diffuse_kernel,
        out_shape=jax.ShapeDtypeStruct((width_x, width_y, features), jnp.float32),
        in_specs=[vmem] * 5,
        out_specs=vmem,
        scratch_shapes=[
            pltpu.VMEM((rows_ext, ylen, features), jnp.float32),
            pltpu.VMEM((rows_ext, ylen, features), jnp.float32),
        ],
        compiler_params=pltpu.CompilerParams(vmem_limit_bytes=100 * 1024 * 1024),
    )(state_t, x_before, x_after, y_halo, coeff)
    u_next, v_next = pl.pallas_call(
        finish_kernel,
        out_shape=(
            jax.ShapeDtypeStruct(u_field.shape, jnp.float32),
            jax.ShapeDtypeStruct(v_field.shape, jnp.float32),
        ),
        in_specs=[smem, smem, vmem, vmem],
        out_specs=(hbm, hbm),
        scratch_shapes=[
            pltpu.VMEM((cells, features), jnp.float32),
            pltpu.VMEM((width_x, features, width_y), jnp.float32),
            pltpu.SemaphoreType.DMA((2, width_x)),
        ],
    )(slot_index, active_columns, returned_rows, diffused.reshape(cells, features))
    return (u_next, v_next)


def solution(mesh):
    in_specs = (
        P(None, "tile", "inf"),
        P(None, "tile", "inf"),
        P("tile", "inf"),
        P(("tile", "inf")),
        P(("tile", "inf"), None),
        P(("tile", "inf"), None, None),
        P(("tile", "inf"), None, None),
        P(("tile", "inf"), None, None),
        P(("tile", "inf"), None, None),
    )
    out_specs = (P(None, "tile", "inf"), P(None, "tile", "inf"))
    return jax.shard_map(body, mesh=mesh, in_specs=in_specs, out_specs=out_specs, check_vma=False)
```

```python
import jax
import jax.numpy as jnp
from jax import lax
from jax.experimental import pallas as pl
from jax.experimental.pallas import tpu as pltpu
from jax.sharding import PartitionSpec as P

PASSES = 4


def halos(x, axis, dim, width):
    count, length = (lax.axis_size(axis), x.shape[dim])
    up = [(i, i + 1) for i in range(count - 1)]
    down = [(j, i) for i, j in up]
    last = lax.slice_in_dim(x, length - width, length, axis=dim)
    first = lax.slice_in_dim(x, 0, width, axis=dim)
    before = lax.ppermute(last, axis, up)
    after = lax.ppermute(first, axis, down)
    return before, after


def stencil_start(u_field, v_field, diffusivity, depth):
    width_x = u_field.shape[1]

    def x_piece(start):
        rows = lambda a: lax.slice_in_dim(a, start, start + depth, axis=a.ndim - 2)
        return jnp.concatenate([rows(u_field), rows(v_field), rows(diffusivity)[None]], axis=0)

    tile_count = lax.axis_size("tile")
    up = [(i, i + 1) for i in range(tile_count - 1)]
    down = [(j, i) for i, j in up]
    before = lax.ppermute(x_piece(width_x - depth), "tile", up)
    after = lax.ppermute(x_piece(0), "tile", down)
    return before, after


def stencil_finish(state_t, diffusivity, before, after, depth):
    width_x, width_y, features = state_t.shape
    x_before = before[:features].transpose(1, 2, 0)
    x_after = after[:features].transpose(1, 2, 0)
    c_rows = jnp.concatenate([before[features], diffusivity, after[features]], axis=0)
    extended = jnp.concatenate([x_before, state_t, x_after], axis=0)

    def y_piece(start):
        rows = lax.slice_in_dim(extended, start, start + depth, axis=1)
        cols = lax.slice_in_dim(c_rows, start, start + depth, axis=1).T
        cols = jnp.pad(cols, ((0, 0), (0, features - cols.shape[1])))
        return jnp.concatenate([rows, cols[None]], axis=0)

    inf_count = lax.axis_size("inf")
    up = [(i, i + 1) for i in range(inf_count - 1)]
    down = [(j, i) for i, j in up]
    before = lax.ppermute(y_piece(width_y - depth), "inf", up)
    after = lax.ppermute(y_piece(0), "inf", down)
    rows_ext = extended.shape[0]
    y_halo = jnp.concatenate([after[:rows_ext], before[:rows_ext]], axis=1)
    c_ext = jnp.concatenate(
        [c_rows, after[rows_ext, :, :rows_ext].T, before[rows_ext, :, :rows_ext].T], axis=1
    )
    ylen = c_ext.shape[1]
    coeff = jnp.broadcast_to(c_ext[:, :, None], (rows_ext, ylen, features))
    return x_before, x_after, y_halo, coeff


def standardize(rows):
    center = jnp.mean(rows, axis=-1, keepdims=True)
    spread = jnp.mean(jnp.square(rows - center), axis=-1, keepdims=True)
    return (rows - center) * lax.rsqrt(spread + 1e-05)


def network_rows(rows, first_layer, second_layer, third_layer, last_layer):
    highest = lax.Precision.HIGH
    hidden = jax.nn.silu(jnp.dot(rows, first_layer, precision=highest))
    hidden = jax.nn.silu(jnp.dot(hidden, second_layer, precision=highest))
    hidden = jax.nn.silu(jnp.dot(hidden, third_layer, precision=highest))
    return jnp.dot(hidden, last_layer, precision=highest)


def gather_kernel(slot_ref, act_ref, u_hbm, v_hbm, st_hbm, o_ref, buf, st_ref, sems, st_sems):
    levels = u_hbm.shape[0]
    width_x, features, width_y = buf.shape
    chunk = 128

    def copies(x):
        return (
            pltpu.make_async_copy(u_hbm.at[:, x, :], buf.at[x, pl.ds(0, levels), :], sems.at[0, x]),
            pltpu.make_async_copy(v_hbm.at[:, x, :], buf.at[x, pl.ds(levels, levels), :], sems.at[1, x]),
        )

    def start(x, carry):
        for copy in copies(x):
            copy.start()
        return carry

    lax.fori_loop(0, width_x, start, 0)

    def clear(k, carry):
        at = pl.ds(pl.multiple_of(k * chunk, chunk), chunk)
        o_ref[at, :] = jnp.zeros((chunk, features), jnp.float32)
        return carry

    lax.fori_loop(0, o_ref.shape[0] // chunk, clear, 0)

    def write_back(x):
        at = pl.ds(pl.multiple_of(x * width_y, width_y), width_y)
        return pltpu.make_async_copy(st_ref.at[at, :], st_hbm.at[at, :], st_sems.at[x])

    def transpose_tile(x, carry):
        for copy in copies(x):
            copy.wait()
        st_ref[pl.ds(pl.multiple_of(x * width_y, width_y), width_y), :] = buf[x].T
        write_back(x).start()
        return carry

    lax.fori_loop(0, width_x, transpose_tile, 0)

    def place(r, carry):
        o_ref[pl.ds(slot_ref[r], 1), :] = st_ref[pl.ds(act_ref[r], 1), :]
        return carry

    lax.fori_loop(0, act_ref.shape[0], place, 0, unroll=8)

    def settle(x, carry):
        write_back(x).wait()
        return carry

    lax.fori_loop(0, width_x, settle, 0)


def diffuse_kernel(st_ref, xb_ref, xa_ref, yh_ref, c_ref, f_ref, e_ref, a_ref):
    width_x, width_y, _ = st_ref.shape
    depth = xb_ref.shape[0]
    rows_ext, ylen, _ = c_ref.shape
    e_ref[0:depth, 0:width_y, :] = xb_ref[...]
    e_ref[depth + width_x :, 0:width_y, :] = xa_ref[...]

    def fill(x, carry):
        e_ref[x + depth, 0:width_y, :] = st_ref[x]
        return carry

    lax.fori_loop(0, width_x, fill, 0)
    e_ref[:, width_y:, :] = yh_ref[...]

    def sweep(src, dst, p, last):
        def one(x, carry):
            q = src[x]
            n = src[x + 1] + src[x - 1]
            n = n + pltpu.roll(q, ylen - 1, 0) + pltpu.roll(q, 1, 0)
            new = q + c_ref[x] * (n - 4.0 * q)
            if last:
                f_ref[x - depth] = new[:width_y]
            else:
                dst[x] = new
            return carry

        lax.fori_loop(p + 1, rows_ext - 1 - p, one, 0)

    for p in range(PASSES):
        src, dst = (e_ref, a_ref) if p % 2 == 0 else (a_ref, e_ref)
        sweep(src, dst, p, p == PASSES - 1)


def finish_kernel(slot_ref, act_ref, r_ref, f_hbm, uo_hbm, vo_hbm, d_ref, obuf, f_ref, sems, f_sems):
    levels = uo_hbm.shape[0]
    width_x, features, width_y = obuf.shape

    def fetch(x):
        at = pl.ds(pl.multiple_of(x * width_y, width_y), width_y)
        return pltpu.make_async_copy(f_hbm.at[at, :], f_ref.at[at, :], f_sems.at[x])

    def begin(x, carry):
        fetch(x).start()
        return carry

    lax.fori_loop(0, width_x, begin, 0)

    def clear(x, carry):
        at = pl.ds(pl.multiple_of(x * width_y, width_y), width_y)
        d_ref[at, :] = jnp.zeros((width_y, features), jnp.float32)
        return carry

    lax.fori_loop(0, width_x, clear, 0)

    def place(r, carry):
        d_ref[pl.ds(act_ref[r], 1), :] = r_ref[pl.ds(slot_ref[r], 1), :]
        return carry

    lax.fori_loop(0, act_ref.shape[0], place, 0, unroll=8)

    def copies(x):
        return (
            pltpu.make_async_copy(obuf.at[x, pl.ds(0, levels), :], uo_hbm.at[:, x, :], sems.at[0, x]),
            pltpu.make_async_copy(obuf.at[x, pl.ds(levels, levels), :], vo_hbm.at[:, x, :], sems.at[1, x]),
        )

    def transpose_tile(x, carry):
        at = pl.ds(pl.multiple_of(x * width_y, width_y), width_y)
        fetch(x).wait()
        obuf[x] = (f_ref[at, :] + d_ref[at, :]).T
        for copy in copies(x):
            copy.start()
        return carry

    lax.fori_loop(0, width_x, transpose_tile, 0)

    def finish(x, carry):
        for copy in copies(x):
            copy.wait()
        return carry

    lax.fori_loop(0, width_x, finish, 0)


def body(
    u_field,
    v_field,
    diffusivity,
    active_columns,
    regimes,
    first_layer,
    second_layer,
    third_layer,
    last_layer,
):
    levels, width_x, width_y = u_field.shape
    features = 2 * levels
    cells = width_x * width_y
    active_count = active_columns.shape[0]
    devices_all = lax.axis_size(("tile", "inf"))
    capacity = 2 * active_count // devices_all
    slot_total = devices_all * capacity
    block_rows = min(512, active_count)
    block_count = active_count // block_rows
    target = regimes[:, 0]
    labels = jnp.arange(devices_all, dtype=jnp.int32)
    one_hot = (
        (target[:, None] == labels[None, :])
        .astype(jnp.bfloat16)
        .reshape(block_count, block_rows, devices_all)
    )
    row_ids = jnp.arange(block_rows, dtype=jnp.int32)
    lower = (row_ids[:, None] > row_ids[None, :]).astype(jnp.bfloat16)

    def rank_step(counts, piece):
        earlier = jnp.dot(lower, piece, preferred_element_type=jnp.float32) + counts[None, :]
        wide_piece = piece.astype(jnp.float32)
        rank = jnp.sum(earlier * wide_piece, axis=1)
        return (counts + jnp.sum(wide_piece, axis=0), rank)

    _, ranks = lax.scan(rank_step, jnp.zeros((devices_all,), jnp.float32), one_hot)
    tile_count, inf_count = lax.axis_size("tile"), lax.axis_size("inf")
    half_tiles = tile_count // 2
    my_half = lax.axis_index("tile") // half_tiles
    target_tile = target // inf_count
    place = (target_tile % half_tiles) * inf_count + target % inf_count
    kind = (target_tile // half_tiles != my_half).astype(jnp.int32)
    pair_slots = 2 * capacity
    slot_index = place * pair_slots + kind * capacity + ranks.reshape(-1).astype(jnp.int32)
    groups = [
        [t * inf_count + i for t in range(h * half_tiles, (h + 1) * half_tiles) for i in range(inf_count)]
        for h in range(2)
    ]
    group_size = half_tiles * inf_count
    swap = [(t, (t + half_tiles) % tile_count) for t in range(tile_count)]
    mirrored = [
        lax.ppermute(w[0], "tile", swap) for w in (first_layer, second_layer, third_layer, last_layer)
    ]
    vmem = pl.BlockSpec(memory_space=pltpu.VMEM)
    smem = pl.BlockSpec(memory_space=pltpu.SMEM)
    x_from_before, x_from_after = stencil_start(u_field, v_field, diffusivity, PASSES)
    hbm = pl.BlockSpec(memory_space=pl.ANY)
    state_t, outgoing = pl.pallas_call(
        gather_kernel,
        out_shape=(
            jax.ShapeDtypeStruct((cells, features), jnp.float32),
            jax.ShapeDtypeStruct((slot_total, features), jnp.float32),
        ),
        in_specs=[smem, smem, hbm, hbm],
        out_specs=(hbm, vmem),
        scratch_shapes=[
            pltpu.VMEM((width_x, features, width_y), jnp.float32),
            pltpu.VMEM((cells, features), jnp.float32),
            pltpu.SemaphoreType.DMA((2, width_x)),
            pltpu.SemaphoreType.DMA((width_x,)),
        ],
    )(slot_index, active_columns, u_field, v_field)
    state_t = state_t.reshape(width_x, width_y, features)
    outgoing, x_from_before, x_from_after = lax.optimization_barrier(
        (outgoing, x_from_before, x_from_after)
    )
    block = lax.all_to_all(
        outgoing.reshape(group_size, pair_slots, features),
        ("tile", "inf"),
        split_axis=0,
        concat_axis=0,
        tiled=True,
        axis_index_groups=groups,
    )
    block_shape = block.shape
    x_before, x_after, y_halo, coeff = stencil_finish(
        state_t, diffusivity, x_from_before, x_from_after, PASSES
    )
    block, x_before, x_after, y_halo = lax.optimization_barrier(
        (block, x_before, x_after, y_halo)
    )
    own_rows = standardize(block[:, :capacity].reshape(-1, features))
    own = network_rows(own_rows, first_layer[0], second_layer[0], third_layer[0], last_layer[0])
    other_rows = standardize(block[:, capacity:].reshape(-1, features))
    other = network_rows(other_rows, *mirrored)
    answered = jnp.concatenate(
        [own.reshape(group_size, capacity, features), other.reshape(group_size, capacity, features)],
        axis=1,
    )
    returned = lax.all_to_all(
        answered,
        ("tile", "inf"),
        split_axis=0,
        concat_axis=0,
        tiled=True,
        axis_index_groups=groups,
    )
    returned_rows = returned.reshape(slot_total, features)

    rows_ext, ylen = coeff.shape[:2]
    diffused = pl.pallas_call(
        diffuse_kernel,
        out_shape=jax.ShapeDtypeStruct((width_x, width_y, features), jnp.float32),
        in_specs=[vmem] * 5,
        out_specs=vmem,
        scratch_shapes=[
            pltpu.VMEM((rows_ext, ylen, features), jnp.float32),
            pltpu.VMEM((rows_ext, ylen, features), jnp.float32),
        ],
        compiler_params=pltpu.CompilerParams(vmem_limit_bytes=100 * 1024 * 1024),
    )(state_t, x_before, x_after, y_halo, coeff)
    u_next, v_next = pl.pallas_call(
        finish_kernel,
        out_shape=(
            jax.ShapeDtypeStruct(u_field.shape, jnp.float32),
            jax.ShapeDtypeStruct(v_field.shape, jnp.float32),
        ),
        in_specs=[smem, smem, vmem, hbm],
        out_specs=(hbm, hbm),
        scratch_shapes=[
            pltpu.VMEM((cells, features), jnp.float32),
            pltpu.VMEM((width_x, features, width_y), jnp.float32),
            pltpu.VMEM((cells, features), jnp.float32),
            pltpu.SemaphoreType.DMA((2, width_x)),
            pltpu.SemaphoreType.DMA((width_x,)),
        ],
    )(slot_index, active_columns, returned_rows, diffused.reshape(cells, features))
    return (u_next, v_next)


def solution(mesh):
    in_specs = (
        P(None, "tile", "inf"),
        P(None, "tile", "inf"),
        P("tile", "inf"),
        P(("tile", "inf")),
        P(("tile", "inf"), None),
        P(("tile", "inf"), None, None),
        P(("tile", "inf"), None, None),
        P(("tile", "inf"), None, None),
        P(("tile", "inf"), None, None),
    )
    out_specs = (P(None, "tile", "inf"), P(None, "tile", "inf"))
    return jax.shard_map(body, mesh=mesh, in_specs=in_specs, out_specs=out_specs, check_vma=False)
```

```python
import jax
import jax.numpy as jnp
from jax import lax
from jax.experimental import pallas as pl
from jax.experimental.pallas import tpu as pltpu
from jax.sharding import PartitionSpec as P

PASSES = 4


def halos(x, axis, dim, width):
    count, length = (lax.axis_size(axis), x.shape[dim])
    up = [(i, i + 1) for i in range(count - 1)]
    down = [(j, i) for i, j in up]
    last = lax.slice_in_dim(x, length - width, length, axis=dim)
    first = lax.slice_in_dim(x, 0, width, axis=dim)
    before = lax.ppermute(last, axis, up)
    after = lax.ppermute(first, axis, down)
    return before, after


def stencil_start(u_field, v_field, diffusivity, depth):
    width_x = u_field.shape[1]

    def x_piece(start):
        rows = lambda a: lax.slice_in_dim(a, start, start + depth, axis=a.ndim - 2)
        return jnp.concatenate([rows(u_field), rows(v_field), rows(diffusivity)[None]], axis=0)

    tile_count = lax.axis_size("tile")
    up = [(i, i + 1) for i in range(tile_count - 1)]
    down = [(j, i) for i, j in up]
    before = lax.ppermute(x_piece(width_x - depth), "tile", up)
    after = lax.ppermute(x_piece(0), "tile", down)
    return before, after


def stencil_finish(state_t, diffusivity, before, after, depth):
    width_x, width_y, features = state_t.shape
    x_before = before[:features].transpose(1, 2, 0)
    x_after = after[:features].transpose(1, 2, 0)
    c_rows = jnp.concatenate([before[features], diffusivity, after[features]], axis=0)
    extended = jnp.concatenate([x_before, state_t, x_after], axis=0)

    def y_piece(start):
        rows = lax.slice_in_dim(extended, start, start + depth, axis=1)
        cols = lax.slice_in_dim(c_rows, start, start + depth, axis=1).T
        cols = jnp.pad(cols, ((0, 0), (0, features - cols.shape[1])))
        return jnp.concatenate([rows, cols[None]], axis=0)

    inf_count = lax.axis_size("inf")
    up = [(i, i + 1) for i in range(inf_count - 1)]
    down = [(j, i) for i, j in up]
    before = lax.ppermute(y_piece(width_y - depth), "inf", up)
    after = lax.ppermute(y_piece(0), "inf", down)
    rows_ext = extended.shape[0]
    y_halo = jnp.concatenate([after[:rows_ext], before[:rows_ext]], axis=1)
    c_ext = jnp.concatenate(
        [c_rows, after[rows_ext, :, :rows_ext].T, before[rows_ext, :, :rows_ext].T], axis=1
    )
    ylen = c_ext.shape[1]
    coeff = jnp.broadcast_to(c_ext[:, :, None], (rows_ext, ylen, features))
    return x_before, x_after, y_halo, coeff


def standardize(rows):
    center = jnp.mean(rows, axis=-1, keepdims=True)
    spread = jnp.mean(jnp.square(rows - center), axis=-1, keepdims=True)
    return (rows - center) * lax.rsqrt(spread + 1e-05)


def network_rows(rows, first_layer, second_layer, third_layer, last_layer):
    highest = lax.Precision.HIGH
    hidden = jax.nn.silu(jnp.dot(rows, first_layer, precision=highest))
    hidden = jax.nn.silu(jnp.dot(hidden, second_layer, precision=highest))
    hidden = jax.nn.silu(jnp.dot(hidden, third_layer, precision=highest))
    return jnp.dot(hidden, last_layer, precision=highest)


def gather_kernel(slot_ref, act_ref, u_hbm, v_hbm, st_ref, o_ref, buf, sems):
    levels = u_hbm.shape[0]
    width_x, features, width_y = buf.shape
    chunk = 128

    def copies(x):
        return (
            pltpu.make_async_copy(u_hbm.at[:, x, :], buf.at[x, pl.ds(0, levels), :], sems.at[0, x]),
            pltpu.make_async_copy(v_hbm.at[:, x, :], buf.at[x, pl.ds(levels, levels), :], sems.at[1, x]),
        )

    def start(x, carry):
        for copy in copies(x):
            copy.start()
        return carry

    lax.fori_loop(0, width_x, start, 0)

    def clear(k, carry):
        at = pl.ds(pl.multiple_of(k * chunk, chunk), chunk)
        o_ref[at, :] = jnp.zeros((chunk, features), jnp.float32)
        return carry

    lax.fori_loop(0, o_ref.shape[0] // chunk, clear, 0)

    def transpose_tile(x, carry):
        for copy in copies(x):
            copy.wait()
        st_ref[pl.ds(pl.multiple_of(x * width_y, width_y), width_y), :] = buf[x].T
        return carry

    lax.fori_loop(0, width_x, transpose_tile, 0)

    def place(r, carry):
        o_ref[pl.ds(slot_ref[r], 1), :] = st_ref[pl.ds(act_ref[r], 1), :]
        return carry

    lax.fori_loop(0, act_ref.shape[0], place, 0, unroll=32)


def diffuse_kernel(st_ref, xb_ref, xa_ref, yh_ref, c_ref, f_ref, e_ref, a_ref):
    width_x, width_y, _ = st_ref.shape
    depth = xb_ref.shape[0]
    rows_ext, ylen, _ = c_ref.shape
    e_ref[0:depth, 0:width_y, :] = xb_ref[...]
    e_ref[depth + width_x :, 0:width_y, :] = xa_ref[...]

    def fill(x, carry):
        e_ref[x + depth, 0:width_y, :] = st_ref[x]
        return carry

    lax.fori_loop(0, width_x, fill, 0)
    e_ref[:, width_y:, :] = yh_ref[...]

    def sweep(src, dst, p, last):
        def one(x, carry):
            q = src[x]
            n = src[x + 1] + src[x - 1]
            n = n + pltpu.roll(q, ylen - 1, 0) + pltpu.roll(q, 1, 0)
            new = q + c_ref[x] * (n - 4.0 * q)
            if last:
                f_ref[x - depth] = new[:width_y]
            else:
                dst[x] = new
            return carry

        lax.fori_loop(p + 1, rows_ext - 1 - p, one, 0)

    for p in range(PASSES):
        src, dst = (e_ref, a_ref) if p % 2 == 0 else (a_ref, e_ref)
        sweep(src, dst, p, p == PASSES - 1)


def finish_kernel(slot_ref, act_ref, r_ref, f_ref, uo_hbm, vo_hbm, d_ref, obuf, sems):
    levels = uo_hbm.shape[0]
    width_x, features, width_y = obuf.shape

    def clear(x, carry):
        at = pl.ds(pl.multiple_of(x * width_y, width_y), width_y)
        d_ref[at, :] = jnp.zeros((width_y, features), jnp.float32)
        return carry

    lax.fori_loop(0, width_x, clear, 0)

    def place(r, carry):
        d_ref[pl.ds(act_ref[r], 1), :] = r_ref[pl.ds(slot_ref[r], 1), :]
        return carry

    lax.fori_loop(0, act_ref.shape[0], place, 0, unroll=32)

    def copies(x):
        return (
            pltpu.make_async_copy(obuf.at[x, pl.ds(0, levels), :], uo_hbm.at[:, x, :], sems.at[0, x]),
            pltpu.make_async_copy(obuf.at[x, pl.ds(levels, levels), :], vo_hbm.at[:, x, :], sems.at[1, x]),
        )

    def transpose_tile(x, carry):
        at = pl.ds(pl.multiple_of(x * width_y, width_y), width_y)
        obuf[x] = (f_ref[at, :] + d_ref[at, :]).T
        for copy in copies(x):
            copy.start()
        return carry

    lax.fori_loop(0, width_x, transpose_tile, 0)

    def finish(x, carry):
        for copy in copies(x):
            copy.wait()
        return carry

    lax.fori_loop(0, width_x, finish, 0)


def body(
    u_field,
    v_field,
    diffusivity,
    active_columns,
    regimes,
    first_layer,
    second_layer,
    third_layer,
    last_layer,
):
    levels, width_x, width_y = u_field.shape
    features = 2 * levels
    cells = width_x * width_y
    active_count = active_columns.shape[0]
    devices_all = lax.axis_size(("tile", "inf"))
    capacity = 2 * active_count // devices_all
    slot_total = devices_all * capacity
    block_rows = min(512, active_count)
    block_count = active_count // block_rows
    target = regimes[:, 0]
    labels = jnp.arange(devices_all, dtype=jnp.int32)
    one_hot = (
        (target[:, None] == labels[None, :])
        .astype(jnp.bfloat16)
        .reshape(block_count, block_rows, devices_all)
    )
    row_ids = jnp.arange(block_rows, dtype=jnp.int32)
    lower = (row_ids[:, None] > row_ids[None, :]).astype(jnp.bfloat16)

    def rank_step(counts, piece):
        earlier = jnp.dot(lower, piece, preferred_element_type=jnp.float32) + counts[None, :]
        wide_piece = piece.astype(jnp.float32)
        rank = jnp.sum(earlier * wide_piece, axis=1)
        return (counts + jnp.sum(wide_piece, axis=0), rank)

    _, ranks = lax.scan(rank_step, jnp.zeros((devices_all,), jnp.float32), one_hot)
    tile_count, inf_count = lax.axis_size("tile"), lax.axis_size("inf")
    half_tiles = tile_count // 2
    my_half = lax.axis_index("tile") // half_tiles
    target_tile = target // inf_count
    place = (target_tile % half_tiles) * inf_count + target % inf_count
    kind = (target_tile // half_tiles != my_half).astype(jnp.int32)
    pair_slots = 2 * capacity
    slot_index = place * pair_slots + kind * capacity + ranks.reshape(-1).astype(jnp.int32)
    groups = [
        [t * inf_count + i for t in range(h * half_tiles, (h + 1) * half_tiles) for i in range(inf_count)]
        for h in range(2)
    ]
    group_size = half_tiles * inf_count
    swap = [(t, (t + half_tiles) % tile_count) for t in range(tile_count)]
    mirrored = [
        lax.ppermute(w[0], "tile", swap) for w in (first_layer, second_layer, third_layer, last_layer)
    ]
    vmem = pl.BlockSpec(memory_space=pltpu.VMEM)
    smem = pl.BlockSpec(memory_space=pltpu.SMEM)
    x_from_before, x_from_after = stencil_start(u_field, v_field, diffusivity, PASSES)
    hbm = pl.BlockSpec(memory_space=pl.ANY)
    state_t, outgoing = pl.pallas_call(
        gather_kernel,
        out_shape=(
            jax.ShapeDtypeStruct((cells, features), jnp.float32),
            jax.ShapeDtypeStruct((slot_total, features), jnp.float32),
        ),
        in_specs=[smem, smem, hbm, hbm],
        out_specs=(vmem, vmem),
        scratch_shapes=[
            pltpu.VMEM((width_x, features, width_y), jnp.float32),
            pltpu.SemaphoreType.DMA((2, width_x)),
        ],
    )(slot_index, active_columns, u_field, v_field)
    state_t = state_t.reshape(width_x, width_y, features)
    outgoing, x_from_before, x_from_after = lax.optimization_barrier(
        (outgoing, x_from_before, x_from_after)
    )
    block = lax.all_to_all(
        outgoing.reshape(group_size, pair_slots, features),
        ("tile", "inf"),
        split_axis=0,
        concat_axis=0,
        tiled=True,
        axis_index_groups=groups,
    )
    block_shape = block.shape
    x_before, x_after, y_halo, coeff = stencil_finish(
        state_t, diffusivity, x_from_before, x_from_after, PASSES
    )
    block, x_before, x_after, y_halo = lax.optimization_barrier(
        (block, x_before, x_after, y_halo)
    )
    own_rows = standardize(block[:, :capacity].reshape(-1, features))
    own = network_rows(own_rows, first_layer[0], second_layer[0], third_layer[0], last_layer[0])
    other_rows = standardize(block[:, capacity:].reshape(-1, features))
    other = network_rows(other_rows, *mirrored)
    answered = jnp.concatenate(
        [own.reshape(group_size, capacity, features), other.reshape(group_size, capacity, features)],
        axis=1,
    )
    returned = lax.all_to_all(
        answered,
        ("tile", "inf"),
        split_axis=0,
        concat_axis=0,
        tiled=True,
        axis_index_groups=groups,
    )
    returned_rows = returned.reshape(slot_total, features)

    rows_ext, ylen = coeff.shape[:2]
    diffused = pl.pallas_call(
        diffuse_kernel,
        out_shape=jax.ShapeDtypeStruct((width_x, width_y, features), jnp.float32),
        in_specs=[vmem] * 5,
        out_specs=vmem,
        scratch_shapes=[
            pltpu.VMEM((rows_ext, ylen, features), jnp.float32),
            pltpu.VMEM((rows_ext, ylen, features), jnp.float32),
        ],
        compiler_params=pltpu.CompilerParams(vmem_limit_bytes=100 * 1024 * 1024),
    )(state_t, x_before, x_after, y_halo, coeff)
    u_next, v_next = pl.pallas_call(
        finish_kernel,
        out_shape=(
            jax.ShapeDtypeStruct(u_field.shape, jnp.float32),
            jax.ShapeDtypeStruct(v_field.shape, jnp.float32),
        ),
        in_specs=[smem, smem, vmem, vmem],
        out_specs=(hbm, hbm),
        scratch_shapes=[
            pltpu.VMEM((cells, features), jnp.float32),
            pltpu.VMEM((width_x, features, width_y), jnp.float32),
            pltpu.SemaphoreType.DMA((2, width_x)),
        ],
    )(slot_index, active_columns, returned_rows, diffused.reshape(cells, features))
    return (u_next, v_next)


def solution(mesh):
    in_specs = (
        P(None, "tile", "inf"),
        P(None, "tile", "inf"),
        P("tile", "inf"),
        P(("tile", "inf")),
        P(("tile", "inf"), None),
        P(("tile", "inf"), None, None),
        P(("tile", "inf"), None, None),
        P(("tile", "inf"), None, None),
        P(("tile", "inf"), None, None),
    )
    out_specs = (P(None, "tile", "inf"), P(None, "tile", "inf"))
    return jax.shard_map(body, mesh=mesh, in_specs=in_specs, out_specs=out_specs, check_vma=False)
```

```python
import jax
import jax.numpy as jnp
from jax import lax
from jax.experimental import pallas as pl
from jax.experimental.pallas import tpu as pltpu
from jax.sharding import PartitionSpec as P

PASSES = 4


def halos(x, axis, dim, width):
    count, length = (lax.axis_size(axis), x.shape[dim])
    up = [(i, i + 1) for i in range(count - 1)]
    down = [(j, i) for i, j in up]
    last = lax.slice_in_dim(x, length - width, length, axis=dim)
    first = lax.slice_in_dim(x, 0, width, axis=dim)
    before = lax.ppermute(last, axis, up)
    after = lax.ppermute(first, axis, down)
    return before, after


def stencil_start(u_field, v_field, diffusivity, depth):
    width_x = u_field.shape[1]

    def x_piece(start):
        rows = lambda a: lax.slice_in_dim(a, start, start + depth, axis=a.ndim - 2)
        return jnp.concatenate([rows(u_field), rows(v_field), rows(diffusivity)[None]], axis=0)

    tile_count = lax.axis_size("tile")
    up = [(i, i + 1) for i in range(tile_count - 1)]
    down = [(j, i) for i, j in up]
    before = lax.ppermute(x_piece(width_x - depth), "tile", up)
    after = lax.ppermute(x_piece(0), "tile", down)
    return before, after


def stencil_finish(state_t, diffusivity, before, after, depth):
    width_x, width_y, features = state_t.shape
    x_before = before[:features].transpose(1, 2, 0)
    x_after = after[:features].transpose(1, 2, 0)
    c_rows = jnp.concatenate([before[features], diffusivity, after[features]], axis=0)
    extended = jnp.concatenate([x_before, state_t, x_after], axis=0)

    def y_piece(start):
        rows = lax.slice_in_dim(extended, start, start + depth, axis=1)
        cols = lax.slice_in_dim(c_rows, start, start + depth, axis=1).T
        cols = jnp.pad(cols, ((0, 0), (0, features - cols.shape[1])))
        return jnp.concatenate([rows, cols[None]], axis=0)

    inf_count = lax.axis_size("inf")
    up = [(i, i + 1) for i in range(inf_count - 1)]
    down = [(j, i) for i, j in up]
    before = lax.ppermute(y_piece(width_y - depth), "inf", up)
    after = lax.ppermute(y_piece(0), "inf", down)
    rows_ext = extended.shape[0]
    y_halo = jnp.concatenate([after[:rows_ext], before[:rows_ext]], axis=1)
    c_ext = jnp.concatenate(
        [c_rows, after[rows_ext, :, :rows_ext].T, before[rows_ext, :, :rows_ext].T], axis=1
    )
    ylen = c_ext.shape[1]
    coeff = jnp.broadcast_to(c_ext[:, :, None], (rows_ext, ylen, features))
    return x_before, x_after, y_halo, coeff


def standardize(rows):
    center = jnp.mean(rows, axis=-1, keepdims=True)
    spread = jnp.mean(jnp.square(rows - center), axis=-1, keepdims=True)
    return (rows - center) * lax.rsqrt(spread + 1e-05)


def network_rows(rows, first_layer, second_layer, third_layer, last_layer):
    highest = lax.Precision.HIGH
    hidden = jax.nn.silu(jnp.dot(rows, first_layer, precision=highest))
    hidden = jax.nn.silu(jnp.dot(hidden, second_layer, precision=highest))
    hidden = jax.nn.silu(jnp.dot(hidden, third_layer, precision=highest))
    return jnp.dot(hidden, last_layer, precision=highest)


def gather_kernel(slot_ref, act_ref, u_hbm, v_hbm, st_ref, o_ref, buf, sems):
    levels = u_hbm.shape[0]
    width_x, features, width_y = buf.shape
    chunk = 128

    def copies(x):
        return (
            pltpu.make_async_copy(u_hbm.at[:, x, :], buf.at[x, pl.ds(0, levels), :], sems.at[0, x]),
            pltpu.make_async_copy(v_hbm.at[:, x, :], buf.at[x, pl.ds(levels, levels), :], sems.at[1, x]),
        )

    def start(x, carry):
        for copy in copies(x):
            copy.start()
        return carry

    lax.fori_loop(0, width_x, start, 0)

    def clear(k, carry):
        at = pl.ds(pl.multiple_of(k * chunk, chunk), chunk)
        o_ref[at, :] = jnp.zeros((chunk, features), jnp.float32)
        return carry

    lax.fori_loop(0, o_ref.shape[0] // chunk, clear, 0)

    def transpose_tile(x, carry):
        for copy in copies(x):
            copy.wait()
        st_ref[pl.ds(pl.multiple_of(x * width_y, width_y), width_y), :] = buf[x].T
        return carry

    lax.fori_loop(0, width_x, transpose_tile, 0, unroll=4)

    def place(r, carry):
        o_ref[pl.ds(slot_ref[r], 1), :] = st_ref[pl.ds(act_ref[r], 1), :]
        return carry

    lax.fori_loop(0, act_ref.shape[0], place, 0, unroll=64)


def diffuse_kernel(st_ref, xb_ref, xa_ref, yh_ref, c_ref, f_ref, e_ref, a_ref):
    width_x, width_y, _ = st_ref.shape
    depth = xb_ref.shape[0]
    rows_ext, ylen, _ = c_ref.shape
    e_ref[0:depth, 0:width_y, :] = xb_ref[...]
    e_ref[depth + width_x :, 0:width_y, :] = xa_ref[...]

    def fill(x, carry):
        e_ref[x + depth, 0:width_y, :] = st_ref[x]
        return carry

    lax.fori_loop(0, width_x, fill, 0)
    e_ref[:, width_y:, :] = yh_ref[...]

    def sweep(src, dst, p, last):
        def one(x, carry):
            q = src[x]
            n = src[x + 1] + src[x - 1]
            n = n + pltpu.roll(q, ylen - 1, 0) + pltpu.roll(q, 1, 0)
            new = q + c_ref[x] * (n - 4.0 * q)
            if last:
                f_ref[x - depth] = new[:width_y]
            else:
                dst[x] = new
            return carry

        lax.fori_loop(p + 1, rows_ext - 1 - p, one, 0)

    for p in range(PASSES):
        src, dst = (e_ref, a_ref) if p % 2 == 0 else (a_ref, e_ref)
        sweep(src, dst, p, p == PASSES - 1)


def finish_kernel(slot_ref, act_ref, r_ref, f_ref, uo_hbm, vo_hbm, d_ref, obuf, sems):
    levels = uo_hbm.shape[0]
    width_x, features, width_y = obuf.shape

    def clear(x, carry):
        at = pl.ds(pl.multiple_of(x * width_y, width_y), width_y)
        d_ref[at, :] = jnp.zeros((width_y, features), jnp.float32)
        return carry

    lax.fori_loop(0, width_x, clear, 0)

    def place(r, carry):
        d_ref[pl.ds(act_ref[r], 1), :] = r_ref[pl.ds(slot_ref[r], 1), :]
        return carry

    lax.fori_loop(0, act_ref.shape[0], place, 0, unroll=64)

    def copies(x):
        return (
            pltpu.make_async_copy(obuf.at[x, pl.ds(0, levels), :], uo_hbm.at[:, x, :], sems.at[0, x]),
            pltpu.make_async_copy(obuf.at[x, pl.ds(levels, levels), :], vo_hbm.at[:, x, :], sems.at[1, x]),
        )

    def transpose_tile(x, carry):
        at = pl.ds(pl.multiple_of(x * width_y, width_y), width_y)
        obuf[x] = (f_ref[at, :] + d_ref[at, :]).T
        for copy in copies(x):
            copy.start()
        return carry

    lax.fori_loop(0, width_x, transpose_tile, 0, unroll=4)

    def finish(x, carry):
        for copy in copies(x):
            copy.wait()
        return carry

    lax.fori_loop(0, width_x, finish, 0)


def body(
    u_field,
    v_field,
    diffusivity,
    active_columns,
    regimes,
    first_layer,
    second_layer,
    third_layer,
    last_layer,
):
    levels, width_x, width_y = u_field.shape
    features = 2 * levels
    cells = width_x * width_y
    active_count = active_columns.shape[0]
    devices_all = lax.axis_size(("tile", "inf"))
    capacity = 2 * active_count // devices_all
    slot_total = devices_all * capacity
    block_rows = min(512, active_count)
    block_count = active_count // block_rows
    target = regimes[:, 0]
    labels = jnp.arange(devices_all, dtype=jnp.int32)
    one_hot = (
        (target[:, None] == labels[None, :])
        .astype(jnp.bfloat16)
        .reshape(block_count, block_rows, devices_all)
    )
    row_ids = jnp.arange(block_rows, dtype=jnp.int32)
    lower = (row_ids[:, None] > row_ids[None, :]).astype(jnp.bfloat16)

    def rank_step(counts, piece):
        earlier = jnp.dot(lower, piece, preferred_element_type=jnp.float32) + counts[None, :]
        wide_piece = piece.astype(jnp.float32)
        rank = jnp.sum(earlier * wide_piece, axis=1)
        return (counts + jnp.sum(wide_piece, axis=0), rank)

    _, ranks = lax.scan(rank_step, jnp.zeros((devices_all,), jnp.float32), one_hot)
    tile_count, inf_count = lax.axis_size("tile"), lax.axis_size("inf")
    half_tiles = tile_count // 2
    my_half = lax.axis_index("tile") // half_tiles
    target_tile = target // inf_count
    place = (target_tile % half_tiles) * inf_count + target % inf_count
    kind = (target_tile // half_tiles != my_half).astype(jnp.int32)
    pair_slots = 2 * capacity
    slot_index = place * pair_slots + kind * capacity + ranks.reshape(-1).astype(jnp.int32)
    groups = [
        [t * inf_count + i for t in range(h * half_tiles, (h + 1) * half_tiles) for i in range(inf_count)]
        for h in range(2)
    ]
    group_size = half_tiles * inf_count
    swap = [(t, (t + half_tiles) % tile_count) for t in range(tile_count)]
    mirrored = [
        lax.ppermute(w[0], "tile", swap) for w in (first_layer, second_layer, third_layer, last_layer)
    ]
    vmem = pl.BlockSpec(memory_space=pltpu.VMEM)
    smem = pl.BlockSpec(memory_space=pltpu.SMEM)
    x_from_before, x_from_after = stencil_start(u_field, v_field, diffusivity, PASSES)
    hbm = pl.BlockSpec(memory_space=pl.ANY)
    state_t, outgoing = pl.pallas_call(
        gather_kernel,
        out_shape=(
            jax.ShapeDtypeStruct((cells, features), jnp.float32),
            jax.ShapeDtypeStruct((slot_total, features), jnp.float32),
        ),
        in_specs=[smem, smem, hbm, hbm],
        out_specs=(vmem, vmem),
        scratch_shapes=[
            pltpu.VMEM((width_x, features, width_y), jnp.float32),
            pltpu.SemaphoreType.DMA((2, width_x)),
        ],
    )(slot_index, active_columns, u_field, v_field)
    state_t = state_t.reshape(width_x, width_y, features)
    outgoing, x_from_before, x_from_after = lax.optimization_barrier(
        (outgoing, x_from_before, x_from_after)
    )
    block = lax.all_to_all(
        outgoing.reshape(group_size, pair_slots, features),
        ("tile", "inf"),
        split_axis=0,
        concat_axis=0,
        tiled=True,
        axis_index_groups=groups,
    )
    block_shape = block.shape
    x_before, x_after, y_halo, coeff = stencil_finish(
        state_t, diffusivity, x_from_before, x_from_after, PASSES
    )
    block, x_before, x_after, y_halo = lax.optimization_barrier(
        (block, x_before, x_after, y_halo)
    )
    own_rows = standardize(block[:, :capacity].reshape(-1, features))
    own = network_rows(own_rows, first_layer[0], second_layer[0], third_layer[0], last_layer[0])
    other_rows = standardize(block[:, capacity:].reshape(-1, features))
    other = network_rows(other_rows, *mirrored)
    answered = jnp.concatenate(
        [own.reshape(group_size, capacity, features), other.reshape(group_size, capacity, features)],
        axis=1,
    )
    returned = lax.all_to_all(
        answered,
        ("tile", "inf"),
        split_axis=0,
        concat_axis=0,
        tiled=True,
        axis_index_groups=groups,
    )
    returned_rows = returned.reshape(slot_total, features)

    rows_ext, ylen = coeff.shape[:2]
    diffused = pl.pallas_call(
        diffuse_kernel,
        out_shape=jax.ShapeDtypeStruct((width_x, width_y, features), jnp.float32),
        in_specs=[vmem] * 5,
        out_specs=vmem,
        scratch_shapes=[
            pltpu.VMEM((rows_ext, ylen, features), jnp.float32),
            pltpu.VMEM((rows_ext, ylen, features), jnp.float32),
        ],
        compiler_params=pltpu.CompilerParams(vmem_limit_bytes=100 * 1024 * 1024),
    )(state_t, x_before, x_after, y_halo, coeff)
    u_next, v_next = pl.pallas_call(
        finish_kernel,
        out_shape=(
            jax.ShapeDtypeStruct(u_field.shape, jnp.float32),
            jax.ShapeDtypeStruct(v_field.shape, jnp.float32),
        ),
        in_specs=[smem, smem, vmem, vmem],
        out_specs=(hbm, hbm),
        scratch_shapes=[
            pltpu.VMEM((cells, features), jnp.float32),
            pltpu.VMEM((width_x, features, width_y), jnp.float32),
            pltpu.SemaphoreType.DMA((2, width_x)),
        ],
    )(slot_index, active_columns, returned_rows, diffused.reshape(cells, features))
    return (u_next, v_next)


def solution(mesh):
    in_specs = (
        P(None, "tile", "inf"),
        P(None, "tile", "inf"),
        P("tile", "inf"),
        P(("tile", "inf")),
        P(("tile", "inf"), None),
        P(("tile", "inf"), None, None),
        P(("tile", "inf"), None, None),
        P(("tile", "inf"), None, None),
        P(("tile", "inf"), None, None),
    )
    out_specs = (P(None, "tile", "inf"), P(None, "tile", "inf"))
    return jax.shard_map(body, mesh=mesh, in_specs=in_specs, out_specs=out_specs, check_vma=False)
```

```python
import jax
import jax.numpy as jnp
from jax import lax
from jax.experimental import pallas as pl
from jax.experimental.pallas import tpu as pltpu
from jax.sharding import PartitionSpec as P

PASSES = 4


def halos(x, axis, dim, width):
    count, length = (lax.axis_size(axis), x.shape[dim])
    up = [(i, i + 1) for i in range(count - 1)]
    down = [(j, i) for i, j in up]
    last = lax.slice_in_dim(x, length - width, length, axis=dim)
    first = lax.slice_in_dim(x, 0, width, axis=dim)
    before = lax.ppermute(last, axis, up)
    after = lax.ppermute(first, axis, down)
    return before, after


def stencil_start(u_field, v_field, diffusivity, depth):
    width_x = u_field.shape[1]

    def x_piece(start):
        rows = lambda a: lax.slice_in_dim(a, start, start + depth, axis=a.ndim - 2)
        return jnp.concatenate([rows(u_field), rows(v_field), rows(diffusivity)[None]], axis=0)

    tile_count = lax.axis_size("tile")
    up = [(i, i + 1) for i in range(tile_count - 1)]
    down = [(j, i) for i, j in up]
    before = lax.ppermute(x_piece(width_x - depth), "tile", up)
    after = lax.ppermute(x_piece(0), "tile", down)
    return before, after


def stencil_finish(state_t, diffusivity, before, after, depth):
    width_x, width_y, features = state_t.shape
    x_before = before[:features].transpose(1, 2, 0)
    x_after = after[:features].transpose(1, 2, 0)
    c_rows = jnp.concatenate([before[features], diffusivity, after[features]], axis=0)
    extended = jnp.concatenate([x_before, state_t, x_after], axis=0)

    def y_piece(start):
        rows = lax.slice_in_dim(extended, start, start + depth, axis=1)
        cols = lax.slice_in_dim(c_rows, start, start + depth, axis=1).T
        cols = jnp.pad(cols, ((0, 0), (0, features - cols.shape[1])))
        return jnp.concatenate([rows, cols[None]], axis=0)

    inf_count = lax.axis_size("inf")
    up = [(i, i + 1) for i in range(inf_count - 1)]
    down = [(j, i) for i, j in up]
    before = lax.ppermute(y_piece(width_y - depth), "inf", up)
    after = lax.ppermute(y_piece(0), "inf", down)
    rows_ext = extended.shape[0]
    y_halo = jnp.concatenate([after[:rows_ext], before[:rows_ext]], axis=1)
    c_ext = jnp.concatenate(
        [c_rows, after[rows_ext, :, :rows_ext].T, before[rows_ext, :, :rows_ext].T], axis=1
    )
    ylen = c_ext.shape[1]
    coeff = jnp.broadcast_to(c_ext[:, :, None], (rows_ext, ylen, features))
    return x_before, x_after, y_halo, coeff


def standardize(rows):
    center = jnp.mean(rows, axis=-1, keepdims=True)
    spread = jnp.mean(jnp.square(rows - center), axis=-1, keepdims=True)
    return (rows - center) * lax.rsqrt(spread + 1e-05)


def network_rows(rows, first_layer, second_layer, third_layer, last_layer):
    highest = lax.Precision.HIGH
    hidden = jax.nn.silu(jnp.dot(rows, first_layer, precision=highest))
    hidden = jax.nn.silu(jnp.dot(hidden, second_layer, precision=highest))
    hidden = jax.nn.silu(jnp.dot(hidden, third_layer, precision=highest))
    return jnp.dot(hidden, last_layer, precision=highest)


def gather_kernel(slot_ref, act_ref, u_hbm, v_hbm, st_ref, o_ref, buf, sems):
    levels = u_hbm.shape[0]
    width_x, features, width_y = buf.shape
    chunk = 128

    def copies(x):
        return (
            pltpu.make_async_copy(u_hbm.at[:, x, :], buf.at[x, pl.ds(0, levels), :], sems.at[0, x]),
            pltpu.make_async_copy(v_hbm.at[:, x, :], buf.at[x, pl.ds(levels, levels), :], sems.at[1, x]),
        )

    def start(x, carry):
        for copy in copies(x):
            copy.start()
        return carry

    lax.fori_loop(0, width_x, start, 0)

    def clear(k, carry):
        at = pl.ds(pl.multiple_of(k * chunk, chunk), chunk)
        o_ref[at, :] = jnp.zeros((chunk, features), jnp.float32)
        return carry

    lax.fori_loop(0, o_ref.shape[0] // chunk, clear, 0)

    def transpose_tile(x, carry):
        for copy in copies(x):
            copy.wait()
        st_ref[pl.ds(pl.multiple_of(x * width_y, width_y), width_y), :] = buf[x].T
        return carry

    lax.fori_loop(0, width_x, transpose_tile, 0, unroll=8)

    def place(r, carry):
        o_ref[pl.ds(slot_ref[r], 1), :] = st_ref[pl.ds(act_ref[r], 1), :]
        return carry

    lax.fori_loop(0, act_ref.shape[0], place, 0, unroll=64)


def diffuse_kernel(st_ref, xb_ref, xa_ref, yh_ref, c_ref, f_ref, e_ref, a_ref):
    width_x, width_y, _ = st_ref.shape
    depth = xb_ref.shape[0]
    rows_ext, ylen, _ = c_ref.shape
    e_ref[0:depth, 0:width_y, :] = xb_ref[...]
    e_ref[depth + width_x :, 0:width_y, :] = xa_ref[...]

    def fill(x, carry):
        e_ref[x + depth, 0:width_y, :] = st_ref[x]
        return carry

    lax.fori_loop(0, width_x, fill, 0)
    e_ref[:, width_y:, :] = yh_ref[...]

    def sweep(src, dst, p, last):
        def one(x, carry):
            q = src[x]
            n = src[x + 1] + src[x - 1]
            n = n + pltpu.roll(q, ylen - 1, 0) + pltpu.roll(q, 1, 0)
            new = q + c_ref[x] * (n - 4.0 * q)
            if last:
                f_ref[x - depth] = new[:width_y]
            else:
                dst[x] = new
            return carry

        lax.fori_loop(p + 1, rows_ext - 1 - p, one, 0)

    for p in range(PASSES):
        src, dst = (e_ref, a_ref) if p % 2 == 0 else (a_ref, e_ref)
        sweep(src, dst, p, p == PASSES - 1)


def finish_kernel(slot_ref, act_ref, r_ref, f_ref, uo_hbm, vo_hbm, d_ref, obuf, sems):
    levels = uo_hbm.shape[0]
    width_x, features, width_y = obuf.shape

    def clear(x, carry):
        at = pl.ds(pl.multiple_of(x * width_y, width_y), width_y)
        d_ref[at, :] = jnp.zeros((width_y, features), jnp.float32)
        return carry

    lax.fori_loop(0, width_x, clear, 0)

    def place(r, carry):
        d_ref[pl.ds(act_ref[r], 1), :] = r_ref[pl.ds(slot_ref[r], 1), :]
        return carry

    lax.fori_loop(0, act_ref.shape[0], place, 0, unroll=64)

    def copies(x):
        return (
            pltpu.make_async_copy(obuf.at[x, pl.ds(0, levels), :], uo_hbm.at[:, x, :], sems.at[0, x]),
            pltpu.make_async_copy(obuf.at[x, pl.ds(levels, levels), :], vo_hbm.at[:, x, :], sems.at[1, x]),
        )

    def transpose_tile(x, carry):
        at = pl.ds(pl.multiple_of(x * width_y, width_y), width_y)
        obuf[x] = (f_ref[at, :] + d_ref[at, :]).T
        for copy in copies(x):
            copy.start()
        return carry

    lax.fori_loop(0, width_x, transpose_tile, 0, unroll=8)

    def finish(x, carry):
        for copy in copies(x):
            copy.wait()
        return carry

    lax.fori_loop(0, width_x, finish, 0)


def body(
    u_field,
    v_field,
    diffusivity,
    active_columns,
    regimes,
    first_layer,
    second_layer,
    third_layer,
    last_layer,
):
    levels, width_x, width_y = u_field.shape
    features = 2 * levels
    cells = width_x * width_y
    active_count = active_columns.shape[0]
    devices_all = lax.axis_size(("tile", "inf"))
    capacity = 2 * active_count // devices_all
    slot_total = devices_all * capacity
    block_rows = min(512, active_count)
    block_count = active_count // block_rows
    target = regimes[:, 0]
    labels = jnp.arange(devices_all, dtype=jnp.int32)
    one_hot = (
        (target[:, None] == labels[None, :])
        .astype(jnp.bfloat16)
        .reshape(block_count, block_rows, devices_all)
    )
    row_ids = jnp.arange(block_rows, dtype=jnp.int32)
    lower = (row_ids[:, None] > row_ids[None, :]).astype(jnp.bfloat16)

    def rank_step(counts, piece):
        earlier = jnp.dot(lower, piece, preferred_element_type=jnp.float32) + counts[None, :]
        wide_piece = piece.astype(jnp.float32)
        rank = jnp.sum(earlier * wide_piece, axis=1)
        return (counts + jnp.sum(wide_piece, axis=0), rank)

    _, ranks = lax.scan(rank_step, jnp.zeros((devices_all,), jnp.float32), one_hot)
    tile_count, inf_count = lax.axis_size("tile"), lax.axis_size("inf")
    half_tiles = tile_count // 2
    my_half = lax.axis_index("tile") // half_tiles
    target_tile = target // inf_count
    place = (target_tile % half_tiles) * inf_count + target % inf_count
    kind = (target_tile // half_tiles != my_half).astype(jnp.int32)
    pair_slots = 2 * capacity
    slot_index = place * pair_slots + kind * capacity + ranks.reshape(-1).astype(jnp.int32)
    groups = [
        [t * inf_count + i for t in range(h * half_tiles, (h + 1) * half_tiles) for i in range(inf_count)]
        for h in range(2)
    ]
    group_size = half_tiles * inf_count
    swap = [(t, (t + half_tiles) % tile_count) for t in range(tile_count)]
    mirrored = [
        lax.ppermute(w[0], "tile", swap) for w in (first_layer, second_layer, third_layer, last_layer)
    ]
    vmem = pl.BlockSpec(memory_space=pltpu.VMEM)
    smem = pl.BlockSpec(memory_space=pltpu.SMEM)
    x_from_before, x_from_after = stencil_start(u_field, v_field, diffusivity, PASSES)
    hbm = pl.BlockSpec(memory_space=pl.ANY)
    state_t, outgoing = pl.pallas_call(
        gather_kernel,
        out_shape=(
            jax.ShapeDtypeStruct((cells, features), jnp.float32),
            jax.ShapeDtypeStruct((slot_total, features), jnp.float32),
        ),
        in_specs=[smem, smem, hbm, hbm],
        out_specs=(vmem, vmem),
        scratch_shapes=[
            pltpu.VMEM((width_x, features, width_y), jnp.float32),
            pltpu.SemaphoreType.DMA((2, width_x)),
        ],
    )(slot_index, active_columns, u_field, v_field)
    state_t = state_t.reshape(width_x, width_y, features)
    outgoing, x_from_before, x_from_after = lax.optimization_barrier(
        (outgoing, x_from_before, x_from_after)
    )
    block = lax.all_to_all(
        outgoing.reshape(group_size, pair_slots, features),
        ("tile", "inf"),
        split_axis=0,
        concat_axis=0,
        tiled=True,
        axis_index_groups=groups,
    )
    block_shape = block.shape
    x_before, x_after, y_halo, coeff = stencil_finish(
        state_t, diffusivity, x_from_before, x_from_after, PASSES
    )
    block, x_before, x_after, y_halo = lax.optimization_barrier(
        (block, x_before, x_after, y_halo)
    )
    own_rows = standardize(block[:, :capacity].reshape(-1, features))
    own = network_rows(own_rows, first_layer[0], second_layer[0], third_layer[0], last_layer[0])
    other_rows = standardize(block[:, capacity:].reshape(-1, features))
    other = network_rows(other_rows, *mirrored)
    answered = jnp.concatenate(
        [own.reshape(group_size, capacity, features), other.reshape(group_size, capacity, features)],
        axis=1,
    )
    returned = lax.all_to_all(
        answered,
        ("tile", "inf"),
        split_axis=0,
        concat_axis=0,
        tiled=True,
        axis_index_groups=groups,
    )
    returned_rows = returned.reshape(slot_total, features)

    rows_ext, ylen = coeff.shape[:2]
    diffused = pl.pallas_call(
        diffuse_kernel,
        out_shape=jax.ShapeDtypeStruct((width_x, width_y, features), jnp.float32),
        in_specs=[vmem] * 5,
        out_specs=vmem,
        scratch_shapes=[
            pltpu.VMEM((rows_ext, ylen, features), jnp.float32),
            pltpu.VMEM((rows_ext, ylen, features), jnp.float32),
        ],
        compiler_params=pltpu.CompilerParams(vmem_limit_bytes=100 * 1024 * 1024),
    )(state_t, x_before, x_after, y_halo, coeff)
    u_next, v_next = pl.pallas_call(
        finish_kernel,
        out_shape=(
            jax.ShapeDtypeStruct(u_field.shape, jnp.float32),
            jax.ShapeDtypeStruct(v_field.shape, jnp.float32),
        ),
        in_specs=[smem, smem, vmem, vmem],
        out_specs=(hbm, hbm),
        scratch_shapes=[
            pltpu.VMEM((cells, features), jnp.float32),
            pltpu.VMEM((width_x, features, width_y), jnp.float32),
            pltpu.SemaphoreType.DMA((2, width_x)),
        ],
    )(slot_index, active_columns, returned_rows, diffused.reshape(cells, features))
    return (u_next, v_next)


def solution(mesh):
    in_specs = (
        P(None, "tile", "inf"),
        P(None, "tile", "inf"),
        P("tile", "inf"),
        P(("tile", "inf")),
        P(("tile", "inf"), None),
        P(("tile", "inf"), None, None),
        P(("tile", "inf"), None, None),
        P(("tile", "inf"), None, None),
        P(("tile", "inf"), None, None),
    )
    out_specs = (P(None, "tile", "inf"), P(None, "tile", "inf"))
    return jax.shard_map(body, mesh=mesh, in_specs=in_specs, out_specs=out_specs, check_vma=False)
```

```python
import jax
import jax.numpy as jnp
from jax import lax
from jax.experimental import pallas as pl
from jax.experimental.pallas import tpu as pltpu
from jax.sharding import PartitionSpec as P

PASSES = 4


def halos(x, axis, dim, width):
    count, length = (lax.axis_size(axis), x.shape[dim])
    up = [(i, i + 1) for i in range(count - 1)]
    down = [(j, i) for i, j in up]
    last = lax.slice_in_dim(x, length - width, length, axis=dim)
    first = lax.slice_in_dim(x, 0, width, axis=dim)
    before = lax.ppermute(last, axis, up)
    after = lax.ppermute(first, axis, down)
    return before, after


def stencil_start(u_field, v_field, diffusivity, depth):
    width_x = u_field.shape[1]

    def x_piece(start):
        rows = lambda a: lax.slice_in_dim(a, start, start + depth, axis=a.ndim - 2)
        return jnp.concatenate([rows(u_field), rows(v_field), rows(diffusivity)[None]], axis=0)

    tile_count = lax.axis_size("tile")
    up = [(i, i + 1) for i in range(tile_count - 1)]
    down = [(j, i) for i, j in up]
    before = lax.ppermute(x_piece(width_x - depth), "tile", up)
    after = lax.ppermute(x_piece(0), "tile", down)
    return before, after


def stencil_finish(state_t, diffusivity, before, after, depth):
    width_x, width_y, features = state_t.shape
    x_before = before[:features].transpose(1, 2, 0)
    x_after = after[:features].transpose(1, 2, 0)
    c_rows = jnp.concatenate([before[features], diffusivity, after[features]], axis=0)
    extended = jnp.concatenate([x_before, state_t, x_after], axis=0)

    def y_piece(start):
        rows = lax.slice_in_dim(extended, start, start + depth, axis=1)
        cols = lax.slice_in_dim(c_rows, start, start + depth, axis=1).T
        cols = jnp.pad(cols, ((0, 0), (0, features - cols.shape[1])))
        return jnp.concatenate([rows, cols[None]], axis=0)

    inf_count = lax.axis_size("inf")
    up = [(i, i + 1) for i in range(inf_count - 1)]
    down = [(j, i) for i, j in up]
    before = lax.ppermute(y_piece(width_y - depth), "inf", up)
    after = lax.ppermute(y_piece(0), "inf", down)
    rows_ext = extended.shape[0]
    y_halo = jnp.concatenate([after[:rows_ext], before[:rows_ext]], axis=1)
    c_ext = jnp.concatenate(
        [c_rows, after[rows_ext, :, :rows_ext].T, before[rows_ext, :, :rows_ext].T], axis=1
    )
    ylen = c_ext.shape[1]
    coeff = jnp.broadcast_to(c_ext[:, :, None], (rows_ext, ylen, features))
    return x_before, x_after, y_halo, coeff


def standardize(rows):
    center = jnp.mean(rows, axis=-1, keepdims=True)
    spread = jnp.mean(jnp.square(rows - center), axis=-1, keepdims=True)
    return (rows - center) * lax.rsqrt(spread + 1e-05)


def network_rows(rows, first_layer, second_layer, third_layer, last_layer):
    highest = lax.Precision.HIGH
    hidden = jax.nn.silu(jnp.dot(rows, first_layer, precision=highest))
    hidden = jax.nn.silu(jnp.dot(hidden, second_layer, precision=highest))
    hidden = jax.nn.silu(jnp.dot(hidden, third_layer, precision=highest))
    return jnp.dot(hidden, last_layer, precision=highest)


def gather_kernel(slot_ref, act_ref, u_hbm, v_hbm, st_ref, o_ref, buf, sems):
    levels = u_hbm.shape[0]
    width_x, features, width_y = buf.shape
    chunk = 128

    def copies(x):
        return (
            pltpu.make_async_copy(u_hbm.at[:, x, :], buf.at[x, pl.ds(0, levels), :], sems.at[0, x]),
            pltpu.make_async_copy(v_hbm.at[:, x, :], buf.at[x, pl.ds(levels, levels), :], sems.at[1, x]),
        )

    def start(x, carry):
        for copy in copies(x):
            copy.start()
        return carry

    lax.fori_loop(0, width_x, start, 0)

    def clear(k, carry):
        at = pl.ds(pl.multiple_of(k * chunk, chunk), chunk)
        o_ref[at, :] = jnp.zeros((chunk, features), jnp.float32)
        return carry

    lax.fori_loop(0, o_ref.shape[0] // chunk, clear, 0, unroll=8)

    def transpose_tile(x, carry):
        for copy in copies(x):
            copy.wait()
        st_ref[pl.ds(pl.multiple_of(x * width_y, width_y), width_y), :] = buf[x].T
        return carry

    lax.fori_loop(0, width_x, transpose_tile, 0, unroll=8)

    def place(r, carry):
        o_ref[pl.ds(slot_ref[r], 1), :] = st_ref[pl.ds(act_ref[r], 1), :]
        return carry

    lax.fori_loop(0, act_ref.shape[0], place, 0, unroll=64)


def diffuse_kernel(st_ref, xb_ref, xa_ref, yh_ref, c_ref, f_ref, e_ref, a_ref):
    width_x, width_y, _ = st_ref.shape
    depth = xb_ref.shape[0]
    rows_ext, ylen, _ = c_ref.shape
    e_ref[0:depth, 0:width_y, :] = xb_ref[...]
    e_ref[depth + width_x :, 0:width_y, :] = xa_ref[...]

    def fill(x, carry):
        e_ref[x + depth, 0:width_y, :] = st_ref[x]
        return carry

    lax.fori_loop(0, width_x, fill, 0)
    e_ref[:, width_y:, :] = yh_ref[...]

    def sweep(src, dst, p, last):
        def one(x, carry):
            q = src[x]
            n = src[x + 1] + src[x - 1]
            n = n + pltpu.roll(q, ylen - 1, 0) + pltpu.roll(q, 1, 0)
            new = q + c_ref[x] * (n - 4.0 * q)
            if last:
                f_ref[x - depth] = new[:width_y]
            else:
                dst[x] = new
            return carry

        lax.fori_loop(p + 1, rows_ext - 1 - p, one, 0)

    for p in range(PASSES):
        src, dst = (e_ref, a_ref) if p % 2 == 0 else (a_ref, e_ref)
        sweep(src, dst, p, p == PASSES - 1)


def finish_kernel(slot_ref, act_ref, r_ref, f_ref, uo_hbm, vo_hbm, d_ref, obuf, sems):
    levels = uo_hbm.shape[0]
    width_x, features, width_y = obuf.shape

    def clear(x, carry):
        at = pl.ds(pl.multiple_of(x * width_y, width_y), width_y)
        d_ref[at, :] = jnp.zeros((width_y, features), jnp.float32)
        return carry

    lax.fori_loop(0, width_x, clear, 0, unroll=8)

    def place(r, carry):
        d_ref[pl.ds(act_ref[r], 1), :] = r_ref[pl.ds(slot_ref[r], 1), :]
        return carry

    lax.fori_loop(0, act_ref.shape[0], place, 0, unroll=64)

    def copies(x):
        return (
            pltpu.make_async_copy(obuf.at[x, pl.ds(0, levels), :], uo_hbm.at[:, x, :], sems.at[0, x]),
            pltpu.make_async_copy(obuf.at[x, pl.ds(levels, levels), :], vo_hbm.at[:, x, :], sems.at[1, x]),
        )

    def transpose_tile(x, carry):
        at = pl.ds(pl.multiple_of(x * width_y, width_y), width_y)
        obuf[x] = (f_ref[at, :] + d_ref[at, :]).T
        for copy in copies(x):
            copy.start()
        return carry

    lax.fori_loop(0, width_x, transpose_tile, 0, unroll=8)

    def finish(x, carry):
        for copy in copies(x):
            copy.wait()
        return carry

    lax.fori_loop(0, width_x, finish, 0)


def body(
    u_field,
    v_field,
    diffusivity,
    active_columns,
    regimes,
    first_layer,
    second_layer,
    third_layer,
    last_layer,
):
    levels, width_x, width_y = u_field.shape
    features = 2 * levels
    cells = width_x * width_y
    active_count = active_columns.shape[0]
    devices_all = lax.axis_size(("tile", "inf"))
    capacity = 2 * active_count // devices_all
    slot_total = devices_all * capacity
    block_rows = min(512, active_count)
    block_count = active_count // block_rows
    target = regimes[:, 0]
    labels = jnp.arange(devices_all, dtype=jnp.int32)
    one_hot = (
        (target[:, None] == labels[None, :])
        .astype(jnp.bfloat16)
        .reshape(block_count, block_rows, devices_all)
    )
    row_ids = jnp.arange(block_rows, dtype=jnp.int32)
    lower = (row_ids[:, None] > row_ids[None, :]).astype(jnp.bfloat16)

    def rank_step(counts, piece):
        earlier = jnp.dot(lower, piece, preferred_element_type=jnp.float32) + counts[None, :]
        wide_piece = piece.astype(jnp.float32)
        rank = jnp.sum(earlier * wide_piece, axis=1)
        return (counts + jnp.sum(wide_piece, axis=0), rank)

    _, ranks = lax.scan(rank_step, jnp.zeros((devices_all,), jnp.float32), one_hot)
    tile_count, inf_count = lax.axis_size("tile"), lax.axis_size("inf")
    half_tiles = tile_count // 2
    my_half = lax.axis_index("tile") // half_tiles
    target_tile = target // inf_count
    place = (target_tile % half_tiles) * inf_count + target % inf_count
    kind = (target_tile // half_tiles != my_half).astype(jnp.int32)
    pair_slots = 2 * capacity
    slot_index = place * pair_slots + kind * capacity + ranks.reshape(-1).astype(jnp.int32)
    groups = [
        [t * inf_count + i for t in range(h * half_tiles, (h + 1) * half_tiles) for i in range(inf_count)]
        for h in range(2)
    ]
    group_size = half_tiles * inf_count
    swap = [(t, (t + half_tiles) % tile_count) for t in range(tile_count)]
    mirrored = [
        lax.ppermute(w[0], "tile", swap) for w in (first_layer, second_layer, third_layer, last_layer)
    ]
    vmem = pl.BlockSpec(memory_space=pltpu.VMEM)
    smem = pl.BlockSpec(memory_space=pltpu.SMEM)
    x_from_before, x_from_after = stencil_start(u_field, v_field, diffusivity, PASSES)
    hbm = pl.BlockSpec(memory_space=pl.ANY)
    state_t, outgoing = pl.pallas_call(
        gather_kernel,
        out_shape=(
            jax.ShapeDtypeStruct((cells, features), jnp.float32),
            jax.ShapeDtypeStruct((slot_total, features), jnp.float32),
        ),
        in_specs=[smem, smem, hbm, hbm],
        out_specs=(vmem, vmem),
        scratch_shapes=[
            pltpu.VMEM((width_x, features, width_y), jnp.float32),
            pltpu.SemaphoreType.DMA((2, width_x)),
        ],
    )(slot_index, active_columns, u_field, v_field)
    state_t = state_t.reshape(width_x, width_y, features)
    outgoing, x_from_before, x_from_after = lax.optimization_barrier(
        (outgoing, x_from_before, x_from_after)
    )
    block = lax.all_to_all(
        outgoing.reshape(group_size, pair_slots, features),
        ("tile", "inf"),
        split_axis=0,
        concat_axis=0,
        tiled=True,
        axis_index_groups=groups,
    )
    block_shape = block.shape
    x_before, x_after, y_halo, coeff = stencil_finish(
        state_t, diffusivity, x_from_before, x_from_after, PASSES
    )
    block, x_before, x_after, y_halo = lax.optimization_barrier(
        (block, x_before, x_after, y_halo)
    )
    own_rows = standardize(block[:, :capacity].reshape(-1, features))
    own = network_rows(own_rows, first_layer[0], second_layer[0], third_layer[0], last_layer[0])
    other_rows = standardize(block[:, capacity:].reshape(-1, features))
    other = network_rows(other_rows, *mirrored)
    answered = jnp.concatenate(
        [own.reshape(group_size, capacity, features), other.reshape(group_size, capacity, features)],
        axis=1,
    )
    returned = lax.all_to_all(
        answered,
        ("tile", "inf"),
        split_axis=0,
        concat_axis=0,
        tiled=True,
        axis_index_groups=groups,
    )
    returned_rows = returned.reshape(slot_total, features)

    rows_ext, ylen = coeff.shape[:2]
    diffused = pl.pallas_call(
        diffuse_kernel,
        out_shape=jax.ShapeDtypeStruct((width_x, width_y, features), jnp.float32),
        in_specs=[vmem] * 5,
        out_specs=vmem,
        scratch_shapes=[
            pltpu.VMEM((rows_ext, ylen, features), jnp.float32),
            pltpu.VMEM((rows_ext, ylen, features), jnp.float32),
        ],
        compiler_params=pltpu.CompilerParams(vmem_limit_bytes=100 * 1024 * 1024),
    )(state_t, x_before, x_after, y_halo, coeff)
    u_next, v_next = pl.pallas_call(
        finish_kernel,
        out_shape=(
            jax.ShapeDtypeStruct(u_field.shape, jnp.float32),
            jax.ShapeDtypeStruct(v_field.shape, jnp.float32),
        ),
        in_specs=[smem, smem, vmem, vmem],
        out_specs=(hbm, hbm),
        scratch_shapes=[
            pltpu.VMEM((cells, features), jnp.float32),
            pltpu.VMEM((width_x, features, width_y), jnp.float32),
            pltpu.SemaphoreType.DMA((2, width_x)),
        ],
    )(slot_index, active_columns, returned_rows, diffused.reshape(cells, features))
    return (u_next, v_next)


def solution(mesh):
    in_specs = (
        P(None, "tile", "inf"),
        P(None, "tile", "inf"),
        P("tile", "inf"),
        P(("tile", "inf")),
        P(("tile", "inf"), None),
        P(("tile", "inf"), None, None),
        P(("tile", "inf"), None, None),
        P(("tile", "inf"), None, None),
        P(("tile", "inf"), None, None),
    )
    out_specs = (P(None, "tile", "inf"), P(None, "tile", "inf"))
    return jax.shard_map(body, mesh=mesh, in_specs=in_specs, out_specs=out_specs, check_vma=False)
```
